32 devices in a mesh: grp: 4 (over x, core), seq: 8 (over z, y).
Axes of the slice: x: 2, y: 2, z: 4, core: 2. Of those that a mesh axis runs over, the one named last changes fastest.
Arguments:
- mixer_input: bfloat16 [6144, 4096], P(('grp', 'seq')), may hold values from -6 to 6
- write_vectors: bfloat16 [6144, 256], P(('grp', 'seq')), may hold values from -6 to 6
- read_vectors: bfloat16 [6144, 256], P(('grp', 'seq')), may hold values from -0.75 to 0.75
- step_sizes: float32 [6144, 64], P(('grp', 'seq')), may hold values from 0 to 1, as said below
- decay_rate: float32 [64], replicated, may hold values from 0 to 1, as said below
- skip_gain: float32 [64], replicated, may hold values from 0.5 to 2
- document_ids: int32 [6144], P(('grp', 'seq')), may hold values from 0 to 7, as said below
Outputs:
- ssm_output: bfloat16 [6144, 4096], P(('grp', 'seq'))
The draws below stay inside these ranges and needn't reach their ends.
Inputs may be any that keep to these rules, and one draw needn't show every extreme that they name: `step_sizes`: positive step sizes. `decay_rate`: positive rates. `document_ids`: document ids never fall along the tokens; every one of the 8 documents holds 1 to 3072 tokens and one holds exactly 3072.
All inputs are finite; a program needn't handle non-finite values.
Results may differ from the reference program's by a relative error of at most 0.0029.
Values sent between devices are 32-bit elements; how exact they have to be, the bound alone decides.
No kernel may reach another device: no remote copies, remote signals or barrier semaphores. Data moves between devices by JAX's collectives and lax.ppermute only.
A program may use at most 64 MiB of HBM per device.

```python
import math
import jax
import jax.numpy as jnp
from jax import lax

H = 64
P_SIZE = 64
N = 64
G = 4
BLOCK = 192
DOCS = 8
TOKENS = 6144


def head_reach(key):
    order = jax.random.permutation(jax.random.fold_in(key, 7), H)
    fast_count = H // 2
    slow_count = H - fast_count
    jitter = jax.random.uniform(jax.random.fold_in(key, 23), (H,), jnp.float32)
    rank = order.astype(jnp.float32)
    fast_pos = (rank + jitter) / fast_count
    slow_pos = (rank - fast_count + jitter) / slow_count
    low_end = math.log(30.0)
    middle = math.log(TOKENS / 2.0)
    high_end = math.log(8.0 * TOKENS)
    log_reach = jnp.where(order < fast_count, low_end + fast_pos * (middle - low_end), middle + slow_pos * (high_end - middle))
    share = jnp.exp(jax.random.uniform(jax.random.fold_in(key, 29), (H,), jnp.float32, math.log(0.5), math.log(1.5)))
    return (log_reach, share)


def draw_decay_rate(key, part):
    log_reach, share = head_reach(key)
    return (jnp.exp(-0.5 * log_reach) / share).astype(jnp.float32)


def draw_step_sizes(key, part):
    log_reach, share = head_reach(key)
    base = share * jnp.exp(-0.5 * log_reach)
    blocks = TOKENS // BLOCK
    block_factor = jnp.exp(jax.random.uniform(jax.random.fold_in(key, 17), (blocks, 1, H), jnp.float32, -math.log(2.0), math.log(2.0)))
    token_factor = jnp.exp(jax.random.uniform(jax.random.fold_in(key, 19), (blocks, BLOCK, H), jnp.float32, math.log(0.7), math.log(1.4)))
    values = base[None, None, :] * block_factor * token_factor
    return values.reshape(TOKENS, H).astype(jnp.float32)


def draw_document_ids(key, part):
    half = TOKENS // 2
    half_blocks = half // BLOCK
    cut_count = DOCS - 2
    aligned_count = cut_count // 2
    picks = jax.random.permutation(jax.random.fold_in(key, 31), half_blocks - 1)[:cut_count].astype(jnp.int32) + 1
    offsets = jax.random.randint(jax.random.fold_in(key, 37), (cut_count,), 1, BLOCK).astype(jnp.int32)
    offsets = jnp.where(jnp.arange(cut_count) < aligned_count, 0, offsets)
    cuts = jnp.sort(picks * BLOCK + offsets).astype(jnp.int32)
    big_index = jax.random.randint(jax.random.fold_in(key, 41), (), 0, DOCS).astype(jnp.int32)
    edges = jnp.concatenate([jnp.zeros((1,), jnp.int32), cuts, jnp.full((1,), half, jnp.int32)])
    big_start = edges[big_index]
    positions = jnp.arange(TOKENS, dtype=jnp.int32)
    before = positions < big_start
    inside = positions < big_start + half
    shifted = jnp.where(before, positions, positions - half)
    small_id = jnp.sum((cuts[None, :] <= shifted[:, None]).astype(jnp.int32), axis=1).astype(jnp.int32)
    ids = jnp.where(before, small_id, jnp.where(inside, big_index, small_id + 1))
    return ids.astype(jnp.int32)


def shard_levels(rng, extent, pieces, smallest, top_value):
    loudness, own = 1.0, jax.random.fold_in(rng, 6)
    for dim, parts in pieces:
        draws = jnp.exp(jax.random.uniform(jax.random.fold_in(own, dim), (parts,), jnp.float32, smallest / len(pieces), top_value / len(pieces)))
        loudness = loudness * jnp.repeat(draws, extent[dim] // parts).reshape([-1 if axis == dim else 1 for axis in range(len(extent))])
    return loudness


def scatter_about(key, extent, deviation, bound, pieces=(), held_as=jnp.bfloat16):
    entries = deviation * jax.random.normal(key, extent, jnp.float32)
    if pieces:
        entries = entries * shard_levels(key, extent, pieces, -0.22, 0.18)
    return jnp.clip(entries, -bound, bound).astype(held_as)


def setup_inputs(seed: int = 0) -> dict:
    arg_keys = jax.random.split(jax.random.key(seed), 8)
    mixer_input = scatter_about(arg_keys[0], (TOKENS, H * P_SIZE), 1.0, 6.0, ((0, 32),))
    write_vectors = scatter_about(arg_keys[1], (TOKENS, G * N), 1.0, 6.0, ((0, 32),))
    read_vectors = scatter_about(arg_keys[2], (TOKENS, G * N), N ** -0.5, 0.75, ((0, 32),))
    step_sizes = draw_step_sizes(jax.random.fold_in(arg_keys[7], 71), 0)
    decay_rate = draw_decay_rate(jax.random.fold_in(arg_keys[7], 71), 0)
    skip_gain = jnp.clip(jax.random.uniform(arg_keys[5], (H,), jnp.float32, 0.5, 2.0), 0.5, 2.0)
    document_ids = draw_document_ids(jax.random.fold_in(arg_keys[7], 71), 0)
    return dict(mixer_input=mixer_input, write_vectors=write_vectors, read_vectors=read_vectors, step_sizes=step_sizes, decay_rate=decay_rate, skip_gain=skip_gain, document_ids=document_ids)


def combine(earlier, latter):
    e_decays, e_states, e_first, e_last = earlier
    l_decays, l_states, l_first, l_last = latter
    linked = jnp.logical_or(e_last == l_first, jnp.logical_or(e_first < 0, l_first < 0)).astype(e_decays.dtype)
    decays = e_decays * l_decays * linked
    states = l_states + (l_decays * linked)[:, None] * e_states
    first_id = jnp.where(e_first < 0, l_first, e_first)
    last_id = jnp.where(l_first < 0, e_last, l_last)
    return decays, states, first_id, last_id


def local_terms(block_input, write_block, read_block, step_block, rates, doc_block):
    block_rows = block_input.shape[0]
    per_group = H // G
    grouped = block_input.reshape(block_rows, G, per_group, P_SIZE).astype(jnp.float32)
    writes = write_block.reshape(block_rows, G, N).astype(jnp.float32)
    reads = read_block.reshape(block_rows, G, N).astype(jnp.float32)
    cumulative = jnp.cumsum(-step_block * rates[None, :], axis=0)
    cum_heads = cumulative.T.reshape(G, per_group, block_rows)
    step_heads = step_block.T.reshape(G, per_group, block_rows)
    positions = jnp.arange(block_rows)
    visible = jnp.logical_and(doc_block[:, None] == doc_block[None, :], positions[:, None] >= positions[None, :])
    gaps = jnp.where(visible[None, None], cum_heads[:, :, :, None] - cum_heads[:, :, None, :], -jnp.inf)
    inner_prod = jnp.einsum('ign,jgn->gij', reads, writes)
    weights = (inner_prod[:, None] * jnp.exp(gaps) * step_heads[:, :, None, :]).astype(jnp.bfloat16)
    weights = lax.optimization_barrier(weights).astype(jnp.float32)
    local_part = jnp.einsum('ghij,jghp->ighp', weights, grouped)
    same_last = (doc_block == doc_block[-1]).astype(jnp.float32)
    tail_weight = jnp.exp(cumulative[-1][None, :] - cumulative) * step_block * same_last[:, None]
    scaled = (writes[:, :, None, :] * tail_weight.reshape(block_rows, G, per_group)[:, :, :, None]).astype(jnp.bfloat16)
    scaled = lax.optimization_barrier(scaled).astype(jnp.float32)
    states = jnp.einsum('jghn,jghp->ghnp', scaled, grouped).reshape(H, N * P_SIZE)
    decays = jnp.exp(cumulative[-1]) * (doc_block[0] == doc_block[-1]).astype(jnp.float32)
    first_id = doc_block[:1].astype(jnp.float32)
    last_id = doc_block[-1:].astype(jnp.float32)
    return local_part, (decays, states, first_id, last_id), cumulative


def finish(local_part, carried, cumulative, read_block, block_input, gains, doc_block):
    block_rows = block_input.shape[0]
    per_group = H // G
    decays_in, states_in, first_in, last_in = carried
    carried_in = (doc_block.astype(jnp.float32) == last_in).astype(jnp.float32)
    factor = jnp.exp(cumulative) * carried_in[:, None]
    reads = read_block.reshape(block_rows, G, N).astype(jnp.float32)
    held = states_in.reshape(G, per_group, N, P_SIZE)
    reached = jnp.einsum('ign,ghnp->ighp', reads, held, precision=lax.Precision.HIGHEST)
    direct = gains.reshape(G, per_group)[None, :, :, None] * block_input.reshape(block_rows, G, per_group, P_SIZE).astype(jnp.float32)
    result = local_part + reached * factor.reshape(block_rows, G, per_group)[:, :, :, None] + direct
    return result.reshape(block_rows, H * P_SIZE).astype(jnp.bfloat16)


def reference(mixer_input, write_vectors, read_vectors, step_sizes, decay_rate, skip_gain, document_ids):
    blocks = TOKENS // BLOCK
    inputs_blocked = mixer_input.reshape(blocks, BLOCK, H * P_SIZE)
    writes_blocked = write_vectors.reshape(blocks, BLOCK, G * N)
    reads_blocked = read_vectors.reshape(blocks, BLOCK, G * N)
    steps_blocked = step_sizes.reshape(blocks, BLOCK, H)
    docs_blocked = document_ids.reshape(blocks, BLOCK)
    identity = (jnp.ones((H,), jnp.float32), jnp.zeros((H, N * P_SIZE), jnp.float32), jnp.full((1,), -1.0, jnp.float32), jnp.full((1,), -1.0, jnp.float32))

    def advance(carried, block_in):
        block_input, write_block, read_block, step_block, doc_block = block_in
        local_part, summary, cumulative = local_terms(block_input, write_block, read_block, step_block, decay_rate, doc_block)
        output_block = finish(local_part, carried, cumulative, read_block, block_input, skip_gain, doc_block)
        return combine(carried, summary), output_block

    unused, outputs = lax.scan(advance, identity, (inputs_blocked, writes_blocked, reads_blocked, steps_blocked, docs_blocked))
    return outputs.reshape(TOKENS, H * P_SIZE)
```

```python
import jax
import jax.numpy as jnp
from jax import lax
from jax.sharding import PartitionSpec as P

N = 64
G = 4


def local_terms(block_input, write_block, read_block, step_block, rates, doc_block):
    block_rows = block_input.shape[0]
    num_heads = step_block.shape[1]
    per_group = num_heads // G
    width = block_input.shape[1] // num_heads
    grouped = block_input.reshape(block_rows, G, per_group, width)
    writes = write_block.reshape(block_rows, G, N)
    reads = read_block.reshape(block_rows, G, N)
    cumulative = jnp.cumsum(-step_block * rates[None, :], axis=0)
    cum_heads = cumulative.T.reshape(G, per_group, block_rows)
    step_heads = step_block.T.reshape(G, per_group, block_rows)
    positions = jnp.arange(block_rows)
    visible = jnp.logical_and(
        doc_block[:, None] == doc_block[None, :], positions[:, None] >= positions[None, :]
    )
    gaps = jnp.where(
        visible[None, None], cum_heads[:, :, :, None] - cum_heads[:, :, None, :], -jnp.inf
    )
    inner_prod = jnp.einsum("ign,jgn->gij", reads, writes, preferred_element_type=jnp.float32)
    weights = (inner_prod[:, None] * jnp.exp(gaps) * step_heads[:, :, None, :]).astype(jnp.bfloat16)
    local_part = jnp.einsum("ghij,jghp->ighp", weights, grouped, preferred_element_type=jnp.float32)
    same_last = (doc_block == doc_block[-1]).astype(jnp.float32)
    tail_weight = jnp.exp(cumulative[-1][None, :] - cumulative) * step_block * same_last[:, None]
    scaled = (
        writes[:, :, None, :].astype(jnp.float32)
        * tail_weight.reshape(block_rows, G, per_group)[:, :, :, None]
    ).astype(jnp.bfloat16)
    states = jnp.einsum(
        "jghn,jghp->ghnp", scaled, grouped, preferred_element_type=jnp.float32
    ).reshape(num_heads, N * width)
    decays = jnp.exp(cumulative[-1]) * (doc_block[0] == doc_block[-1]).astype(jnp.float32)
    return local_part, states, decays, cumulative


def finish(local_part, states_in, last_in, cumulative, read_block, block_input, gains, doc_block):
    block_rows = block_input.shape[0]
    num_heads = cumulative.shape[1]
    per_group = num_heads // G
    width = block_input.shape[1] // num_heads
    carried_in = (doc_block.astype(jnp.float32) == last_in).astype(jnp.float32)
    factor = jnp.exp(cumulative) * carried_in[:, None]
    reads = read_block.reshape(block_rows, G, N).astype(jnp.float32)
    held = states_in.reshape(G, per_group, N, width)
    reached = jnp.einsum("ign,ghnp->ighp", reads, held, precision=lax.Precision.HIGHEST)
    direct = gains.reshape(G, per_group)[None, :, :, None] * block_input.reshape(
        block_rows, G, per_group, width
    ).astype(jnp.float32)
    result = local_part + reached * factor.reshape(block_rows, G, per_group)[:, :, :, None] + direct
    return result.reshape(block_rows, num_heads * width).astype(jnp.bfloat16)


def exclusive_reverse_prod(values, axis_len):
    rev = jnp.cumprod(jnp.flip(values, 0), axis=0)
    inclusive = jnp.flip(rev, 0)
    ones = jnp.ones_like(values[:1])
    return jnp.concatenate([inclusive[1:], ones], axis=0)


def local(
    mixer_input, write_vectors, read_vectors, step_sizes, decay_rate, skip_gain, document_ids
):
    num_heads = step_sizes.shape[1]
    n_seq = lax.axis_size("seq")
    n_grp = lax.axis_size("grp")
    me = lax.axis_index("seq")
    grp = lax.axis_index("grp")
    local_part, states, decays, cumulative = local_terms(
        mixer_input, write_vectors, read_vectors, step_sizes, decay_rate, document_ids
    )
    state_width = states.shape[1]
    docs_f = document_ids.astype(jnp.float32)

    small = jnp.concatenate([decays, docs_f[:1], docs_f[-1:]])
    every = lax.all_gather(small, ("grp", "seq"))
    total_blocks = every.shape[0]
    all_decays = every[:, :num_heads]
    all_first = every[:, num_heads]
    all_last = every[:, num_heads + 1]
    prev_last = jnp.concatenate([jnp.full((1,), -1.0, jnp.float32), all_last[:-1]])
    link = jnp.logical_and(jnp.arange(total_blocks) > 0, all_first == prev_last)
    factors = all_decays * link.astype(jnp.float32)[:, None]

    flat = states.reshape(n_seq, -1)
    row_len = flat.shape[1]
    row_heads = max(1, num_heads // n_seq)
    sub_len = row_len // row_heads
    head_idx = (me * row_len + jnp.arange(row_heads) * sub_len) // state_width
    pieces = flat.reshape(n_seq, row_heads, sub_len)
    owned = lax.all_to_all(pieces, "seq", 0, 0, tiled=False)

    own_f = jnp.take(factors, head_idx, axis=1)
    grp_f = own_f.reshape(n_grp, n_seq, row_heads)
    my_f = jnp.take(grp_f, grp, axis=0)
    dest = jnp.arange(n_seq + 1)
    src = jnp.arange(n_seq)
    gated = jnp.where((src[:, None] < dest[None, :])[:, :, None], my_f[:, None, :], 1.0)
    coef = exclusive_reverse_prod(gated, n_seq)
    coef = jnp.where((src[:, None] < dest[None, :])[:, :, None], coef, 0.0)
    within = jnp.einsum("tsh,thl->shl", coef, owned, precision=lax.Precision.HIGHEST)

    entry = jnp.concatenate(
        [jnp.ones((1, row_heads), jnp.float32), jnp.cumprod(my_f, axis=0)], axis=0
    )
    whole_grp = jnp.prod(grp_f, axis=1)
    totals = lax.all_gather(within[n_seq], "grp")
    g_idx = jnp.arange(n_grp)
    g_gated = jnp.where((g_idx < grp)[:, None], whole_grp, 1.0)
    g_coef = exclusive_reverse_prod(g_gated, n_grp)
    g_coef = jnp.where((g_idx < grp)[:, None], g_coef, 0.0)
    carry = jnp.sum(g_coef[:, :, None] * totals, axis=0)
    result = within[:n_seq] + entry[:n_seq, :, None] * carry[None]

    back = lax.all_to_all(result, "seq", 0, 0, tiled=False)
    states_in = back.reshape(num_heads, state_width)
    block = grp * n_seq + me
    last_in = jnp.where(block > 0, jnp.take(all_last, jnp.maximum(block - 1, 0)), -1.0)
    return finish(
        local_part, states_in, last_in, cumulative, read_vectors, mixer_input, skip_gain, document_ids
    )


def solution(mesh):
    in_specs = (
        P(("grp", "seq"), None),
        P(("grp", "seq"), None),
        P(("grp", "seq"), None),
        P(("grp", "seq"), None),
        P(),
        P(),
        P(("grp", "seq")),
    )
    out_specs = P(("grp", "seq"), None)
    return jax.shard_map(local, mesh=mesh, in_specs=in_specs, out_specs=out_specs, check_vma=False)
```

```python
import numpy as np
import jax
import jax.numpy as jnp
from jax import lax
from jax.sharding import PartitionSpec as P

N = 64
G = 4
TAIL = 128


def local_terms(block_input, write_block, read_block, step_block, rates, doc_block):
    block_rows = block_input.shape[0]
    num_heads = step_block.shape[1]
    per_group = num_heads // G
    width = block_input.shape[1] // num_heads
    grouped = block_input.reshape(block_rows, G, per_group, width)
    writes = write_block.reshape(block_rows, G, N)
    reads = read_block.reshape(block_rows, G, N)
    cumulative = jnp.cumsum(-step_block * rates[None, :], axis=0)
    cum_heads = cumulative.T.reshape(G, per_group, block_rows)
    step_heads = step_block.T.reshape(G, per_group, block_rows)
    positions = jnp.arange(block_rows)
    visible = jnp.logical_and(
        doc_block[:, None] == doc_block[None, :], positions[:, None] >= positions[None, :]
    )
    gaps = jnp.where(
        visible[None, None], cum_heads[:, :, :, None] - cum_heads[:, :, None, :], -jnp.inf
    )
    inner_prod = jnp.einsum("ign,jgn->gij", reads, writes, preferred_element_type=jnp.float32)
    weights = (inner_prod[:, None] * jnp.exp(gaps) * step_heads[:, :, None, :]).astype(jnp.bfloat16)
    local_part = jnp.einsum("ghij,jghp->ighp", weights, grouped, preferred_element_type=jnp.float32)
    same_last = (doc_block == doc_block[-1]).astype(jnp.float32)
    tail_weight = jnp.exp(cumulative[-1][None, :] - cumulative) * step_block * same_last[:, None]
    scaled = (
        writes[:, :, None, :].astype(jnp.float32)
        * tail_weight.reshape(block_rows, G, per_group)[:, :, :, None]
    ).astype(jnp.bfloat16)
    states = jnp.einsum(
        "jghn,jghp->ghnp", scaled, grouped, preferred_element_type=jnp.float32
    ).reshape(num_heads, N * width)
    decays = jnp.exp(cumulative[-1]) * (doc_block[0] == doc_block[-1]).astype(jnp.float32)
    return local_part, states, decays, cumulative


def finish(local_part, states_in, last_in, cumulative, read_block, block_input, gains, doc_block):
    block_rows = block_input.shape[0]
    num_heads = cumulative.shape[1]
    per_group = num_heads // G
    width = block_input.shape[1] // num_heads
    carried_in = (doc_block.astype(jnp.float32) == last_in).astype(jnp.float32)
    factor = jnp.exp(cumulative) * carried_in[:, None]
    reads = read_block.reshape(block_rows, G, N).astype(jnp.float32)
    held = states_in.reshape(G, per_group, N, width)
    reached = jnp.einsum("ign,ghnp->ighp", reads, held, precision=lax.Precision.HIGHEST)
    direct = gains.reshape(G, per_group)[None, :, :, None] * block_input.reshape(
        block_rows, G, per_group, width
    ).astype(jnp.float32)
    result = local_part + reached * factor.reshape(block_rows, G, per_group)[:, :, :, None] + direct
    return result.reshape(block_rows, num_heads * width).astype(jnp.bfloat16)


def exclusive_reverse_prod(values):
    inclusive = jnp.flip(jnp.cumprod(jnp.flip(values, 0), axis=0), 0)
    return jnp.concatenate([inclusive[1:], jnp.ones_like(values[:1])], axis=0)


def with_tail(rows, tail):
    pad = TAIL - tail.shape[1]
    tail = jnp.concatenate([tail, jnp.zeros((tail.shape[0], pad), jnp.float32)], axis=1)
    return jnp.concatenate([rows, tail], axis=1)


def local(
    mixer_input, write_vectors, read_vectors, step_sizes, decay_rate, skip_gain, document_ids
):
    num_heads = step_sizes.shape[1]
    n_seq = lax.axis_size("seq")
    n_grp = lax.axis_size("grp")
    me = lax.axis_index("seq")
    grp = lax.axis_index("grp")
    local_part, states, decays, cumulative = local_terms(
        mixer_input, write_vectors, read_vectors, step_sizes, decay_rate, document_ids
    )
    state_width = states.shape[1]
    docs_f = document_ids.astype(jnp.float32)
    first_id = docs_f[0]
    last_id = docs_f[-1]

    flat = states.reshape(n_seq, -1)
    row_len = flat.shape[1]
    row_heads = max(1, num_heads // n_seq)
    sub_len = row_len // row_heads
    heads_of = (np.arange(n_seq)[:, None] * row_len + np.arange(row_heads)[None, :] * sub_len)
    heads_of = heads_of // state_width
    sent_decays = jnp.take(decays, jnp.asarray(heads_of.reshape(-1)), axis=0).reshape(
        n_seq, row_heads
    )
    ids = jnp.broadcast_to(jnp.stack([first_id, last_id])[None, :], (n_seq, 2))
    payload = with_tail(flat, jnp.concatenate([sent_decays, ids], axis=1))
    owned = lax.all_to_all(payload, "seq", 0, 0, tiled=False)
    rows = owned[:, :row_len].reshape(n_seq, row_heads, sub_len)
    blk_decay = owned[:, row_len:row_len + row_heads]
    blk_first = owned[:, row_len + row_heads]
    blk_last = owned[:, row_len + row_heads + 1]

    src = jnp.arange(n_seq)
    prev_last = jnp.concatenate([jnp.full((1,), -1.0, jnp.float32), blk_last[:-1]])
    inner_link = jnp.logical_and(src > 0, blk_first == prev_last).astype(jnp.float32)
    inner_f = blk_decay * inner_link[:, None]
    dest = jnp.arange(n_seq + 1)
    before = (src[:, None] < dest[None, :])[:, :, None]
    gated = jnp.where(before, inner_f[:, None, :], 1.0)
    coef = jnp.where(before, exclusive_reverse_prod(gated), 0.0)
    within = jnp.einsum("tsh,thl->shl", coef, rows, precision=lax.Precision.HIGHEST)

    rest_prod = jnp.prod(inner_f[1:], axis=0)
    grp_tail = jnp.concatenate(
        [rest_prod, blk_decay[0], jnp.stack([blk_first[0], blk_last[-1]])]
    )
    grp_payload = with_tail(within[n_seq].reshape(1, row_len), grp_tail[None, :])
    gathered = lax.all_gather(grp_payload[0], "grp")
    totals = gathered[:, :row_len].reshape(n_grp, row_heads, sub_len)
    g_rest = gathered[:, row_len:row_len + row_heads]
    g_decay0 = gathered[:, row_len + row_heads:row_len + 2 * row_heads]
    g_first = gathered[:, row_len + 2 * row_heads]
    g_last = gathered[:, row_len + 2 * row_heads + 1]
    g_idx = jnp.arange(n_grp)
    g_prev_last = jnp.concatenate([jnp.full((1,), -1.0, jnp.float32), g_last[:-1]])
    g_link = jnp.logical_and(g_idx > 0, g_first == g_prev_last).astype(jnp.float32)
    g_first_f = g_decay0 * g_link[:, None]
    whole_grp = g_rest * g_first_f
    g_before = (g_idx < grp)[:, None]
    g_gated = jnp.where(g_before, whole_grp, 1.0)
    g_coef = jnp.where(g_before, exclusive_reverse_prod(g_gated), 0.0)
    carry = jnp.sum(g_coef[:, :, None] * totals, axis=0)

    my_first_f = jnp.take(g_first_f, grp, axis=0)
    chain_f = jnp.concatenate([my_first_f[None, :], inner_f[1:]], axis=0)
    entry = jnp.concatenate(
        [jnp.ones((1, row_heads), jnp.float32), jnp.cumprod(chain_f, axis=0)[:-1]], axis=0
    )
    result = within[:n_seq] + entry[:, :, None] * carry[None]

    group_prev_last = jnp.where(grp > 0, jnp.take(g_last, jnp.maximum(grp - 1, 0)), -1.0)
    pred_last = jnp.concatenate([group_prev_last[None], blk_last[:-1]])
    back_payload = with_tail(result.reshape(n_seq, row_len), pred_last[:, None])
    back = lax.all_to_all(back_payload, "seq", 0, 0, tiled=False)
    states_in = back[:, :row_len].reshape(num_heads, state_width)
    last_in = back[0, row_len]
    return finish(
        local_part, states_in, last_in, cumulative, read_vectors, mixer_input, skip_gain, document_ids
    )


def solution(mesh):
    in_specs = (
        P(("grp", "seq"), None),
        P(("grp", "seq"), None),
        P(("grp", "seq"), None),
        P(("grp", "seq"), None),
        P(),
        P(),
        P(("grp", "seq")),
    )
    out_specs = P(("grp", "seq"), None)
    return jax.shard_map(local, mesh=mesh, in_specs=in_specs, out_specs=out_specs, check_vma=False)
```

```python
import numpy as np
import jax
import jax.numpy as jnp
from jax import lax
from jax.sharding import PartitionSpec as P

N = 64
G = 4
TAIL = 128


def local_terms(block_input, write_block, read_block, step_block, rates, doc_block):
    block_rows = block_input.shape[0]
    num_heads = step_block.shape[1]
    per_group = num_heads // G
    width = block_input.shape[1] // num_heads
    grouped = block_input.reshape(block_rows, G, per_group, width)
    writes = write_block.reshape(block_rows, G, N)
    reads = read_block.reshape(block_rows, G, N)
    cumulative = jnp.cumsum(-step_block * rates[None, :], axis=0)
    cum_heads = cumulative.T.reshape(G, per_group, block_rows)
    step_heads = step_block.T.reshape(G, per_group, block_rows)
    positions = jnp.arange(block_rows)
    visible = jnp.logical_and(
        doc_block[:, None] == doc_block[None, :], positions[:, None] >= positions[None, :]
    )
    gaps = jnp.where(
        visible[None, None], cum_heads[:, :, :, None] - cum_heads[:, :, None, :], -jnp.inf
    )
    inner_prod = jnp.einsum("ign,jgn->gij", reads, writes, preferred_element_type=jnp.float32)
    weights = (inner_prod[:, None] * jnp.exp(gaps) * step_heads[:, :, None, :]).astype(jnp.bfloat16)
    local_part = jnp.einsum("ghij,jghp->ighp", weights, grouped, preferred_element_type=jnp.float32)
    same_last = (doc_block == doc_block[-1]).astype(jnp.float32)
    tail_weight = jnp.exp(cumulative[-1][None, :] - cumulative) * step_block * same_last[:, None]
    scaled = (
        writes[:, :, None, :].astype(jnp.float32)
        * tail_weight.reshape(block_rows, G, per_group)[:, :, :, None]
    ).astype(jnp.bfloat16)
    states = jnp.einsum(
        "jghn,jghp->ghnp", scaled, grouped, preferred_element_type=jnp.float32
    ).reshape(num_heads, N * width)
    decays = jnp.exp(cumulative[-1]) * (doc_block[0] == doc_block[-1]).astype(jnp.float32)
    return local_part, states, decays, cumulative


def finish(local_part, states_in, last_in, cumulative, read_block, block_input, gains, doc_block):
    block_rows = block_input.shape[0]
    num_heads = cumulative.shape[1]
    per_group = num_heads // G
    width = block_input.shape[1] // num_heads
    carried_in = (doc_block.astype(jnp.float32) == last_in).astype(jnp.float32)
    factor = jnp.exp(cumulative) * carried_in[:, None]
    reads = read_block.reshape(block_rows, G, N).astype(jnp.float32)
    held = states_in.reshape(G, per_group, N, width)
    reached = jnp.einsum("ign,ghnp->ighp", reads, held, precision=lax.Precision.HIGHEST)
    direct = gains.reshape(G, per_group)[None, :, :, None] * block_input.reshape(
        block_rows, G, per_group, width
    ).astype(jnp.float32)
    result = local_part + reached * factor.reshape(block_rows, G, per_group)[:, :, :, None] + direct
    return result.reshape(block_rows, num_heads * width).astype(jnp.bfloat16)


def exclusive_reverse_prod(values):
    inclusive = jnp.flip(jnp.cumprod(jnp.flip(values, 0), axis=0), 0)
    return jnp.concatenate([inclusive[1:], jnp.ones_like(values[:1])], axis=0)


def with_tail(rows, tail):
    pad = TAIL - tail.shape[1]
    tail = jnp.concatenate([tail, jnp.zeros((tail.shape[0], pad), jnp.float32)], axis=1)
    return jnp.concatenate([rows, tail], axis=1)


def local(
    mixer_input, write_vectors, read_vectors, step_sizes, decay_rate, skip_gain, document_ids
):
    num_heads = step_sizes.shape[1]
    axes = ("grp", "seq")
    n_blk = lax.axis_size(axes)
    me = lax.axis_index(axes)
    local_part, states, decays, cumulative = local_terms(
        mixer_input, write_vectors, read_vectors, step_sizes, decay_rate, document_ids
    )
    state_width = states.shape[1]
    docs_f = document_ids.astype(jnp.float32)
    first_id = docs_f[0]
    last_id = docs_f[-1]

    flat = states.reshape(n_blk, -1)
    row_len = flat.shape[1]
    row_heads = max(1, num_heads // n_blk)
    sub_len = row_len // row_heads
    heads_of = (np.arange(n_blk)[:, None] * row_len + np.arange(row_heads)[None, :] * sub_len)
    heads_of = heads_of // state_width
    sent_decays = jnp.take(decays, jnp.asarray(heads_of.reshape(-1)), axis=0).reshape(
        n_blk, row_heads
    )
    ids = jnp.broadcast_to(jnp.stack([first_id, last_id])[None, :], (n_blk, 2))
    payload = with_tail(flat, jnp.concatenate([sent_decays, ids], axis=1))
    owned = lax.all_to_all(payload, axes, 0, 0, tiled=False)
    rows = owned[:, :row_len].reshape(n_blk, row_heads, sub_len)
    blk_decay = owned[:, row_len:row_len + row_heads]
    blk_first = owned[:, row_len + row_heads]
    blk_last = owned[:, row_len + row_heads + 1]

    src = jnp.arange(n_blk)
    prev_last = jnp.concatenate([jnp.full((1,), -1.0, jnp.float32), blk_last[:-1]])
    link = jnp.logical_and(src > 0, blk_first == prev_last).astype(jnp.float32)
    factors = blk_decay * link[:, None]
    before = (src[:, None] < src[None, :])[:, :, None]
    gated = jnp.where(before, factors[:, None, :], 1.0)
    coef = jnp.where(before, exclusive_reverse_prod(gated), 0.0)
    result = jnp.einsum("tsh,thl->shl", coef, rows, precision=lax.Precision.HIGHEST)

    back_payload = with_tail(result.reshape(n_blk, row_len), prev_last[:, None])
    back = lax.all_to_all(back_payload, axes, 0, 0, tiled=False)
    states_in = back[:, :row_len].reshape(num_heads, state_width)
    last_in = back[0, row_len]
    return finish(
        local_part, states_in, last_in, cumulative, read_vectors, mixer_input, skip_gain, document_ids
    )


def solution(mesh):
    in_specs = (
        P(("grp", "seq"), None),
        P(("grp", "seq"), None),
        P(("grp", "seq"), None),
        P(("grp", "seq"), None),
        P(),
        P(),
        P(("grp", "seq")),
    )
    out_specs = P(("grp", "seq"), None)
    return jax.shard_map(local, mesh=mesh, in_specs=in_specs, out_specs=out_specs, check_vma=False)
```

```python
import numpy as np
import jax
import jax.numpy as jnp
from jax import lax
from jax.sharding import PartitionSpec as P

N = 64
G = 4
TAIL = 128


def local_terms(block_input, write_block, read_block, step_block, rates, doc_block):
    block_rows = block_input.shape[0]
    num_heads = step_block.shape[1]
    per_group = num_heads // G
    width = block_input.shape[1] // num_heads
    grouped = block_input.reshape(block_rows, G, per_group, width)
    writes = write_block.reshape(block_rows, G, N)
    reads = read_block.reshape(block_rows, G, N)
    cumulative = jnp.cumsum(-step_block * rates[None, :], axis=0)
    cum_heads = cumulative.T.reshape(G, per_group, block_rows)
    step_heads = step_block.T.reshape(G, per_group, block_rows)
    positions = jnp.arange(block_rows)
    visible = jnp.logical_and(
        doc_block[:, None] == doc_block[None, :], positions[:, None] >= positions[None, :]
    )
    gaps = jnp.where(
        visible[None, None], cum_heads[:, :, :, None] - cum_heads[:, :, None, :], -jnp.inf
    )
    inner_prod = jnp.einsum("ign,jgn->gij", reads, writes, preferred_element_type=jnp.float32)
    weights = (inner_prod[:, None] * jnp.exp(gaps) * step_heads[:, :, None, :]).astype(jnp.bfloat16)
    local_part = jnp.einsum("ghij,jghp->ighp", weights, grouped, preferred_element_type=jnp.float32)
    same_last = (doc_block == doc_block[-1]).astype(jnp.float32)
    tail_weight = jnp.exp(cumulative[-1][None, :] - cumulative) * step_block * same_last[:, None]
    scaled = (
        writes[:, :, None, :].astype(jnp.float32)
        * tail_weight.reshape(block_rows, G, per_group)[:, :, :, None]
    ).astype(jnp.bfloat16)
    states = jnp.einsum(
        "jghn,jghp->ghnp", scaled, grouped, preferred_element_type=jnp.float32
    ).reshape(num_heads, N * width)
    decays = jnp.exp(cumulative[-1]) * (doc_block[0] == doc_block[-1]).astype(jnp.float32)
    return local_part, states, decays, cumulative


def early_terms(local_part, block_input, gains):
    block_rows = block_input.shape[0]
    num_heads = gains.shape[0]
    per_group = num_heads // G
    width = block_input.shape[1] // num_heads
    direct = gains.reshape(G, per_group)[None, :, :, None] * block_input.reshape(
        block_rows, G, per_group, width
    ).astype(jnp.float32)
    return (local_part + direct).reshape(block_rows, num_heads * width)


def finish(early, states_in, last_in, cumulative, read_block, doc_block):
    block_rows = read_block.shape[0]
    num_heads = cumulative.shape[1]
    per_group = num_heads // G
    width = early.shape[1] // num_heads
    carried_in = (doc_block.astype(jnp.float32) == last_in).astype(jnp.float32)
    factor = jnp.exp(cumulative) * carried_in[:, None]
    reads = read_block.reshape(block_rows, G, N).astype(jnp.float32)
    held = states_in.reshape(G, per_group, N, width)
    reached = jnp.einsum("ign,ghnp->ighp", reads, held, precision=lax.Precision.HIGHEST)
    result = early.reshape(block_rows, G, per_group, width) + reached * factor.reshape(
        block_rows, G, per_group
    )[:, :, :, None]
    return result.reshape(block_rows, num_heads * width).astype(jnp.bfloat16)


def exclusive_reverse_prod(values):
    inclusive = jnp.flip(jnp.cumprod(jnp.flip(values, 0), axis=0), 0)
    return jnp.concatenate([inclusive[1:], jnp.ones_like(values[:1])], axis=0)


def with_tail(rows, tail):
    pad = TAIL - tail.shape[1]
    tail = jnp.concatenate([tail, jnp.zeros((tail.shape[0], pad), jnp.float32)], axis=1)
    return jnp.concatenate([rows, tail], axis=1)


def local(
    mixer_input, write_vectors, read_vectors, step_sizes, decay_rate, skip_gain, document_ids
):
    num_heads = step_sizes.shape[1]
    axes = ("grp", "seq")
    n_blk = lax.axis_size(axes)
    me = lax.axis_index(axes)
    local_part, states, decays, cumulative = local_terms(
        mixer_input, write_vectors, read_vectors, step_sizes, decay_rate, document_ids
    )
    state_width = states.shape[1]
    docs_f = document_ids.astype(jnp.float32)
    first_id = docs_f[0]
    last_id = docs_f[-1]

    flat = states.reshape(n_blk, -1)
    row_len = flat.shape[1]
    row_heads = max(1, num_heads // n_blk)
    sub_len = row_len // row_heads
    heads_of = (np.arange(n_blk)[:, None] * row_len + np.arange(row_heads)[None, :] * sub_len)
    heads_of = heads_of // state_width
    sent_decays = jnp.take(decays, jnp.asarray(heads_of.reshape(-1)), axis=0).reshape(
        n_blk, row_heads
    )
    ids = jnp.broadcast_to(jnp.stack([first_id, last_id])[None, :], (n_blk, 2))
    payload = with_tail(flat, jnp.concatenate([sent_decays, ids], axis=1))
    owned = lax.all_to_all(payload, axes, 0, 0, tiled=False)
    early = early_terms(local_part, mixer_input, skip_gain)
    early, owned = lax.optimization_barrier((early, owned))
    rows = owned[:, :row_len].reshape(n_blk, row_heads, sub_len)
    blk_decay = owned[:, row_len:row_len + row_heads]
    blk_first = owned[:, row_len + row_heads]
    blk_last = owned[:, row_len + row_heads + 1]

    src = jnp.arange(n_blk)
    prev_last = jnp.concatenate([jnp.full((1,), -1.0, jnp.float32), blk_last[:-1]])
    link = jnp.logical_and(src > 0, blk_first == prev_last).astype(jnp.float32)
    factors = blk_decay * link[:, None]
    before = (src[:, None] < src[None, :])[:, :, None]
    gated = jnp.where(before, factors[:, None, :], 1.0)
    coef = jnp.where(before, exclusive_reverse_prod(gated), 0.0)
    result = jnp.einsum("tsh,thl->shl", coef, rows, precision=lax.Precision.HIGHEST)

    back_payload = with_tail(result.reshape(n_blk, row_len), prev_last[:, None])
    back = lax.all_to_all(back_payload, axes, 0, 0, tiled=False)
    states_in = back[:, :row_len].reshape(num_heads, state_width)
    last_in = back[0, row_len]
    return finish(early, states_in, last_in, cumulative, read_vectors, document_ids)


def solution(mesh):
    in_specs = (
        P(("grp", "seq"), None),
        P(("grp", "seq"), None),
        P(("grp", "seq"), None),
        P(("grp", "seq"), None),
        P(),
        P(),
        P(("grp", "seq")),
    )
    out_specs = P(("grp", "seq"), None)
    return jax.shard_map(local, mesh=mesh, in_specs=in_specs, out_specs=out_specs, check_vma=False)
```

```python
import numpy as np
import jax
import jax.numpy as jnp
from jax import lax
from jax.sharding import PartitionSpec as P

N = 64
G = 4
TAIL = 128


def local_terms(block_input, write_block, read_block, step_block, rates, doc_block):
    block_rows = block_input.shape[0]
    num_heads = step_block.shape[1]
    per_group = num_heads // G
    width = block_input.shape[1] // num_heads
    grouped = block_input.reshape(block_rows, G, per_group, width)
    writes = write_block.reshape(block_rows, G, N)
    reads = read_block.reshape(block_rows, G, N)
    cumulative = jnp.cumsum(-step_block * rates[None, :], axis=0)
    cum_heads = cumulative.T.reshape(G, per_group, block_rows)
    step_heads = step_block.T.reshape(G, per_group, block_rows)
    positions = jnp.arange(block_rows)
    visible = jnp.logical_and(
        doc_block[:, None] == doc_block[None, :], positions[:, None] >= positions[None, :]
    )
    gaps = jnp.where(
        visible[None, None], cum_heads[:, :, :, None] - cum_heads[:, :, None, :], -jnp.inf
    )
    inner_prod = jnp.einsum("ign,jgn->gij", reads, writes, preferred_element_type=jnp.float32)
    weights = (inner_prod[:, None] * jnp.exp(gaps) * step_heads[:, :, None, :]).astype(jnp.bfloat16)
    local_part = jnp.einsum("ghij,jghp->ighp", weights, grouped, preferred_element_type=jnp.float32)
    same_last = (doc_block == doc_block[-1]).astype(jnp.float32)
    tail_weight = jnp.exp(cumulative[-1][None, :] - cumulative) * step_block * same_last[:, None]
    scaled = (
        writes[:, :, None, :].astype(jnp.float32)
        * tail_weight.reshape(block_rows, G, per_group)[:, :, :, None]
    ).astype(jnp.bfloat16)
    states = jnp.einsum(
        "jghn,jghp->ghnp", scaled, grouped, preferred_element_type=jnp.float32
    )
    states = states.reshape(G, per_group // 2, 2, N, width).transpose(0, 1, 3, 2, 4)
    states = states.reshape(num_heads, N * width)
    decays = jnp.exp(cumulative[-1]) * (doc_block[0] == doc_block[-1]).astype(jnp.float32)
    return local_part, states, decays, cumulative


def early_terms(local_part, block_input, gains):
    block_rows = block_input.shape[0]
    num_heads = gains.shape[0]
    per_group = num_heads // G
    width = block_input.shape[1] // num_heads
    direct = gains.reshape(G, per_group)[None, :, :, None] * block_input.reshape(
        block_rows, G, per_group, width
    ).astype(jnp.float32)
    return (local_part + direct).reshape(block_rows, num_heads * width)


def finish(early, states_in, last_in, cumulative, read_block, doc_block):
    block_rows = read_block.shape[0]
    num_heads = cumulative.shape[1]
    per_group = num_heads // G
    width = early.shape[1] // num_heads
    carried_in = (doc_block.astype(jnp.float32) == last_in).astype(jnp.float32)
    factor = jnp.exp(cumulative) * carried_in[:, None]
    reads = read_block.reshape(block_rows, G, N).astype(jnp.float32)
    held = states_in.reshape(G, per_group // 2, N, 2 * width)
    reached = jnp.einsum("ign,gknq->igkq", reads, held, precision=lax.Precision.HIGHEST)
    spread = jnp.broadcast_to(
        factor.reshape(block_rows, G, per_group // 2, 2, 1),
        (block_rows, G, per_group // 2, 2, width),
    ).reshape(block_rows, G, per_group // 2, 2 * width)
    result = early.reshape(block_rows, G, per_group // 2, 2 * width) + reached * spread
    return result.reshape(block_rows, num_heads * width).astype(jnp.bfloat16)


def exclusive_reverse_prod(values):
    inclusive = jnp.flip(jnp.cumprod(jnp.flip(values, 0), axis=0), 0)
    return jnp.concatenate([inclusive[1:], jnp.ones_like(values[:1])], axis=0)


def width_of(state_width):
    return state_width // N


def with_tail(rows, tail):
    pad = TAIL - tail.shape[1]
    tail = jnp.concatenate([tail, jnp.zeros((tail.shape[0], pad), jnp.float32)], axis=1)
    return jnp.concatenate([rows, tail], axis=1)


def local(
    mixer_input, write_vectors, read_vectors, step_sizes, decay_rate, skip_gain, document_ids
):
    num_heads = step_sizes.shape[1]
    axes = ("grp", "seq")
    n_blk = lax.axis_size(axes)
    me = lax.axis_index(axes)
    local_part, states, decays, cumulative = local_terms(
        mixer_input, write_vectors, read_vectors, step_sizes, decay_rate, document_ids
    )
    state_width = states.shape[1]
    docs_f = document_ids.astype(jnp.float32)
    first_id = docs_f[0]
    last_id = docs_f[-1]

    flat = states.reshape(n_blk, -1)
    row_len = flat.shape[1]
    pair_len = 2 * state_width
    row_heads = 2 * max(1, row_len // pair_len)
    first_head = 2 * ((np.arange(n_blk) * row_len) // pair_len)
    heads_of = first_head[:, None] + np.arange(row_heads)[None, :]
    sent_decays = jnp.take(decays, jnp.asarray(heads_of.reshape(-1)), axis=0).reshape(
        n_blk, row_heads
    )
    ids = jnp.broadcast_to(jnp.stack([first_id, last_id])[None, :], (n_blk, 2))
    payload = with_tail(flat, jnp.concatenate([sent_decays, ids], axis=1))
    owned = lax.all_to_all(payload, axes, 0, 0, tiled=False)
    early = early_terms(local_part, mixer_input, skip_gain)
    early, owned = lax.optimization_barrier((early, owned))
    rows = owned[:, :row_len]
    blk_decay = owned[:, row_len:row_len + row_heads]
    blk_first = owned[:, row_len + row_heads]
    blk_last = owned[:, row_len + row_heads + 1]

    src = jnp.arange(n_blk)
    prev_last = jnp.concatenate([jnp.full((1,), -1.0, jnp.float32), blk_last[:-1]])
    link = jnp.logical_and(src > 0, blk_first == prev_last).astype(jnp.float32)
    factors = blk_decay * link[:, None]
    before = (src[:, None] < src[None, :])[:, :, None]
    gated = jnp.where(before, factors[:, None, :], 1.0)
    coef = jnp.where(before, exclusive_reverse_prod(gated), 0.0)
    lane = np.arange(row_len)
    lane_head = 2 * (lane // pair_len) + (lane // width_of(state_width)) % 2
    result = None
    for j in range(row_heads):
        part = jnp.einsum("ts,tl->sl", coef[:, :, j], rows, precision=lax.Precision.HIGHEST)
        result = part if result is None else jnp.where(jnp.asarray(lane_head == j)[None, :], part, result)

    back_payload = with_tail(result, prev_last[:, None])
    back = lax.all_to_all(back_payload, axes, 0, 0, tiled=False)
    states_in = back[:, :row_len].reshape(num_heads, state_width)
    last_in = back[0, row_len]
    return finish(early, states_in, last_in, cumulative, read_vectors, document_ids)


def solution(mesh):
    in_specs = (
        P(("grp", "seq"), None),
        P(("grp", "seq"), None),
        P(("grp", "seq"), None),
        P(("grp", "seq"), None),
        P(),
        P(),
        P(("grp", "seq")),
    )
    out_specs = P(("grp", "seq"), None)
    return jax.shard_map(local, mesh=mesh, in_specs=in_specs, out_specs=out_specs, check_vma=False)
```

```python
import numpy as np
import jax
import jax.numpy as jnp
from jax import lax
from jax.sharding import PartitionSpec as P
from jax.experimental import pallas as pl

N = 64
G = 4
TAIL = 128


def local_terms(block_input, write_block, read_block, step_block, rates, doc_block):
    block_rows = block_input.shape[0]
    num_heads = step_block.shape[1]
    per_group = num_heads // G
    width = block_input.shape[1] // num_heads
    grouped = block_input.reshape(block_rows, G, per_group, width)
    writes = write_block.reshape(block_rows, G, N)
    reads = read_block.reshape(block_rows, G, N)
    cumulative = jnp.cumsum(-step_block * rates[None, :], axis=0)
    cum_heads = cumulative.T.reshape(G, per_group, block_rows)
    step_heads = step_block.T.reshape(G, per_group, block_rows)
    positions = jnp.arange(block_rows)
    visible = jnp.logical_and(
        doc_block[:, None] == doc_block[None, :], positions[:, None] >= positions[None, :]
    )
    gaps = jnp.where(
        visible[None, None], cum_heads[:, :, :, None] - cum_heads[:, :, None, :], -jnp.inf
    )
    inner_prod = jnp.einsum("ign,jgn->gij", reads, writes, preferred_element_type=jnp.float32)
    weights = (inner_prod[:, None] * jnp.exp(gaps) * step_heads[:, :, None, :]).astype(jnp.bfloat16)
    local_part = jnp.einsum("ghij,jghp->ighp", weights, grouped, preferred_element_type=jnp.float32)
    same_last = (doc_block == doc_block[-1]).astype(jnp.float32)
    tail_weight = jnp.exp(cumulative[-1][None, :] - cumulative) * step_block * same_last[:, None]
    scaled = (
        writes[:, :, None, :].astype(jnp.float32)
        * tail_weight.reshape(block_rows, G, per_group)[:, :, :, None]
    ).astype(jnp.bfloat16)
    states = jnp.einsum(
        "jghn,jghp->ghnp", scaled, grouped, preferred_element_type=jnp.float32
    ).reshape(num_heads, N * width)
    decays = jnp.exp(cumulative[-1]) * (doc_block[0] == doc_block[-1]).astype(jnp.float32)
    return local_part, states, decays, cumulative


def early_terms(local_part, block_input, gains):
    block_rows = block_input.shape[0]
    num_heads = gains.shape[0]
    per_group = num_heads // G
    width = block_input.shape[1] // num_heads
    direct = gains.reshape(G, per_group)[None, :, :, None] * block_input.reshape(
        block_rows, G, per_group, width
    ).astype(jnp.float32)
    return (local_part + direct).reshape(block_rows, num_heads * width)


def finish_kernel(early_ref, cum_ref, carried_ref, reads_ref, pairs_ref, out_ref):
    grp = pl.program_id(0)
    pairs = pairs_ref.shape[0]
    lanes = pairs_ref.shape[2]
    half = lanes // 2
    heads = cum_ref.shape[1]
    factor = jnp.exp(cum_ref[...]) * carried_ref[...]
    reads = reads_ref[...]
    head_row = lax.broadcasted_iota(jnp.int32, (heads, lanes), 0)
    lane_head = lax.broadcasted_iota(jnp.int32, (heads, lanes), 1) // half
    for k in range(pairs):
        pick = (head_row == grp * (2 * pairs) + 2 * k + lane_head).astype(jnp.float32)
        spread = jnp.dot(factor, pick, precision=lax.Precision.HIGHEST,
                         preferred_element_type=jnp.float32)
        reached = jnp.dot(reads, pairs_ref[k], precision=lax.Precision.HIGHEST,
                          preferred_element_type=jnp.float32)
        cols = slice(k * lanes, (k + 1) * lanes)
        out_ref[:, cols] = (early_ref[:, cols] + reached * spread).astype(out_ref.dtype)


def finish(early, states_in, last_in, cumulative, read_block, doc_block):
    block_rows = read_block.shape[0]
    num_heads = cumulative.shape[1]
    per_group = num_heads // G
    width = early.shape[1] // num_heads
    pairs = per_group // 2
    carried_in = (doc_block.astype(jnp.float32) == last_in).astype(jnp.float32)[:, None]
    reads = read_block.reshape(block_rows, G, 1, N).astype(jnp.float32)
    reads2 = jnp.broadcast_to(reads, (block_rows, G, 2, N)).reshape(block_rows, G * 2 * N)
    held = states_in.reshape(num_heads // 2, 2, N, width)
    eye = jnp.eye(2, dtype=jnp.float32)
    diag = held[:, :, :, None, :] * eye[None, :, None, :, None]
    diag = diag.reshape(num_heads // 2, 2 * N, 2 * width)
    lanes = 2 * width
    return pl.pallas_call(
        finish_kernel,
        grid=(G,),
        in_specs=[
            pl.BlockSpec((block_rows, pairs * lanes), lambda g: (0, g)),
            pl.BlockSpec((block_rows, num_heads), lambda g: (0, 0)),
            pl.BlockSpec((block_rows, 1), lambda g: (0, 0)),
            pl.BlockSpec((block_rows, 2 * N), lambda g: (0, g)),
            pl.BlockSpec((pairs, 2 * N, lanes), lambda g: (g, 0, 0)),
        ],
        out_specs=pl.BlockSpec((block_rows, pairs * lanes), lambda g: (0, g)),
        out_shape=jax.ShapeDtypeStruct((block_rows, num_heads * width), jnp.bfloat16),
    )(early, cumulative, carried_in, reads2, diag)


def exclusive_reverse_prod(values):
    inclusive = jnp.flip(jnp.cumprod(jnp.flip(values, 0), axis=0), 0)
    return jnp.concatenate([inclusive[1:], jnp.ones_like(values[:1])], axis=0)


def with_tail(rows, tail):
    pad = TAIL - tail.shape[1]
    tail = jnp.concatenate([tail, jnp.zeros((tail.shape[0], pad), jnp.float32)], axis=1)
    return jnp.concatenate([rows, tail], axis=1)


def local(
    mixer_input, write_vectors, read_vectors, step_sizes, decay_rate, skip_gain, document_ids
):
    num_heads = step_sizes.shape[1]
    axes = ("grp", "seq")
    n_blk = lax.axis_size(axes)
    me = lax.axis_index(axes)
    local_part, states, decays, cumulative = local_terms(
        mixer_input, write_vectors, read_vectors, step_sizes, decay_rate, document_ids
    )
    state_width = states.shape[1]
    docs_f = document_ids.astype(jnp.float32)
    first_id = docs_f[0]
    last_id = docs_f[-1]

    flat = states.reshape(n_blk, -1)
    row_len = flat.shape[1]
    row_heads = max(1, num_heads // n_blk)
    sub_len = row_len // row_heads
    heads_of = (np.arange(n_blk)[:, None] * row_len + np.arange(row_heads)[None, :] * sub_len)
    heads_of = heads_of // state_width
    sent_decays = jnp.take(decays, jnp.asarray(heads_of.reshape(-1)), axis=0).reshape(
        n_blk, row_heads
    )
    ids = jnp.broadcast_to(jnp.stack([first_id, last_id])[None, :], (n_blk, 2))
    payload = with_tail(flat, jnp.concatenate([sent_decays, ids], axis=1))
    owned = lax.all_to_all(payload, axes, 0, 0, tiled=False)
    early = early_terms(local_part, mixer_input, skip_gain)
    early, owned = lax.optimization_barrier((early, owned))
    rows = owned[:, :row_len].reshape(n_blk, row_heads, sub_len)
    blk_decay = owned[:, row_len:row_len + row_heads]
    blk_first = owned[:, row_len + row_heads]
    blk_last = owned[:, row_len + row_heads + 1]

    src = jnp.arange(n_blk)
    prev_last = jnp.concatenate([jnp.full((1,), -1.0, jnp.float32), blk_last[:-1]])
    link = jnp.logical_and(src > 0, blk_first == prev_last).astype(jnp.float32)
    factors = blk_decay * link[:, None]
    before = (src[:, None] < src[None, :])[:, :, None]
    gated = jnp.where(before, factors[:, None, :], 1.0)
    coef = jnp.where(before, exclusive_reverse_prod(gated), 0.0)
    result = jnp.einsum("tsh,thl->shl", coef, rows, precision=lax.Precision.HIGHEST)

    back_payload = with_tail(result.reshape(n_blk, row_len), prev_last[:, None])
    back = lax.all_to_all(back_payload, axes, 0, 0, tiled=False)
    states_in = back[:, :row_len].reshape(num_heads, state_width)
    last_in = back[0, row_len]
    return finish(early, states_in, last_in, cumulative, read_vectors, document_ids)


def solution(mesh):
    in_specs = (
        P(("grp", "seq"), None),
        P(("grp", "seq"), None),
        P(("grp", "seq"), None),
        P(("grp", "seq"), None),
        P(),
        P(),
        P(("grp", "seq")),
    )
    out_specs = P(("grp", "seq"), None)
    return jax.shard_map(local, mesh=mesh, in_specs=in_specs, out_specs=out_specs, check_vma=False)
```

```python
import numpy as np
import jax
import jax.numpy as jnp
from jax import lax
from jax.sharding import PartitionSpec as P

N = 64
G = 4
TAIL = 128


def local_terms(block_input, write_block, read_block, step_block, rates, doc_block):
    block_rows = block_input.shape[0]
    num_heads = step_block.shape[1]
    per_group = num_heads // G
    width = block_input.shape[1] // num_heads
    grouped = block_input.reshape(block_rows, G, per_group, width)
    writes = write_block.reshape(block_rows, G, N)
    reads = read_block.reshape(block_rows, G, N)
    cumulative = jnp.cumsum(-step_block * rates[None, :], axis=0)
    cum_heads = cumulative.T.reshape(G, per_group, block_rows)
    step_heads = step_block.T.reshape(G, per_group, block_rows)
    positions = jnp.arange(block_rows)
    visible = jnp.logical_and(
        doc_block[:, None] == doc_block[None, :], positions[:, None] >= positions[None, :]
    )
    gaps = jnp.where(
        visible[None, None], cum_heads[:, :, :, None] - cum_heads[:, :, None, :], -jnp.inf
    )
    inner_prod = jnp.einsum("ign,jgn->gij", reads, writes, preferred_element_type=jnp.float32)
    weights = (inner_prod[:, None] * jnp.exp(gaps) * step_heads[:, :, None, :]).astype(jnp.bfloat16)
    local_part = jnp.einsum("ghij,jghp->ighp", weights, grouped, preferred_element_type=jnp.float32)
    same_last = (doc_block == doc_block[-1]).astype(jnp.float32)
    tail_weight = jnp.exp(cumulative[-1][None, :] - cumulative) * step_block * same_last[:, None]
    scaled = (
        writes[:, :, None, :].astype(jnp.float32)
        * tail_weight.reshape(block_rows, G, per_group)[:, :, :, None]
    ).astype(jnp.bfloat16)
    states = jnp.einsum(
        "jghn,jghp->ghnp", scaled, grouped, preferred_element_type=jnp.float32
    ).reshape(num_heads, N * width)
    decays = jnp.exp(cumulative[-1]) * (doc_block[0] == doc_block[-1]).astype(jnp.float32)
    return local_part, states, decays, cumulative


def finish(local_part, states_in, last_in, cumulative, read_block, block_input, gains, doc_block):
    block_rows = block_input.shape[0]
    num_heads = cumulative.shape[1]
    per_group = num_heads // G
    width = block_input.shape[1] // num_heads
    carried_in = (doc_block.astype(jnp.float32) == last_in).astype(jnp.float32)
    factor = jnp.exp(cumulative) * carried_in[:, None]
    reads = read_block.reshape(block_rows, G, N).astype(jnp.float32)
    held = states_in.reshape(G, per_group, N, width)
    reached = jnp.einsum("ign,ghnp->ighp", reads, held, precision=lax.Precision.HIGHEST)
    direct = gains.reshape(G, per_group)[None, :, :, None] * block_input.reshape(
        block_rows, G, per_group, width
    ).astype(jnp.float32)
    result = local_part + reached * factor.reshape(block_rows, G, per_group)[:, :, :, None] + direct
    return result.reshape(block_rows, num_heads * width).astype(jnp.bfloat16)


def exclusive_reverse_prod(values):
    inclusive = jnp.flip(jnp.cumprod(jnp.flip(values, 0), axis=0), 0)
    return jnp.concatenate([inclusive[1:], jnp.ones_like(values[:1])], axis=0)


def with_tail(rows, tail):
    pad = TAIL - tail.shape[1]
    tail = jnp.concatenate([tail, jnp.zeros((tail.shape[0], pad), jnp.float32)], axis=1)
    return jnp.concatenate([rows, tail], axis=1)


def local(
    mixer_input, write_vectors, read_vectors, step_sizes, decay_rate, skip_gain, document_ids
):
    num_heads = step_sizes.shape[1]
    axes = ("grp", "seq")
    n_blk = lax.axis_size(axes)
    me = lax.axis_index(axes)
    local_part, states, decays, cumulative = local_terms(
        mixer_input, write_vectors, read_vectors, step_sizes, decay_rate, document_ids
    )
    state_width = states.shape[1]
    docs_f = document_ids.astype(jnp.float32)
    first_id = docs_f[0]
    last_id = docs_f[-1]

    flat = states.reshape(n_blk, -1)
    row_len = flat.shape[1]
    row_heads = max(1, num_heads // n_blk)
    sub_len = row_len // row_heads
    if n_blk <= num_heads:
        sent_decays = decays.reshape(n_blk, row_heads)
    else:
        sent_decays = jnp.repeat(decays, n_blk // num_heads)[:, None]
    ids = jnp.broadcast_to(jnp.stack([first_id, last_id])[None, :], (n_blk, 2))
    tails = with_tail(jnp.zeros((n_blk, 0), jnp.float32), jnp.concatenate([sent_decays, ids], axis=1))
    got = lax.all_to_all(tails, axes, 0, 0, tiled=False)
    blk_decay = got[:, :row_heads]
    blk_first = got[:, row_heads]
    blk_last = got[:, row_heads + 1]

    tile_rows = 8 if row_len % (8 * 128) == 0 else 1
    pieces = flat.reshape(n_blk, tile_rows, row_len // tile_rows)
    owned = lax.all_to_all(pieces, axes, 0, 0, tiled=False)
    rows = owned.reshape(n_blk, row_heads, sub_len)

    src = jnp.arange(n_blk)
    prev_last = jnp.concatenate([jnp.full((1,), -1.0, jnp.float32), blk_last[:-1]])
    link = jnp.logical_and(src > 0, blk_first == prev_last).astype(jnp.float32)
    factors = blk_decay * link[:, None]
    before = (src[:, None] < src[None, :])[:, :, None]
    gated = jnp.where(before, factors[:, None, :], 1.0)
    coef = jnp.where(before, exclusive_reverse_prod(gated), 0.0)
    result = jnp.einsum("tsh,thl->shl", coef, rows, precision=lax.Precision.HIGHEST)

    back = lax.all_to_all(result.reshape(pieces.shape), axes, 0, 0, tiled=False)
    states_in = back.reshape(num_heads, state_width)
    last_in = jnp.where(me > 0, jnp.take(blk_last, jnp.maximum(me - 1, 0)), -1.0)
    return finish(
        local_part, states_in, last_in, cumulative, read_vectors, mixer_input, skip_gain, document_ids
    )


def solution(mesh):
    in_specs = (
        P(("grp", "seq"), None),
        P(("grp", "seq"), None),
        P(("grp", "seq"), None),
        P(("grp", "seq"), None),
        P(),
        P(),
        P(("grp", "seq")),
    )
    out_specs = P(("grp", "seq"), None)
    return jax.shard_map(local, mesh=mesh, in_specs=in_specs, out_specs=out_specs, check_vma=False)
```

```python
import numpy as np
import jax
import jax.numpy as jnp
from jax import lax
from jax.sharding import PartitionSpec as P
from jax.experimental import pallas as pl

N = 64
G = 4
TAIL = 128


def local_terms(block_input, write_block, read_block, step_block, rates, doc_block):
    block_rows = block_input.shape[0]
    num_heads = step_block.shape[1]
    per_group = num_heads // G
    width = block_input.shape[1] // num_heads
    grouped = block_input.reshape(block_rows, G, per_group, width)
    writes = write_block.reshape(block_rows, G, N)
    reads = read_block.reshape(block_rows, G, N)
    cumulative = jnp.cumsum(-step_block * rates[None, :], axis=0)
    cum_heads = cumulative.T.reshape(G, per_group, block_rows)
    step_heads = step_block.T.reshape(G, per_group, block_rows)
    positions = jnp.arange(block_rows)
    visible = jnp.logical_and(
        doc_block[:, None] == doc_block[None, :], positions[:, None] >= positions[None, :]
    )
    gaps = jnp.where(
        visible[None, None], cum_heads[:, :, :, None] - cum_heads[:, :, None, :], -jnp.inf
    )
    inner_prod = jnp.einsum("ign,jgn->gij", reads, writes, preferred_element_type=jnp.float32)
    weights = (inner_prod[:, None] * jnp.exp(gaps) * step_heads[:, :, None, :]).astype(jnp.bfloat16)
    local_part = jnp.einsum("ghij,jghp->ighp", weights, grouped, preferred_element_type=jnp.float32)
    same_last = (doc_block == doc_block[-1]).astype(jnp.float32)
    tail_weight = jnp.exp(cumulative[-1][None, :] - cumulative) * step_block * same_last[:, None]
    scaled = (
        writes[:, :, None, :].astype(jnp.float32)
        * tail_weight.reshape(block_rows, G, per_group)[:, :, :, None]
    ).astype(jnp.bfloat16)
    states = jnp.einsum(
        "jghn,jghp->ghnp", scaled, grouped, preferred_element_type=jnp.float32
    ).reshape(num_heads, N * width)
    decays = jnp.exp(cumulative[-1]) * (doc_block[0] == doc_block[-1]).astype(jnp.float32)
    return local_part, states, decays, cumulative


def early_terms(local_part, block_input, gains):
    block_rows = block_input.shape[0]
    num_heads = gains.shape[0]
    per_group = num_heads // G
    width = block_input.shape[1] // num_heads
    direct = gains.reshape(G, per_group)[None, :, :, None] * block_input.reshape(
        block_rows, G, per_group, width
    ).astype(jnp.float32)
    return (local_part + direct).reshape(block_rows, num_heads * width)


def split_bf16(value):
    high = value.astype(jnp.bfloat16)
    low = (value - high.astype(jnp.float32)).astype(jnp.bfloat16)
    return high, low


def finish_kernel(early_ref, factor_ref, reads_ref, pairs_ref, out_ref):
    pairs = pairs_ref.shape[0]
    lanes = pairs_ref.shape[2]
    rows = reads_ref.shape[1]
    read_hi, read_lo = split_bf16(reads_ref[0])
    lane = lax.broadcasted_iota(jnp.int32, (rows, lanes), 1)
    for k in range(pairs):
        st_hi, st_lo = split_bf16(pairs_ref[k])
        reached = jnp.dot(read_hi, st_hi, preferred_element_type=jnp.float32)
        reached += jnp.dot(read_hi, st_lo, preferred_element_type=jnp.float32)
        reached += jnp.dot(read_lo, st_hi, preferred_element_type=jnp.float32)
        spread = jnp.where(
            lane < lanes // 2, factor_ref[0, :, 2 * k:2 * k + 1], factor_ref[0, :, 2 * k + 1:2 * k + 2]
        )
        cols = slice(k * lanes, (k + 1) * lanes)
        out_ref[:, cols] = (early_ref[:, cols] + reached * spread).astype(out_ref.dtype)


def finish_inputs(cumulative, last_in, read_block, doc_block):
    block_rows = read_block.shape[0]
    num_heads = cumulative.shape[1]
    per_group = num_heads // G
    carried_in = (doc_block.astype(jnp.float32) == last_in).astype(jnp.float32)
    factor = jnp.exp(cumulative) * carried_in[:, None]
    factor = factor.reshape(block_rows, G, per_group).transpose(1, 0, 2)
    reads = read_block.reshape(block_rows, G, 1, N).astype(jnp.float32)
    reads2 = jnp.broadcast_to(reads, (block_rows, G, 2, N)).transpose(1, 0, 2, 3)
    return factor, reads2.reshape(G, block_rows, 2 * N)


def finish(early, factor, reads2, states_in):
    block_rows = early.shape[0]
    num_heads = states_in.shape[0]
    width = early.shape[1] // num_heads
    pairs = num_heads // G // 2
    held = states_in.reshape(num_heads // 2, 2, N, width)
    upper = jnp.pad(held[:, 0], ((0, 0), (0, 0), (0, width)))
    lower = jnp.pad(held[:, 1], ((0, 0), (0, 0), (width, 0)))
    diag = jnp.concatenate([upper, lower], axis=1)
    lanes = 2 * width
    return pl.pallas_call(
        finish_kernel,
        grid=(G,),
        in_specs=[
            pl.BlockSpec((block_rows, pairs * lanes), lambda g: (0, g)),
            pl.BlockSpec((1, block_rows, 2 * pairs), lambda g: (g, 0, 0)),
            pl.BlockSpec((1, block_rows, 2 * N), lambda g: (g, 0, 0)),
            pl.BlockSpec((pairs, 2 * N, lanes), lambda g: (g, 0, 0)),
        ],
        out_specs=pl.BlockSpec((block_rows, pairs * lanes), lambda g: (0, g)),
        out_shape=jax.ShapeDtypeStruct((block_rows, num_heads * width), jnp.bfloat16),
    )(early, factor, reads2, diag)


def exclusive_reverse_prod(values):
    inclusive = jnp.flip(jnp.cumprod(jnp.flip(values, 0), axis=0), 0)
    return jnp.concatenate([inclusive[1:], jnp.ones_like(values[:1])], axis=0)


def with_tail(rows, tail):
    pad = TAIL - tail.shape[1]
    tail = jnp.concatenate([tail, jnp.zeros((tail.shape[0], pad), jnp.float32)], axis=1)
    return jnp.concatenate([rows, tail], axis=1)


def local(
    mixer_input, write_vectors, read_vectors, step_sizes, decay_rate, skip_gain, document_ids
):
    num_heads = step_sizes.shape[1]
    axes = ("grp", "seq")
    n_blk = lax.axis_size(axes)
    me = lax.axis_index(axes)
    local_part, states, decays, cumulative = local_terms(
        mixer_input, write_vectors, read_vectors, step_sizes, decay_rate, document_ids
    )
    state_width = states.shape[1]
    docs_f = document_ids.astype(jnp.float32)
    first_id = docs_f[0]
    last_id = docs_f[-1]

    flat = states.reshape(n_blk, -1)
    row_len = flat.shape[1]
    row_heads = max(1, num_heads // n_blk)
    sub_len = row_len // row_heads
    if n_blk <= num_heads:
        sent_decays = decays.reshape(n_blk, row_heads)
    else:
        sent_decays = jnp.repeat(decays, n_blk // num_heads)[:, None]
    ids = jnp.broadcast_to(jnp.stack([first_id, last_id])[None, :], (n_blk, 2))
    tails = with_tail(jnp.zeros((n_blk, 0), jnp.float32), jnp.concatenate([sent_decays, ids], axis=1))
    got = lax.all_to_all(tails, axes, 0, 0, tiled=False)
    blk_decay = got[:, :row_heads]
    blk_first = got[:, row_heads]
    blk_last = got[:, row_heads + 1]

    tile_rows = 8 if row_len % (8 * 128) == 0 else 1
    pieces = flat.reshape(n_blk, tile_rows, row_len // tile_rows)
    owned = lax.all_to_all(pieces, axes, 0, 0, tiled=False)
    last_in = jnp.where(me > 0, jnp.take(blk_last, jnp.maximum(me - 1, 0)), -1.0)
    early = early_terms(local_part, mixer_input, skip_gain)
    factor, reads2 = finish_inputs(cumulative, last_in, read_vectors, document_ids)
    early, factor, reads2, owned = lax.optimization_barrier((early, factor, reads2, owned))
    rows = owned.reshape(n_blk, row_heads, sub_len)

    src = jnp.arange(n_blk)
    prev_last = jnp.concatenate([jnp.full((1,), -1.0, jnp.float32), blk_last[:-1]])
    link = jnp.logical_and(src > 0, blk_first == prev_last).astype(jnp.float32)
    factors = blk_decay * link[:, None]
    before = (src[:, None] < src[None, :])[:, :, None]
    gated = jnp.where(before, factors[:, None, :], 1.0)
    coef = jnp.where(before, exclusive_reverse_prod(gated), 0.0)
    result = jnp.einsum("tsh,thl->shl", coef, rows, precision=lax.Precision.HIGHEST)

    back = lax.all_to_all(result.reshape(pieces.shape), axes, 0, 0, tiled=False)
    states_in = back.reshape(num_heads, state_width)
    return finish(early, factor, reads2, states_in)


def solution(mesh):
    in_specs = (
        P(("grp", "seq"), None),
        P(("grp", "seq"), None),
        P(("grp", "seq"), None),
        P(("grp", "seq"), None),
        P(),
        P(),
        P(("grp", "seq")),
    )
    out_specs = P(("grp", "seq"), None)
    return jax.shard_map(local, mesh=mesh, in_specs=in_specs, out_specs=out_specs, check_vma=False)
```

```python
import numpy as np
import jax
import jax.numpy as jnp
from jax import lax
from jax.sharding import PartitionSpec as P
from jax.experimental import pallas as pl

N = 64
G = 4
TAIL = 128


def local_terms(block_input, write_block, read_block, step_block, rates, doc_block):
    block_rows = block_input.shape[0]
    num_heads = step_block.shape[1]
    per_group = num_heads // G
    width = block_input.shape[1] // num_heads
    grouped = block_input.reshape(block_rows, G, per_group, width)
    writes = write_block.reshape(block_rows, G, N)
    reads = read_block.reshape(block_rows, G, N)
    cumulative = jnp.cumsum(-step_block * rates[None, :], axis=0)
    cum_heads = cumulative.T.reshape(G, per_group, block_rows)
    step_heads = step_block.T.reshape(G, per_group, block_rows)
    positions = jnp.arange(block_rows)
    visible = jnp.logical_and(
        doc_block[:, None] == doc_block[None, :], positions[:, None] >= positions[None, :]
    )
    gaps = jnp.where(
        visible[None, None], cum_heads[:, :, :, None] - cum_heads[:, :, None, :], -jnp.inf
    )
    inner_prod = jnp.einsum("ign,jgn->gij", reads, writes, preferred_element_type=jnp.float32)
    weights = (inner_prod[:, None] * jnp.exp(gaps) * step_heads[:, :, None, :]).astype(jnp.bfloat16)
    local_part = jnp.einsum("ghij,jghp->ighp", weights, grouped, preferred_element_type=jnp.float32)
    same_last = (doc_block == doc_block[-1]).astype(jnp.float32)
    tail_weight = jnp.exp(cumulative[-1][None, :] - cumulative) * step_block * same_last[:, None]
    scaled = (
        writes[:, :, None, :].astype(jnp.float32)
        * tail_weight.reshape(block_rows, G, per_group)[:, :, :, None]
    ).astype(jnp.bfloat16)
    states = jnp.einsum(
        "jghn,jghp->ghnp", scaled, grouped, preferred_element_type=jnp.float32
    ).reshape(num_heads, N * width)
    decays = jnp.exp(cumulative[-1]) * (doc_block[0] == doc_block[-1]).astype(jnp.float32)
    return local_part, states, decays, cumulative


def early_terms(local_part, block_input, gains):
    block_rows = block_input.shape[0]
    num_heads = gains.shape[0]
    per_group = num_heads // G
    width = block_input.shape[1] // num_heads
    direct = gains.reshape(G, per_group)[None, :, :, None] * block_input.reshape(
        block_rows, G, per_group, width
    ).astype(jnp.float32)
    return (local_part + direct).reshape(block_rows, num_heads * width)


def split_bf16(value):
    high = value.astype(jnp.bfloat16)
    low = (value - high.astype(jnp.float32)).astype(jnp.bfloat16)
    return high, low


def finish_kernel(early_ref, factor_ref, reads_ref, pairs_ref, out_ref):
    pairs = pairs_ref.shape[0]
    lanes = pairs_ref.shape[2]
    rows = reads_ref.shape[1]
    read_hi, read_lo = split_bf16(reads_ref[0])
    lane = lax.broadcasted_iota(jnp.int32, (rows, lanes), 1)
    for k in range(pairs):
        st_hi, st_lo = split_bf16(pairs_ref[k])
        reached = jnp.dot(read_hi, st_hi, preferred_element_type=jnp.float32)
        reached += jnp.dot(read_hi, st_lo, preferred_element_type=jnp.float32)
        reached += jnp.dot(read_lo, st_hi, preferred_element_type=jnp.float32)
        spread = jnp.where(
            lane < lanes // 2, factor_ref[0, :, 2 * k:2 * k + 1], factor_ref[0, :, 2 * k + 1:2 * k + 2]
        )
        cols = slice(k * lanes, (k + 1) * lanes)
        out_ref[:, cols] = (early_ref[:, cols] + reached * spread).astype(out_ref.dtype)


def finish_inputs(cumulative, last_in, read_block, doc_block):
    block_rows = read_block.shape[0]
    num_heads = cumulative.shape[1]
    per_group = num_heads // G
    carried_in = (doc_block.astype(jnp.float32) == last_in).astype(jnp.float32)
    factor = jnp.exp(cumulative) * carried_in[:, None]
    factor = factor.reshape(block_rows, G, per_group).transpose(1, 0, 2)
    reads = read_block.reshape(block_rows, G, 1, N).astype(jnp.float32)
    reads2 = jnp.broadcast_to(reads, (block_rows, G, 2, N)).transpose(1, 0, 2, 3)
    return factor, reads2.reshape(G, block_rows, 2 * N)


def finish(early, factor, reads2, states_in):
    block_rows = early.shape[0]
    num_heads = states_in.shape[0]
    width = early.shape[1] // num_heads
    pairs = num_heads // G // 2
    held = states_in.reshape(num_heads // 2, 2, N, width)
    upper = jnp.pad(held[:, 0], ((0, 0), (0, 0), (0, width)))
    lower = jnp.pad(held[:, 1], ((0, 0), (0, 0), (width, 0)))
    diag = jnp.concatenate([upper, lower], axis=1)
    lanes = 2 * width
    return pl.pallas_call(
        finish_kernel,
        grid=(G,),
        in_specs=[
            pl.BlockSpec((block_rows, pairs * lanes), lambda g: (0, g)),
            pl.BlockSpec((1, block_rows, 2 * pairs), lambda g: (g, 0, 0)),
            pl.BlockSpec((1, block_rows, 2 * N), lambda g: (g, 0, 0)),
            pl.BlockSpec((pairs, 2 * N, lanes), lambda g: (g, 0, 0)),
        ],
        out_specs=pl.BlockSpec((block_rows, pairs * lanes), lambda g: (0, g)),
        out_shape=jax.ShapeDtypeStruct((block_rows, num_heads * width), jnp.bfloat16),
    )(early, factor, reads2, diag)


def exclusive_reverse_prod(values):
    inclusive = jnp.flip(jnp.cumprod(jnp.flip(values, 0), axis=0), 0)
    return jnp.concatenate([inclusive[1:], jnp.ones_like(values[:1])], axis=0)


def with_tail(rows, tail):
    pad = TAIL - tail.shape[1]
    tail = jnp.concatenate([tail, jnp.zeros((tail.shape[0], pad), jnp.float32)], axis=1)
    return jnp.concatenate([rows, tail], axis=1)


def local(
    mixer_input, write_vectors, read_vectors, step_sizes, decay_rate, skip_gain, document_ids
):
    num_heads = step_sizes.shape[1]
    axes = ("grp", "seq")
    n_blk = lax.axis_size(axes)
    me = lax.axis_index(axes)
    local_part, states, decays, cumulative = local_terms(
        mixer_input, write_vectors, read_vectors, step_sizes, decay_rate, document_ids
    )
    state_width = states.shape[1]
    docs_f = document_ids.astype(jnp.float32)
    first_id = docs_f[0]
    last_id = docs_f[-1]

    flat = states.reshape(n_blk, -1)
    row_len = flat.shape[1]
    row_heads = max(1, num_heads // n_blk)
    sub_len = row_len // row_heads
    if n_blk <= num_heads:
        sent_decays = decays.reshape(n_blk, row_heads)
    else:
        sent_decays = jnp.repeat(decays, n_blk // num_heads)[:, None]
    ids = jnp.broadcast_to(jnp.stack([first_id, last_id])[None, :], (n_blk, 2))
    tails = with_tail(jnp.zeros((n_blk, 0), jnp.float32), jnp.concatenate([sent_decays, ids], axis=1))
    got = lax.all_to_all(tails, axes, 0, 0, tiled=False)
    blk_decay = got[:, :row_heads]
    blk_first = got[:, row_heads]
    blk_last = got[:, row_heads + 1]

    tile_rows = 8 if row_len % (8 * 128) == 0 else 1
    pieces = flat.reshape(n_blk, tile_rows, row_len // tile_rows)
    owned = lax.all_to_all(pieces, axes, 0, 0, tiled=False)
    last_in = jnp.where(me > 0, jnp.take(blk_last, jnp.maximum(me - 1, 0)), -1.0)
    early = early_terms(local_part, mixer_input, skip_gain)
    factor, reads2 = finish_inputs(cumulative, last_in, read_vectors, document_ids)
    rows = owned.reshape(n_blk, row_heads, sub_len)

    src = jnp.arange(n_blk)
    prev_last = jnp.concatenate([jnp.full((1,), -1.0, jnp.float32), blk_last[:-1]])
    link = jnp.logical_and(src > 0, blk_first == prev_last).astype(jnp.float32)
    factors = blk_decay * link[:, None]
    before = (src[:, None] < src[None, :])[:, :, None]
    gated = jnp.where(before, factors[:, None, :], 1.0)
    coef = jnp.where(before, exclusive_reverse_prod(gated), 0.0)
    result = jnp.einsum("tsh,thl->shl", coef, rows, precision=lax.Precision.HIGHEST)

    back = lax.all_to_all(result.reshape(pieces.shape), axes, 0, 0, tiled=False)
    states_in = back.reshape(num_heads, state_width)
    return finish(early, factor, reads2, states_in)


def solution(mesh):
    in_specs = (
        P(("grp", "seq"), None),
        P(("grp", "seq"), None),
        P(("grp", "seq"), None),
        P(("grp", "seq"), None),
        P(),
        P(),
        P(("grp", "seq")),
    )
    out_specs = P(("grp", "seq"), None)
    return jax.shard_map(local, mesh=mesh, in_specs=in_specs, out_specs=out_specs, check_vma=False)
```

```python
import numpy as np
import jax
import jax.numpy as jnp
from jax import lax
from jax.sharding import PartitionSpec as P

N = 64
G = 4
TAIL = 128


def local_terms(block_input, write_block, read_block, step_block, rates, doc_block):
    block_rows = block_input.shape[0]
    num_heads = step_block.shape[1]
    per_group = num_heads // G
    width = block_input.shape[1] // num_heads
    grouped = block_input.reshape(block_rows, G, per_group, width)
    writes = write_block.reshape(block_rows, G, N)
    reads = read_block.reshape(block_rows, G, N)
    cumulative = jnp.cumsum(-step_block * rates[None, :], axis=0)
    cum_heads = cumulative.T.reshape(G, per_group, block_rows)
    step_heads = step_block.T.reshape(G, per_group, block_rows)
    positions = jnp.arange(block_rows)
    visible = jnp.logical_and(
        doc_block[:, None] == doc_block[None, :], positions[:, None] >= positions[None, :]
    )
    gaps = jnp.where(
        visible[None, None], cum_heads[:, :, :, None] - cum_heads[:, :, None, :], -jnp.inf
    )
    inner_prod = jnp.einsum("ign,jgn->gij", reads, writes, preferred_element_type=jnp.float32)
    weights = (inner_prod[:, None] * jnp.exp(gaps) * step_heads[:, :, None, :]).astype(jnp.bfloat16)
    local_part = jnp.einsum("ghij,jghp->ighp", weights, grouped, preferred_element_type=jnp.float32)
    same_last = (doc_block == doc_block[-1]).astype(jnp.float32)
    tail_weight = jnp.exp(cumulative[-1][None, :] - cumulative) * step_block * same_last[:, None]
    scaled = (
        writes[:, :, None, :].astype(jnp.float32)
        * tail_weight.reshape(block_rows, G, per_group)[:, :, :, None]
    ).astype(jnp.bfloat16)
    states = jnp.einsum(
        "jghn,jghp->ghnp", scaled, grouped, preferred_element_type=jnp.float32
    ).reshape(num_heads, N * width)
    decays = jnp.exp(cumulative[-1]) * (doc_block[0] == doc_block[-1]).astype(jnp.float32)
    return local_part, states, decays, cumulative


def finish(local_part, states_in, last_in, cumulative, read_block, block_input, gains, doc_block):
    block_rows = block_input.shape[0]
    num_heads = cumulative.shape[1]
    per_group = num_heads // G
    width = block_input.shape[1] // num_heads
    carried_in = (doc_block.astype(jnp.float32) == last_in).astype(jnp.float32)
    factor = jnp.exp(cumulative) * carried_in[:, None]
    reads = read_block.reshape(block_rows, G, N).astype(jnp.float32)
    held = states_in.reshape(G, per_group, N, width)
    reached = jnp.einsum("ign,ghnp->ighp", reads, held, precision=lax.Precision.HIGHEST)
    direct = gains.reshape(G, per_group)[None, :, :, None] * block_input.reshape(
        block_rows, G, per_group, width
    ).astype(jnp.float32)
    result = local_part + reached * factor.reshape(block_rows, G, per_group)[:, :, :, None] + direct
    return result.reshape(block_rows, num_heads * width).astype(jnp.bfloat16)


def exclusive_reverse_prod(values):
    inclusive = jnp.flip(jnp.cumprod(jnp.flip(values, 0), axis=0), 0)
    return jnp.concatenate([inclusive[1:], jnp.ones_like(values[:1])], axis=0)


def with_tail(rows, tail):
    pad = TAIL - tail.shape[1]
    tail = jnp.concatenate([tail, jnp.zeros((tail.shape[0], pad), jnp.float32)], axis=1)
    return jnp.concatenate([rows, tail], axis=1)


def local(
    mixer_input, write_vectors, read_vectors, step_sizes, decay_rate, skip_gain, document_ids
):
    num_heads = step_sizes.shape[1]
    axes = ("grp", "seq")
    n_blk = lax.axis_size(axes)
    me = lax.axis_index(axes)
    local_part, states, decays, cumulative = local_terms(
        mixer_input, write_vectors, read_vectors, step_sizes, decay_rate, document_ids
    )
    state_width = states.shape[1]
    docs_f = document_ids.astype(jnp.float32)
    first_id = docs_f[0]
    last_id = docs_f[-1]

    flat = states.reshape(n_blk, -1)
    row_len = flat.shape[1]
    row_heads = max(1, num_heads // n_blk)
    sub_len = row_len // row_heads
    if n_blk <= num_heads:
        sent_decays = decays.reshape(n_blk, row_heads)
    else:
        sent_decays = jnp.repeat(decays, n_blk // num_heads)[:, None]
    ids = jnp.broadcast_to(jnp.stack([first_id, last_id])[None, :], (n_blk, 2))
    tails = with_tail(jnp.zeros((n_blk, 0), jnp.float32), jnp.concatenate([sent_decays, ids], axis=1))
    got = lax.all_to_all(tails, axes, 0, 0, tiled=False)
    blk_decay = got[:, :row_heads]
    blk_first = got[:, row_heads]
    blk_last = got[:, row_heads + 1]

    head_rows = 8 if sub_len % (8 * 128) == 0 else 1
    pieces = flat.reshape(n_blk, row_heads * head_rows, sub_len // head_rows)
    owned = lax.all_to_all(pieces, axes, 0, 0, tiled=False)

    src = jnp.arange(n_blk)
    prev_last = jnp.concatenate([jnp.full((1,), -1.0, jnp.float32), blk_last[:-1]])
    link = jnp.logical_and(src > 0, blk_first == prev_last).astype(jnp.float32)
    factors = blk_decay * link[:, None]
    before = (src[:, None] < src[None, :])[:, :, None]
    gated = jnp.where(before, factors[:, None, :], 1.0)
    coef = jnp.where(before, exclusive_reverse_prod(gated), 0.0)
    result = jnp.concatenate(
        [
            jnp.einsum(
                "ts,trl->srl",
                coef[:, :, j],
                owned[:, j * head_rows:(j + 1) * head_rows],
                precision=lax.Precision.HIGHEST,
            )
            for j in range(row_heads)
        ],
        axis=1,
    )

    back = lax.all_to_all(result, axes, 0, 0, tiled=False)
    states_in = back.reshape(num_heads, state_width)
    last_in = jnp.where(me > 0, jnp.take(blk_last, jnp.maximum(me - 1, 0)), -1.0)
    return finish(
        local_part, states_in, last_in, cumulative, read_vectors, mixer_input, skip_gain, document_ids
    )


def solution(mesh):
    in_specs = (
        P(("grp", "seq"), None),
        P(("grp", "seq"), None),
        P(("grp", "seq"), None),
        P(("grp", "seq"), None),
        P(),
        P(),
        P(("grp", "seq")),
    )
    out_specs = P(("grp", "seq"), None)
    return jax.shard_map(local, mesh=mesh, in_specs=in_specs, out_specs=out_specs, check_vma=False)
```

```python
import numpy as np
import jax
import jax.numpy as jnp
from jax import lax
from jax.sharding import PartitionSpec as P

N = 64
G = 4
TAIL = 128


def local_terms(block_input, write_block, read_block, step_block, rates, doc_block):
    block_rows = block_input.shape[0]
    num_heads = step_block.shape[1]
    per_group = num_heads // G
    width = block_input.shape[1] // num_heads
    grouped = block_input.reshape(block_rows, G, per_group, width)
    writes = write_block.reshape(block_rows, G, N)
    reads = read_block.reshape(block_rows, G, N)
    cumulative = jnp.cumsum(-step_block * rates[None, :], axis=0)
    cum_heads = cumulative.T.reshape(G, per_group, block_rows)
    step_heads = step_block.T.reshape(G, per_group, block_rows)
    positions = jnp.arange(block_rows)
    visible = jnp.logical_and(
        doc_block[:, None] == doc_block[None, :], positions[:, None] >= positions[None, :]
    )
    gaps = jnp.where(
        visible[None, None], cum_heads[:, :, :, None] - cum_heads[:, :, None, :], -jnp.inf
    )
    inner_prod = jnp.einsum("ign,jgn->gij", reads, writes, preferred_element_type=jnp.float32)
    weights = (inner_prod[:, None] * jnp.exp(gaps) * step_heads[:, :, None, :]).astype(jnp.bfloat16)
    local_part = jnp.einsum("ghij,jghp->ighp", weights, grouped, preferred_element_type=jnp.float32)
    same_last = (doc_block == doc_block[-1]).astype(jnp.float32)
    tail_weight = jnp.exp(cumulative[-1][None, :] - cumulative) * step_block * same_last[:, None]
    scaled = (
        writes[:, :, None, :].astype(jnp.float32)
        * tail_weight.reshape(block_rows, G, per_group)[:, :, :, None]
    ).astype(jnp.bfloat16)
    states = jnp.einsum(
        "jghn,jghp->ghnp", scaled, grouped, preferred_element_type=jnp.float32
    ).reshape(num_heads, N * width)
    decays = jnp.exp(cumulative[-1]) * (doc_block[0] == doc_block[-1]).astype(jnp.float32)
    return local_part, states, decays, cumulative


def finish(local_part, states_in, last_in, cumulative, read_block, block_input, gains, doc_block):
    block_rows = block_input.shape[0]
    num_heads = cumulative.shape[1]
    per_group = num_heads // G
    width = block_input.shape[1] // num_heads
    carried_in = (doc_block.astype(jnp.float32) == last_in).astype(jnp.float32)
    factor = jnp.exp(cumulative) * carried_in[:, None]
    reads = read_block.reshape(block_rows, G, N).astype(jnp.float32)
    held = states_in.reshape(G, per_group, N, width)
    reached = jnp.einsum("ign,ghnp->ighp", reads, held, precision=lax.Precision.HIGHEST)
    direct = gains.reshape(G, per_group)[None, :, :, None] * block_input.reshape(
        block_rows, G, per_group, width
    ).astype(jnp.float32)
    result = local_part + reached * factor.reshape(block_rows, G, per_group)[:, :, :, None] + direct
    return result.reshape(block_rows, num_heads * width).astype(jnp.bfloat16)


def exclusive_reverse_prod(values):
    inclusive = jnp.flip(jnp.cumprod(jnp.flip(values, 0), axis=0), 0)
    return jnp.concatenate([inclusive[1:], jnp.ones_like(values[:1])], axis=0)


def with_tail(rows, tail):
    pad = TAIL - tail.shape[1]
    tail = jnp.concatenate([tail, jnp.zeros((tail.shape[0], pad), jnp.float32)], axis=1)
    return jnp.concatenate([rows, tail], axis=1)


def local(
    mixer_input, write_vectors, read_vectors, step_sizes, decay_rate, skip_gain, document_ids
):
    num_heads = step_sizes.shape[1]
    axes = ("grp", "seq")
    n_blk = lax.axis_size(axes)
    me = lax.axis_index(axes)
    local_part, states, decays, cumulative = local_terms(
        mixer_input, write_vectors, read_vectors, step_sizes, decay_rate, document_ids
    )
    state_width = states.shape[1]
    docs_f = document_ids.astype(jnp.float32)
    first_id = docs_f[0]
    last_id = docs_f[-1]

    flat = states.reshape(n_blk, -1)
    row_len = flat.shape[1]
    row_heads = max(1, num_heads // n_blk)
    sub_len = row_len // row_heads
    if n_blk <= num_heads:
        sent_decays = decays.reshape(n_blk, row_heads)
    else:
        sent_decays = jnp.repeat(decays, n_blk // num_heads)[:, None]
    ids = jnp.broadcast_to(jnp.stack([first_id, last_id])[None, :], (n_blk, 2))
    tails = with_tail(jnp.zeros((n_blk, 0), jnp.float32), jnp.concatenate([sent_decays, ids], axis=1))
    got = lax.all_to_all(tails, axes, 0, 0, tiled=False)

    head_rows = 8 if sub_len % (8 * 128) == 0 else 1
    pieces = flat.reshape(n_blk, row_heads * head_rows, sub_len // head_rows)
    got, pieces = lax.optimization_barrier((got, pieces))
    owned = lax.all_to_all(pieces, axes, 0, 0, tiled=False)
    blk_decay = got[:, :row_heads]
    blk_first = got[:, row_heads]
    blk_last = got[:, row_heads + 1]

    src = jnp.arange(n_blk)
    prev_last = jnp.concatenate([jnp.full((1,), -1.0, jnp.float32), blk_last[:-1]])
    link = jnp.logical_and(src > 0, blk_first == prev_last).astype(jnp.float32)
    factors = blk_decay * link[:, None]
    before = (src[:, None] < src[None, :])[:, :, None]
    gated = jnp.where(before, factors[:, None, :], 1.0)
    coef = jnp.where(before, exclusive_reverse_prod(gated), 0.0)
    result = jnp.concatenate(
        [
            jnp.einsum(
                "ts,trl->srl",
                coef[:, :, j],
                owned[:, j * head_rows:(j + 1) * head_rows],
                precision=lax.Precision.HIGHEST,
            )
            for j in range(row_heads)
        ],
        axis=1,
    )

    back = lax.all_to_all(result, axes, 0, 0, tiled=False)
    states_in = back.reshape(num_heads, state_width)
    last_in = jnp.where(me > 0, jnp.take(blk_last, jnp.maximum(me - 1, 0)), -1.0)
    return finish(
        local_part, states_in, last_in, cumulative, read_vectors, mixer_input, skip_gain, document_ids
    )


def solution(mesh):
    in_specs = (
        P(("grp", "seq"), None),
        P(("grp", "seq"), None),
        P(("grp", "seq"), None),
        P(("grp", "seq"), None),
        P(),
        P(),
        P(("grp", "seq")),
    )
    out_specs = P(("grp", "seq"), None)
    return jax.shard_map(local, mesh=mesh, in_specs=in_specs, out_specs=out_specs, check_vma=False)
```

```python
import numpy as np
import jax
import jax.numpy as jnp
from jax import lax
from jax.sharding import PartitionSpec as P
from jax.experimental import pallas as pl

N = 64
G = 4
TAIL = 128


def local_terms(block_input, write_block, read_block, step_block, rates, doc_block):
    block_rows = block_input.shape[0]
    num_heads = step_block.shape[1]
    per_group = num_heads // G
    width = block_input.shape[1] // num_heads
    grouped = block_input.reshape(block_rows, G, per_group, width)
    writes = write_block.reshape(block_rows, G, N)
    reads = read_block.reshape(block_rows, G, N)
    cumulative = jnp.cumsum(-step_block * rates[None, :], axis=0)
    cum_heads = cumulative.T.reshape(G, per_group, block_rows)
    step_heads = step_block.T.reshape(G, per_group, block_rows)
    positions = jnp.arange(block_rows)
    visible = jnp.logical_and(
        doc_block[:, None] == doc_block[None, :], positions[:, None] >= positions[None, :]
    )
    gaps = jnp.where(
        visible[None, None], cum_heads[:, :, :, None] - cum_heads[:, :, None, :], -jnp.inf
    )
    inner_prod = jnp.einsum("ign,jgn->gij", reads, writes, preferred_element_type=jnp.float32)
    weights = (inner_prod[:, None] * jnp.exp(gaps) * step_heads[:, :, None, :]).astype(jnp.bfloat16)
    local_part = jnp.einsum("ghij,jghp->ighp", weights, grouped, preferred_element_type=jnp.float32)
    same_last = (doc_block == doc_block[-1]).astype(jnp.float32)
    tail_weight = jnp.exp(cumulative[-1][None, :] - cumulative) * step_block * same_last[:, None]
    scaled = (
        writes[:, :, None, :].astype(jnp.float32)
        * tail_weight.reshape(block_rows, G, per_group)[:, :, :, None]
    ).astype(jnp.bfloat16)
    states = jnp.einsum(
        "jghn,jghp->ghnp", scaled, grouped, preferred_element_type=jnp.float32
    ).reshape(num_heads, N * width)
    decays = jnp.exp(cumulative[-1]) * (doc_block[0] == doc_block[-1]).astype(jnp.float32)
    return local_part, states, decays, cumulative


def early_terms(local_part, block_input, gains):
    block_rows = block_input.shape[0]
    num_heads = gains.shape[0]
    per_group = num_heads // G
    width = block_input.shape[1] // num_heads
    direct = gains.reshape(G, per_group)[None, :, :, None] * block_input.reshape(
        block_rows, G, per_group, width
    ).astype(jnp.float32)
    return (local_part + direct).reshape(block_rows, num_heads * width)


def split_bf16(value):
    high = value.astype(jnp.bfloat16)
    low = (value - high.astype(jnp.float32)).astype(jnp.bfloat16)
    return high, low


def finish_kernel(early_ref, factor_ref, reads_ref, pairs_ref, out_ref):
    pairs = pairs_ref.shape[0]
    lanes = pairs_ref.shape[2]
    rows = reads_ref.shape[1]
    read_hi, read_lo = split_bf16(reads_ref[0])
    lane = lax.broadcasted_iota(jnp.int32, (rows, lanes), 1)
    for k in range(pairs):
        st_hi, st_lo = split_bf16(pairs_ref[k])
        reached = jnp.dot(read_hi, st_hi, preferred_element_type=jnp.float32)
        reached += jnp.dot(read_hi, st_lo, preferred_element_type=jnp.float32)
        reached += jnp.dot(read_lo, st_hi, preferred_element_type=jnp.float32)
        spread = jnp.where(
            lane < lanes // 2, factor_ref[0, :, 2 * k:2 * k + 1], factor_ref[0, :, 2 * k + 1:2 * k + 2]
        )
        cols = slice(k * lanes, (k + 1) * lanes)
        out_ref[:, cols] = (early_ref[:, cols] + reached * spread).astype(out_ref.dtype)


def finish_inputs(cumulative, last_in, read_block, doc_block):
    block_rows = read_block.shape[0]
    num_heads = cumulative.shape[1]
    per_group = num_heads // G
    carried_in = (doc_block.astype(jnp.float32) == last_in).astype(jnp.float32)
    factor = jnp.exp(cumulative) * carried_in[:, None]
    factor = factor.reshape(block_rows, G, per_group).transpose(1, 0, 2)
    reads = read_block.reshape(block_rows, G, 1, N).astype(jnp.float32)
    reads2 = jnp.broadcast_to(reads, (block_rows, G, 2, N)).transpose(1, 0, 2, 3)
    return factor, reads2.reshape(G, block_rows, 2 * N)


def finish(early, factor, reads2, states_in):
    block_rows = early.shape[0]
    num_heads = states_in.shape[0]
    width = early.shape[1] // num_heads
    pairs = num_heads // G // 2
    held = states_in.reshape(num_heads // 2, 2, N, width)
    upper = jnp.pad(held[:, 0], ((0, 0), (0, 0), (0, width)))
    lower = jnp.pad(held[:, 1], ((0, 0), (0, 0), (width, 0)))
    diag = jnp.concatenate([upper, lower], axis=1)
    lanes = 2 * width
    return pl.pallas_call(
        finish_kernel,
        grid=(G,),
        in_specs=[
            pl.BlockSpec((block_rows, pairs * lanes), lambda g: (0, g)),
            pl.BlockSpec((1, block_rows, 2 * pairs), lambda g: (g, 0, 0)),
            pl.BlockSpec((1, block_rows, 2 * N), lambda g: (g, 0, 0)),
            pl.BlockSpec((pairs, 2 * N, lanes), lambda g: (g, 0, 0)),
        ],
        out_specs=pl.BlockSpec((block_rows, pairs * lanes), lambda g: (0, g)),
        out_shape=jax.ShapeDtypeStruct((block_rows, num_heads * width), jnp.bfloat16),
    )(early, factor, reads2, diag)


def exclusive_reverse_prod(values):
    inclusive = jnp.flip(jnp.cumprod(jnp.flip(values, 0), axis=0), 0)
    return jnp.concatenate([inclusive[1:], jnp.ones_like(values[:1])], axis=0)


def with_tail(rows, tail):
    pad = TAIL - tail.shape[1]
    tail = jnp.concatenate([tail, jnp.zeros((tail.shape[0], pad), jnp.float32)], axis=1)
    return jnp.concatenate([rows, tail], axis=1)


def local(
    mixer_input, write_vectors, read_vectors, step_sizes, decay_rate, skip_gain, document_ids
):
    num_heads = step_sizes.shape[1]
    axes = ("grp", "seq")
    n_blk = lax.axis_size(axes)
    me = lax.axis_index(axes)
    local_part, states, decays, cumulative = local_terms(
        mixer_input, write_vectors, read_vectors, step_sizes, decay_rate, document_ids
    )
    state_width = states.shape[1]
    docs_f = document_ids.astype(jnp.float32)
    first_id = docs_f[0]
    last_id = docs_f[-1]

    flat = states.reshape(n_blk, -1)
    row_len = flat.shape[1]
    row_heads = max(1, num_heads // n_blk)
    sub_len = row_len // row_heads
    if n_blk <= num_heads:
        sent_decays = decays.reshape(n_blk, row_heads)
    else:
        sent_decays = jnp.repeat(decays, n_blk // num_heads)[:, None]
    ids = jnp.broadcast_to(jnp.stack([first_id, last_id])[None, :], (n_blk, 2))
    tails = with_tail(jnp.zeros((n_blk, 0), jnp.float32), jnp.concatenate([sent_decays, ids], axis=1))
    got = lax.all_to_all(tails, axes, 0, 0, tiled=False)

    head_rows = 8 if sub_len % (8 * 128) == 0 else 1
    pieces = flat.reshape(n_blk, row_heads * head_rows, sub_len // head_rows)
    got, pieces = lax.optimization_barrier((got, pieces))
    owned = lax.all_to_all(pieces, axes, 0, 0, tiled=False)
    blk_decay = got[:, :row_heads]
    blk_first = got[:, row_heads]
    blk_last = got[:, row_heads + 1]
    last_in = jnp.where(me > 0, jnp.take(blk_last, jnp.maximum(me - 1, 0)), -1.0)
    early = early_terms(local_part, mixer_input, skip_gain)
    factor, reads2 = finish_inputs(cumulative, last_in, read_vectors, document_ids)

    src = jnp.arange(n_blk)
    prev_last = jnp.concatenate([jnp.full((1,), -1.0, jnp.float32), blk_last[:-1]])
    link = jnp.logical_and(src > 0, blk_first == prev_last).astype(jnp.float32)
    factors = blk_decay * link[:, None]
    before = (src[:, None] < src[None, :])[:, :, None]
    gated = jnp.where(before, factors[:, None, :], 1.0)
    coef = jnp.where(before, exclusive_reverse_prod(gated), 0.0)
    result = jnp.concatenate(
        [
            jnp.einsum(
                "ts,trl->srl",
                coef[:, :, j],
                owned[:, j * head_rows:(j + 1) * head_rows],
                precision=lax.Precision.HIGHEST,
            )
            for j in range(row_heads)
        ],
        axis=1,
    )

    back = lax.all_to_all(result, axes, 0, 0, tiled=False)
    states_in = back.reshape(num_heads, state_width)
    return finish(early, factor, reads2, states_in)


def solution(mesh):
    in_specs = (
        P(("grp", "seq"), None),
        P(("grp", "seq"), None),
        P(("grp", "seq"), None),
        P(("grp", "seq"), None),
        P(),
        P(),
        P(("grp", "seq")),
    )
    out_specs = P(("grp", "seq"), None)
    return jax.shard_map(local, mesh=mesh, in_specs=in_specs, out_specs=out_specs, check_vma=False)
```

```python
import numpy as np
import jax
import jax.numpy as jnp
from jax import lax
from jax.sharding import PartitionSpec as P
from jax.experimental import pallas as pl

N = 64
G = 4
TAIL = 128


def local_terms(block_input, write_block, read_block, step_block, rates, doc_block):
    block_rows = block_input.shape[0]
    num_heads = step_block.shape[1]
    per_group = num_heads // G
    width = block_input.shape[1] // num_heads
    grouped = block_input.reshape(block_rows, G, per_group, width)
    writes = write_block.reshape(block_rows, G, N)
    reads = read_block.reshape(block_rows, G, N)
    cumulative = jnp.cumsum(-step_block * rates[None, :], axis=0)
    cum_heads = cumulative.T.reshape(G, per_group, block_rows)
    step_heads = step_block.T.reshape(G, per_group, block_rows)
    positions = jnp.arange(block_rows)
    visible = jnp.logical_and(
        doc_block[:, None] == doc_block[None, :], positions[:, None] >= positions[None, :]
    )
    gaps = jnp.where(
        visible[None, None], cum_heads[:, :, :, None] - cum_heads[:, :, None, :], -jnp.inf
    )
    inner_prod = jnp.einsum("ign,jgn->gij", reads, writes, preferred_element_type=jnp.float32)
    weights = (inner_prod[:, None] * jnp.exp(gaps) * step_heads[:, :, None, :]).astype(jnp.bfloat16)
    local_part = jnp.einsum("ghij,jghp->ighp", weights, grouped, preferred_element_type=jnp.float32)
    same_last = (doc_block == doc_block[-1]).astype(jnp.float32)
    tail_weight = jnp.exp(cumulative[-1][None, :] - cumulative) * step_block * same_last[:, None]
    scaled = (
        writes[:, :, None, :].astype(jnp.float32)
        * tail_weight.reshape(block_rows, G, per_group)[:, :, :, None]
    ).astype(jnp.bfloat16)
    states = jnp.einsum(
        "jghn,jghp->ghnp", scaled, grouped, preferred_element_type=jnp.float32
    ).reshape(num_heads, N * width)
    decays = jnp.exp(cumulative[-1]) * (doc_block[0] == doc_block[-1]).astype(jnp.float32)
    return local_part, states, decays, cumulative


def early_terms(local_part, block_input, gains):
    block_rows = block_input.shape[0]
    num_heads = gains.shape[0]
    per_group = num_heads // G
    width = block_input.shape[1] // num_heads
    direct = gains.reshape(G, per_group)[None, :, :, None] * block_input.reshape(
        block_rows, G, per_group, width
    ).astype(jnp.float32)
    return (local_part + direct).reshape(block_rows, num_heads * width)


def split_bf16(value):
    high = value.astype(jnp.bfloat16)
    low = (value - high.astype(jnp.float32)).astype(jnp.bfloat16)
    return high, low


def finish_kernel(early_ref, factor_ref, reads_ref, pairs_ref, out_ref):
    pairs = pairs_ref.shape[0]
    lanes = pairs_ref.shape[2]
    depth = pairs_ref.shape[1] // 2
    rows = reads_ref.shape[1]
    read_hi, read_lo = split_bf16(reads_ref[0])
    lhs = jnp.concatenate([read_hi, read_hi, read_lo], axis=1)
    lane = lax.broadcasted_iota(jnp.int32, (rows, lanes), 1)
    for k in range(pairs):
        tile = pairs_ref[k]
        rhs = jnp.concatenate([tile, tile[:depth]], axis=0)
        reached = jnp.dot(lhs, rhs, preferred_element_type=jnp.float32)
        spread = jnp.where(
            lane < lanes // 2, factor_ref[0, :, 2 * k:2 * k + 1], factor_ref[0, :, 2 * k + 1:2 * k + 2]
        )
        cols = slice(k * lanes, (k + 1) * lanes)
        out_ref[:, cols] = (early_ref[:, cols] + reached * spread).astype(out_ref.dtype)


def finish_inputs(cumulative, last_in, read_block, doc_block):
    block_rows = read_block.shape[0]
    num_heads = cumulative.shape[1]
    per_group = num_heads // G
    carried_in = (doc_block.astype(jnp.float32) == last_in).astype(jnp.float32)
    factor = jnp.exp(cumulative) * carried_in[:, None]
    factor = factor.reshape(block_rows, G, per_group).transpose(1, 0, 2)
    reads = read_block.reshape(block_rows, G, 1, N).astype(jnp.float32)
    reads2 = jnp.broadcast_to(reads, (block_rows, G, 2, N)).transpose(1, 0, 2, 3)
    return factor, reads2.reshape(G, block_rows, 2 * N)


def finish(early, factor, reads2, states_in):
    block_rows = early.shape[0]
    num_heads = states_in.shape[0]
    width = early.shape[1] // num_heads
    pairs = num_heads // G // 2
    held = states_in.reshape(num_heads // 2, 2, N, width)
    upper = jnp.pad(held[:, 0], ((0, 0), (0, 0), (0, width)))
    lower = jnp.pad(held[:, 1], ((0, 0), (0, 0), (width, 0)))
    diag = jnp.concatenate([upper, lower], axis=1)
    diag_hi, diag_lo = split_bf16(diag)
    diag = jnp.concatenate([diag_hi, diag_lo], axis=1)
    lanes = 2 * width
    return pl.pallas_call(
        finish_kernel,
        grid=(G,),
        in_specs=[
            pl.BlockSpec((block_rows, pairs * lanes), lambda g: (0, g)),
            pl.BlockSpec((1, block_rows, 2 * pairs), lambda g: (g, 0, 0)),
            pl.BlockSpec((1, block_rows, 2 * N), lambda g: (g, 0, 0)),
            pl.BlockSpec((pairs, 4 * N, lanes), lambda g: (g, 0, 0)),
        ],
        out_specs=pl.BlockSpec((block_rows, pairs * lanes), lambda g: (0, g)),
        out_shape=jax.ShapeDtypeStruct((block_rows, num_heads * width), jnp.bfloat16),
    )(early, factor, reads2, diag)


def exclusive_reverse_prod(values):
    inclusive = jnp.flip(jnp.cumprod(jnp.flip(values, 0), axis=0), 0)
    return jnp.concatenate([inclusive[1:], jnp.ones_like(values[:1])], axis=0)


def with_tail(rows, tail):
    pad = TAIL - tail.shape[1]
    tail = jnp.concatenate([tail, jnp.zeros((tail.shape[0], pad), jnp.float32)], axis=1)
    return jnp.concatenate([rows, tail], axis=1)


def local(
    mixer_input, write_vectors, read_vectors, step_sizes, decay_rate, skip_gain, document_ids
):
    num_heads = step_sizes.shape[1]
    axes = ("grp", "seq")
    n_blk = lax.axis_size(axes)
    me = lax.axis_index(axes)
    local_part, states, decays, cumulative = local_terms(
        mixer_input, write_vectors, read_vectors, step_sizes, decay_rate, document_ids
    )
    state_width = states.shape[1]
    docs_f = document_ids.astype(jnp.float32)
    first_id = docs_f[0]
    last_id = docs_f[-1]

    flat = states.reshape(n_blk, -1)
    row_len = flat.shape[1]
    row_heads = max(1, num_heads // n_blk)
    sub_len = row_len // row_heads
    if n_blk <= num_heads:
        sent_decays = decays.reshape(n_blk, row_heads)
    else:
        sent_decays = jnp.repeat(decays, n_blk // num_heads)[:, None]
    ids = jnp.broadcast_to(jnp.stack([first_id, last_id])[None, :], (n_blk, 2))
    tails = with_tail(jnp.zeros((n_blk, 0), jnp.float32), jnp.concatenate([sent_decays, ids], axis=1))
    got = lax.all_to_all(tails, axes, 0, 0, tiled=False)

    head_rows = 8 if sub_len % (8 * 128) == 0 else 1
    pieces = flat.reshape(n_blk, row_heads * head_rows, sub_len // head_rows)
    got, pieces = lax.optimization_barrier((got, pieces))
    owned = lax.all_to_all(pieces, axes, 0, 0, tiled=False)
    blk_decay = got[:, :row_heads]
    blk_first = got[:, row_heads]
    blk_last = got[:, row_heads + 1]
    last_in = jnp.where(me > 0, jnp.take(blk_last, jnp.maximum(me - 1, 0)), -1.0)
    early = early_terms(local_part, mixer_input, skip_gain)
    factor, reads2 = finish_inputs(cumulative, last_in, read_vectors, document_ids)

    src = jnp.arange(n_blk)
    prev_last = jnp.concatenate([jnp.full((1,), -1.0, jnp.float32), blk_last[:-1]])
    link = jnp.logical_and(src > 0, blk_first == prev_last).astype(jnp.float32)
    factors = blk_decay * link[:, None]
    before = (src[:, None] < src[None, :])[:, :, None]
    gated = jnp.where(before, factors[:, None, :], 1.0)
    coef = jnp.where(before, exclusive_reverse_prod(gated), 0.0)
    result = jnp.concatenate(
        [
            jnp.einsum(
                "ts,trl->srl",
                coef[:, :, j],
                owned[:, j * head_rows:(j + 1) * head_rows],
                precision=lax.Precision.HIGHEST,
            )
            for j in range(row_heads)
        ],
        axis=1,
    )

    back = lax.all_to_all(result, axes, 0, 0, tiled=False)
    states_in = back.reshape(num_heads, state_width)
    return finish(early, factor, reads2, states_in)


def solution(mesh):
    in_specs = (
        P(("grp", "seq"), None),
        P(("grp", "seq"), None),
        P(("grp", "seq"), None),
        P(("grp", "seq"), None),
        P(),
        P(),
        P(("grp", "seq")),
    )
    out_specs = P(("grp", "seq"), None)
    return jax.shard_map(local, mesh=mesh, in_specs=in_specs, out_specs=out_specs, check_vma=False)
```

```python
import numpy as np
import jax
import jax.numpy as jnp
from jax import lax
from jax.sharding import PartitionSpec as P
from jax.experimental import pallas as pl

N = 64
G = 4
TAIL = 128


def local_terms(block_input, write_block, read_block, step_block, rates, doc_block):
    block_rows = block_input.shape[0]
    num_heads = step_block.shape[1]
    per_group = num_heads // G
    width = block_input.shape[1] // num_heads
    grouped = block_input.reshape(block_rows, G, per_group, width)
    writes = write_block.reshape(block_rows, G, N)
    reads = read_block.reshape(block_rows, G, N)
    cumulative = jnp.cumsum(-step_block * rates[None, :], axis=0)
    cum_heads = cumulative.T.reshape(G, per_group, block_rows)
    step_heads = step_block.T.reshape(G, per_group, block_rows)
    positions = jnp.arange(block_rows)
    visible = jnp.logical_and(
        doc_block[:, None] == doc_block[None, :], positions[:, None] >= positions[None, :]
    )
    gaps = jnp.where(
        visible[None, None], cum_heads[:, :, :, None] - cum_heads[:, :, None, :], -jnp.inf
    )
    inner_prod = jnp.einsum("ign,jgn->gij", reads, writes, preferred_element_type=jnp.float32)
    weights = (inner_prod[:, None] * jnp.exp(gaps) * step_heads[:, :, None, :]).astype(jnp.bfloat16)
    local_part = jnp.einsum("ghij,jghp->ighp", weights, grouped, preferred_element_type=jnp.float32)
    same_last = (doc_block == doc_block[-1]).astype(jnp.float32)
    tail_weight = jnp.exp(cumulative[-1][None, :] - cumulative) * step_block * same_last[:, None]
    scaled = (
        writes[:, :, None, :].astype(jnp.float32)
        * tail_weight.reshape(block_rows, G, per_group)[:, :, :, None]
    ).astype(jnp.bfloat16)
    states = jnp.einsum(
        "jghn,jghp->ghnp", scaled, grouped, preferred_element_type=jnp.float32
    ).reshape(num_heads, N * width)
    decays = jnp.exp(cumulative[-1]) * (doc_block[0] == doc_block[-1]).astype(jnp.float32)
    return local_part, states, decays, cumulative


def early_terms(local_part, block_input, gains):
    block_rows = block_input.shape[0]
    num_heads = gains.shape[0]
    per_group = num_heads // G
    width = block_input.shape[1] // num_heads
    direct = gains.reshape(G, per_group)[None, :, :, None] * block_input.reshape(
        block_rows, G, per_group, width
    ).astype(jnp.float32)
    return (local_part + direct).reshape(block_rows, num_heads * width)


def split_bf16(value):
    high = value.astype(jnp.bfloat16)
    low = (value - high.astype(jnp.float32)).astype(jnp.bfloat16)
    return high, low


def finish_kernel(early_ref, factor_ref, reads_ref, pairs_ref, out_ref):
    pairs = pairs_ref.shape[0]
    lanes = pairs_ref.shape[2]
    rows = reads_ref.shape[1]
    read_hi, read_lo = split_bf16(reads_ref[0])
    lane = lax.broadcasted_iota(jnp.int32, (rows, lanes), 1)
    for k in range(pairs):
        st_hi, st_lo = split_bf16(pairs_ref[k])
        reached = jnp.dot(read_hi, st_hi, preferred_element_type=jnp.float32)
        reached += jnp.dot(read_hi, st_lo, preferred_element_type=jnp.float32)
        reached += jnp.dot(read_lo, st_hi, preferred_element_type=jnp.float32)
        spread = jnp.where(
            lane < lanes // 2, factor_ref[0, :, 2 * k:2 * k + 1], factor_ref[0, :, 2 * k + 1:2 * k + 2]
        )
        cols = slice(k * lanes, (k + 1) * lanes)
        out_ref[:, cols] = (early_ref[:, cols] + reached * spread).astype(out_ref.dtype)


def finish_inputs(cumulative, last_in, read_block, doc_block):
    block_rows = read_block.shape[0]
    num_heads = cumulative.shape[1]
    per_group = num_heads // G
    carried_in = (doc_block.astype(jnp.float32) == last_in).astype(jnp.float32)
    factor = jnp.exp(cumulative) * carried_in[:, None]
    factor = factor.reshape(block_rows, 2 * G, per_group // 2).transpose(1, 0, 2)
    reads = read_block.reshape(block_rows, G, 1, N).astype(jnp.float32)
    reads2 = jnp.broadcast_to(reads, (block_rows, G, 2, N)).transpose(1, 0, 2, 3)
    return factor, reads2.reshape(G, block_rows, 2 * N)


def finish(early, factor, reads2, states_in):
    block_rows = early.shape[0]
    num_heads = states_in.shape[0]
    width = early.shape[1] // num_heads
    pairs = num_heads // G // 4
    held = states_in.reshape(num_heads // 2, 2, N, width)
    upper = jnp.pad(held[:, 0], ((0, 0), (0, 0), (0, width)))
    lower = jnp.pad(held[:, 1], ((0, 0), (0, 0), (width, 0)))
    diag = jnp.concatenate([upper, lower], axis=1)
    lanes = 2 * width
    return pl.pallas_call(
        finish_kernel,
        grid=(2 * G,),
        in_specs=[
            pl.BlockSpec((block_rows, pairs * lanes), lambda g: (0, g)),
            pl.BlockSpec((1, block_rows, 2 * pairs), lambda g: (g, 0, 0)),
            pl.BlockSpec((1, block_rows, 2 * N), lambda g: (g // 2, 0, 0)),
            pl.BlockSpec((pairs, 2 * N, lanes), lambda g: (g, 0, 0)),
        ],
        out_specs=pl.BlockSpec((block_rows, pairs * lanes), lambda g: (0, g)),
        out_shape=jax.ShapeDtypeStruct((block_rows, num_heads * width), jnp.bfloat16),
    )(early, factor, reads2, diag)


def exclusive_reverse_prod(values):
    inclusive = jnp.flip(jnp.cumprod(jnp.flip(values, 0), axis=0), 0)
    return jnp.concatenate([inclusive[1:], jnp.ones_like(values[:1])], axis=0)


def with_tail(rows, tail):
    pad = TAIL - tail.shape[1]
    tail = jnp.concatenate([tail, jnp.zeros((tail.shape[0], pad), jnp.float32)], axis=1)
    return jnp.concatenate([rows, tail], axis=1)


def local(
    mixer_input, write_vectors, read_vectors, step_sizes, decay_rate, skip_gain, document_ids
):
    num_heads = step_sizes.shape[1]
    axes = ("grp", "seq")
    n_blk = lax.axis_size(axes)
    me = lax.axis_index(axes)
    local_part, states, decays, cumulative = local_terms(
        mixer_input, write_vectors, read_vectors, step_sizes, decay_rate, document_ids
    )
    state_width = states.shape[1]
    docs_f = document_ids.astype(jnp.float32)
    first_id = docs_f[0]
    last_id = docs_f[-1]

    flat = states.reshape(n_blk, -1)
    row_len = flat.shape[1]
    row_heads = max(1, num_heads // n_blk)
    sub_len = row_len // row_heads
    if n_blk <= num_heads:
        sent_decays = decays.reshape(n_blk, row_heads)
    else:
        sent_decays = jnp.repeat(decays, n_blk // num_heads)[:, None]
    ids = jnp.broadcast_to(jnp.stack([first_id, last_id])[None, :], (n_blk, 2))
    tails = with_tail(jnp.zeros((n_blk, 0), jnp.float32), jnp.concatenate([sent_decays, ids], axis=1))
    got = lax.all_to_all(tails, axes, 0, 0, tiled=False)

    head_rows = 8 if sub_len % (8 * 128) == 0 else 1
    pieces = flat.reshape(n_blk, row_heads * head_rows, sub_len // head_rows)
    got, pieces = lax.optimization_barrier((got, pieces))
    owned = lax.all_to_all(pieces, axes, 0, 0, tiled=False)
    blk_decay = got[:, :row_heads]
    blk_first = got[:, row_heads]
    blk_last = got[:, row_heads + 1]
    last_in = jnp.where(me > 0, jnp.take(blk_last, jnp.maximum(me - 1, 0)), -1.0)
    early = early_terms(local_part, mixer_input, skip_gain)
    factor, reads2 = finish_inputs(cumulative, last_in, read_vectors, document_ids)

    src = jnp.arange(n_blk)
    prev_last = jnp.concatenate([jnp.full((1,), -1.0, jnp.float32), blk_last[:-1]])
    link = jnp.logical_and(src > 0, blk_first == prev_last).astype(jnp.float32)
    factors = blk_decay * link[:, None]
    before = (src[:, None] < src[None, :])[:, :, None]
    gated = jnp.where(before, factors[:, None, :], 1.0)
    coef = jnp.where(before, exclusive_reverse_prod(gated), 0.0)
    result = jnp.concatenate(
        [
            jnp.einsum(
                "ts,trl->srl",
                coef[:, :, j],
                owned[:, j * head_rows:(j + 1) * head_rows],
                precision=lax.Precision.HIGHEST,
            )
            for j in range(row_heads)
        ],
        axis=1,
    )

    back = lax.all_to_all(result, axes, 0, 0, tiled=False)
    states_in = back.reshape(num_heads, state_width)
    return finish(early, factor, reads2, states_in)


def solution(mesh):
    in_specs = (
        P(("grp", "seq"), None),
        P(("grp", "seq"), None),
        P(("grp", "seq"), None),
        P(("grp", "seq"), None),
        P(),
        P(),
        P(("grp", "seq")),
    )
    out_specs = P(("grp", "seq"), None)
    return jax.shard_map(local, mesh=mesh, in_specs=in_specs, out_specs=out_specs, check_vma=False)
```

```python
import numpy as np
import jax
import jax.numpy as jnp
from jax import lax
from jax.sharding import PartitionSpec as P
from jax.experimental import pallas as pl

N = 64
G = 4
TAIL = 128


def local_terms(block_input, write_block, read_block, step_block, rates, doc_block):
    block_rows = block_input.shape[0]
    num_heads = step_block.shape[1]
    per_group = num_heads // G
    width = block_input.shape[1] // num_heads
    grouped = block_input.reshape(block_rows, G, per_group, width)
    writes = write_block.reshape(block_rows, G, N)
    reads = read_block.reshape(block_rows, G, N)
    cumulative = jnp.cumsum(-step_block * rates[None, :], axis=0)
    cum_heads = cumulative.T.reshape(G, per_group, block_rows)
    step_heads = step_block.T.reshape(G, per_group, block_rows)
    positions = jnp.arange(block_rows)
    visible = jnp.logical_and(
        doc_block[:, None] == doc_block[None, :], positions[:, None] >= positions[None, :]
    )
    gaps = jnp.where(
        visible[None, None], cum_heads[:, :, :, None] - cum_heads[:, :, None, :], -jnp.inf
    )
    inner_prod = jnp.einsum("ign,jgn->gij", reads, writes, preferred_element_type=jnp.float32)
    weights = (inner_prod[:, None] * jnp.exp(gaps) * step_heads[:, :, None, :]).astype(jnp.bfloat16)
    local_part = jnp.einsum("ghij,jghp->ighp", weights, grouped, preferred_element_type=jnp.float32)
    same_last = (doc_block == doc_block[-1]).astype(jnp.float32)
    tail_weight = jnp.exp(cumulative[-1][None, :] - cumulative) * step_block * same_last[:, None]
    scaled = (
        writes[:, :, None, :].astype(jnp.float32)
        * tail_weight.reshape(block_rows, G, per_group)[:, :, :, None]
    ).astype(jnp.bfloat16)
    states = jnp.einsum(
        "jghn,jghp->ghnp", scaled, grouped, preferred_element_type=jnp.float32
    ).reshape(num_heads, N * width)
    decays = jnp.exp(cumulative[-1]) * (doc_block[0] == doc_block[-1]).astype(jnp.float32)
    return local_part, states, decays, cumulative


def early_terms(local_part, block_input, gains):
    block_rows = block_input.shape[0]
    num_heads = gains.shape[0]
    per_group = num_heads // G
    width = block_input.shape[1] // num_heads
    direct = gains.reshape(G, per_group)[None, :, :, None] * block_input.reshape(
        block_rows, G, per_group, width
    ).astype(jnp.float32)
    return (local_part + direct).reshape(block_rows, num_heads * width)


def split_bf16(value):
    high = value.astype(jnp.bfloat16)
    low = (value - high.astype(jnp.float32)).astype(jnp.bfloat16)
    return high, low


def finish_kernel(early_ref, factor_ref, reads_ref, pairs_ref, out_ref):
    pairs = pairs_ref.shape[0]
    lanes = pairs_ref.shape[2]
    rows = reads_ref.shape[1]
    per_read = pairs // reads_ref.shape[0]
    lane = lax.broadcasted_iota(jnp.int32, (rows, lanes), 1)
    for k in range(pairs):
        if k % per_read == 0:
            read_hi, read_lo = split_bf16(reads_ref[k // per_read])
        st_hi, st_lo = split_bf16(pairs_ref[k])
        reached = jnp.dot(read_hi, st_hi, preferred_element_type=jnp.float32)
        reached += jnp.dot(read_hi, st_lo, preferred_element_type=jnp.float32)
        reached += jnp.dot(read_lo, st_hi, preferred_element_type=jnp.float32)
        spread = jnp.where(
            lane < lanes // 2, factor_ref[0, :, 2 * k:2 * k + 1], factor_ref[0, :, 2 * k + 1:2 * k + 2]
        )
        cols = slice(k * lanes, (k + 1) * lanes)
        out_ref[:, cols] = (early_ref[:, cols] + reached * spread).astype(out_ref.dtype)


def finish_inputs(cumulative, last_in, read_block, doc_block):
    block_rows = read_block.shape[0]
    num_heads = cumulative.shape[1]
    per_group = num_heads // G
    carried_in = (doc_block.astype(jnp.float32) == last_in).astype(jnp.float32)
    factor = jnp.exp(cumulative) * carried_in[:, None]
    factor = factor.reshape(block_rows, G // 2, 2 * per_group).transpose(1, 0, 2)
    reads = read_block.reshape(block_rows, G, 1, N).astype(jnp.float32)
    reads2 = jnp.broadcast_to(reads, (block_rows, G, 2, N)).transpose(1, 0, 2, 3)
    return factor, reads2.reshape(G, block_rows, 2 * N)


def finish(early, factor, reads2, states_in):
    block_rows = early.shape[0]
    num_heads = states_in.shape[0]
    width = early.shape[1] // num_heads
    pairs = num_heads // G
    held = states_in.reshape(num_heads // 2, 2, N, width)
    upper = jnp.pad(held[:, 0], ((0, 0), (0, 0), (0, width)))
    lower = jnp.pad(held[:, 1], ((0, 0), (0, 0), (width, 0)))
    diag = jnp.concatenate([upper, lower], axis=1)
    lanes = 2 * width
    return pl.pallas_call(
        finish_kernel,
        grid=(G // 2,),
        in_specs=[
            pl.BlockSpec((block_rows, pairs * lanes), lambda g: (0, g)),
            pl.BlockSpec((1, block_rows, 2 * pairs), lambda g: (g, 0, 0)),
            pl.BlockSpec((2, block_rows, 2 * N), lambda g: (g, 0, 0)),
            pl.BlockSpec((pairs, 2 * N, lanes), lambda g: (g, 0, 0)),
        ],
        out_specs=pl.BlockSpec((block_rows, pairs * lanes), lambda g: (0, g)),
        out_shape=jax.ShapeDtypeStruct((block_rows, num_heads * width), jnp.bfloat16),
    )(early, factor, reads2, diag)


def exclusive_reverse_prod(values):
    inclusive = jnp.flip(jnp.cumprod(jnp.flip(values, 0), axis=0), 0)
    return jnp.concatenate([inclusive[1:], jnp.ones_like(values[:1])], axis=0)


def with_tail(rows, tail):
    pad = TAIL - tail.shape[1]
    tail = jnp.concatenate([tail, jnp.zeros((tail.shape[0], pad), jnp.float32)], axis=1)
    return jnp.concatenate([rows, tail], axis=1)


def local(
    mixer_input, write_vectors, read_vectors, step_sizes, decay_rate, skip_gain, document_ids
):
    num_heads = step_sizes.shape[1]
    axes = ("grp", "seq")
    n_blk = lax.axis_size(axes)
    me = lax.axis_index(axes)
    local_part, states, decays, cumulative = local_terms(
        mixer_input, write_vectors, read_vectors, step_sizes, decay_rate, document_ids
    )
    state_width = states.shape[1]
    docs_f = document_ids.astype(jnp.float32)
    first_id = docs_f[0]
    last_id = docs_f[-1]

    flat = states.reshape(n_blk, -1)
    row_len = flat.shape[1]
    row_heads = max(1, num_heads // n_blk)
    sub_len = row_len // row_heads
    if n_blk <= num_heads:
        sent_decays = decays.reshape(n_blk, row_heads)
    else:
        sent_decays = jnp.repeat(decays, n_blk // num_heads)[:, None]
    ids = jnp.broadcast_to(jnp.stack([first_id, last_id])[None, :], (n_blk, 2))
    tails = with_tail(jnp.zeros((n_blk, 0), jnp.float32), jnp.concatenate([sent_decays, ids], axis=1))
    got = lax.all_to_all(tails, axes, 0, 0, tiled=False)

    head_rows = 8 if sub_len % (8 * 128) == 0 else 1
    pieces = flat.reshape(n_blk, row_heads * head_rows, sub_len // head_rows)
    got, pieces = lax.optimization_barrier((got, pieces))
    owned = lax.all_to_all(pieces, axes, 0, 0, tiled=False)
    blk_decay = got[:, :row_heads]
    blk_first = got[:, row_heads]
    blk_last = got[:, row_heads + 1]
    last_in = jnp.where(me > 0, jnp.take(blk_last, jnp.maximum(me - 1, 0)), -1.0)
    early = early_terms(local_part, mixer_input, skip_gain)
    factor, reads2 = finish_inputs(cumulative, last_in, read_vectors, document_ids)

    src = jnp.arange(n_blk)
    prev_last = jnp.concatenate([jnp.full((1,), -1.0, jnp.float32), blk_last[:-1]])
    link = jnp.logical_and(src > 0, blk_first == prev_last).astype(jnp.float32)
    factors = blk_decay * link[:, None]
    before = (src[:, None] < src[None, :])[:, :, None]
    gated = jnp.where(before, factors[:, None, :], 1.0)
    coef = jnp.where(before, exclusive_reverse_prod(gated), 0.0)
    result = jnp.concatenate(
        [
            jnp.einsum(
                "ts,trl->srl",
                coef[:, :, j],
                owned[:, j * head_rows:(j + 1) * head_rows],
                precision=lax.Precision.HIGHEST,
            )
            for j in range(row_heads)
        ],
        axis=1,
    )

    back = lax.all_to_all(result, axes, 0, 0, tiled=False)
    states_in = back.reshape(num_heads, state_width)
    return finish(early, factor, reads2, states_in)


def solution(mesh):
    in_specs = (
        P(("grp", "seq"), None),
        P(("grp", "seq"), None),
        P(("grp", "seq"), None),
        P(("grp", "seq"), None),
        P(),
        P(),
        P(("grp", "seq")),
    )
    out_specs = P(("grp", "seq"), None)
    return jax.shard_map(local, mesh=mesh, in_specs=in_specs, out_specs=out_specs, check_vma=False)
```

```python
import numpy as np
import jax
import jax.numpy as jnp
from jax import lax
from jax.sharding import PartitionSpec as P
from jax.experimental import pallas as pl

N = 64
G = 4
TAIL = 128


def local_terms(block_input, write_block, read_block, step_block, rates, doc_block):
    block_rows = block_input.shape[0]
    num_heads = step_block.shape[1]
    per_group = num_heads // G
    width = block_input.shape[1] // num_heads
    grouped = block_input.reshape(block_rows, G, per_group, width)
    writes = write_block.reshape(block_rows, G, N)
    reads = read_block.reshape(block_rows, G, N)
    cumulative = jnp.cumsum(-step_block * rates[None, :], axis=0)
    cum_heads = cumulative.T.reshape(G, per_group, block_rows)
    step_heads = step_block.T.reshape(G, per_group, block_rows)
    positions = jnp.arange(block_rows)
    visible = jnp.logical_and(
        doc_block[:, None] == doc_block[None, :], positions[:, None] >= positions[None, :]
    )
    gaps = jnp.where(
        visible[None, None], cum_heads[:, :, :, None] - cum_heads[:, :, None, :], -jnp.inf
    )
    inner_prod = jnp.einsum("ign,jgn->gij", reads, writes, preferred_element_type=jnp.float32)
    weights = (inner_prod[:, None] * jnp.exp(gaps) * step_heads[:, :, None, :]).astype(jnp.bfloat16)
    local_part = jnp.einsum("ghij,jghp->ighp", weights, grouped, preferred_element_type=jnp.float32)
    same_last = (doc_block == doc_block[-1]).astype(jnp.float32)
    tail_weight = jnp.exp(cumulative[-1][None, :] - cumulative) * step_block * same_last[:, None]
    scaled = (
        writes[:, :, None, :].astype(jnp.float32)
        * tail_weight.reshape(block_rows, G, per_group)[:, :, :, None]
    ).astype(jnp.bfloat16)
    states = jnp.einsum(
        "jghn,jghp->ghnp", scaled, grouped, preferred_element_type=jnp.float32
    ).reshape(num_heads, N * width)
    decays = jnp.exp(cumulative[-1]) * (doc_block[0] == doc_block[-1]).astype(jnp.float32)
    return local_part, states, decays, cumulative


def early_terms(local_part, block_input, gains):
    block_rows = block_input.shape[0]
    num_heads = gains.shape[0]
    per_group = num_heads // G
    width = block_input.shape[1] // num_heads
    direct = gains.reshape(G, per_group)[None, :, :, None] * block_input.reshape(
        block_rows, G, per_group, width
    ).astype(jnp.float32)
    return (local_part + direct).reshape(block_rows, num_heads * width)


def split_bf16(value):
    high = value.astype(jnp.bfloat16)
    low = (value - high.astype(jnp.float32)).astype(jnp.bfloat16)
    return high, low


def finish_kernel(early_ref, factor_ref, reads_ref, pairs_ref, out_ref):
    pairs = pairs_ref.shape[0]
    lanes = pairs_ref.shape[2]
    rows = reads_ref.shape[1]
    per_read = pairs // reads_ref.shape[0]
    lane = lax.broadcasted_iota(jnp.int32, (rows, lanes), 1)
    for k in range(pairs):
        if k % per_read == 0:
            read_hi, read_lo = split_bf16(reads_ref[k // per_read])
        st_hi, st_lo = split_bf16(pairs_ref[k])
        reached = jnp.dot(read_hi, st_hi, preferred_element_type=jnp.float32)
        reached += jnp.dot(read_hi, st_lo, preferred_element_type=jnp.float32)
        reached += jnp.dot(read_lo, st_hi, preferred_element_type=jnp.float32)
        spread = jnp.where(
            lane < lanes // 2, factor_ref[0, :, 2 * k:2 * k + 1], factor_ref[0, :, 2 * k + 1:2 * k + 2]
        )
        cols = slice(k * lanes, (k + 1) * lanes)
        out_ref[:, cols] = (early_ref[:, cols] + reached * spread).astype(out_ref.dtype)


def finish_inputs(cumulative, last_in, read_block, doc_block):
    block_rows = read_block.shape[0]
    num_heads = cumulative.shape[1]
    per_group = num_heads // G
    carried_in = (doc_block.astype(jnp.float32) == last_in).astype(jnp.float32)
    factor = jnp.exp(cumulative) * carried_in[:, None]
    factor = factor.reshape(block_rows, 1, G * per_group).transpose(1, 0, 2)
    reads = read_block.reshape(block_rows, G, 1, N).astype(jnp.float32)
    reads2 = jnp.broadcast_to(reads, (block_rows, G, 2, N)).transpose(1, 0, 2, 3)
    return factor, reads2.reshape(G, block_rows, 2 * N)


def finish(early, factor, reads2, states_in):
    block_rows = early.shape[0]
    num_heads = states_in.shape[0]
    width = early.shape[1] // num_heads
    pairs = num_heads // 2
    held = states_in.reshape(num_heads // 2, 2, N, width)
    upper = jnp.pad(held[:, 0], ((0, 0), (0, 0), (0, width)))
    lower = jnp.pad(held[:, 1], ((0, 0), (0, 0), (width, 0)))
    diag = jnp.concatenate([upper, lower], axis=1)
    lanes = 2 * width
    return pl.pallas_call(
        finish_kernel,
        grid=(1,),
        in_specs=[
            pl.BlockSpec((block_rows, pairs * lanes), lambda g: (0, g)),
            pl.BlockSpec((1, block_rows, 2 * pairs), lambda g: (g, 0, 0)),
            pl.BlockSpec((G, block_rows, 2 * N), lambda g: (g, 0, 0)),
            pl.BlockSpec((pairs, 2 * N, lanes), lambda g: (g, 0, 0)),
        ],
        out_specs=pl.BlockSpec((block_rows, pairs * lanes), lambda g: (0, g)),
        out_shape=jax.ShapeDtypeStruct((block_rows, num_heads * width), jnp.bfloat16),
    )(early, factor, reads2, diag)


def exclusive_reverse_prod(values):
    inclusive = jnp.flip(jnp.cumprod(jnp.flip(values, 0), axis=0), 0)
    return jnp.concatenate([inclusive[1:], jnp.ones_like(values[:1])], axis=0)


def with_tail(rows, tail):
    pad = TAIL - tail.shape[1]
    tail = jnp.concatenate([tail, jnp.zeros((tail.shape[0], pad), jnp.float32)], axis=1)
    return jnp.concatenate([rows, tail], axis=1)


def local(
    mixer_input, write_vectors, read_vectors, step_sizes, decay_rate, skip_gain, document_ids
):
    num_heads = step_sizes.shape[1]
    axes = ("grp", "seq")
    n_blk = lax.axis_size(axes)
    me = lax.axis_index(axes)
    local_part, states, decays, cumulative = local_terms(
        mixer_input, write_vectors, read_vectors, step_sizes, decay_rate, document_ids
    )
    state_width = states.shape[1]
    docs_f = document_ids.astype(jnp.float32)
    first_id = docs_f[0]
    last_id = docs_f[-1]

    flat = states.reshape(n_blk, -1)
    row_len = flat.shape[1]
    row_heads = max(1, num_heads // n_blk)
    sub_len = row_len // row_heads
    if n_blk <= num_heads:
        sent_decays = decays.reshape(n_blk, row_heads)
    else:
        sent_decays = jnp.repeat(decays, n_blk // num_heads)[:, None]
    ids = jnp.broadcast_to(jnp.stack([first_id, last_id])[None, :], (n_blk, 2))
    tails = with_tail(jnp.zeros((n_blk, 0), jnp.float32), jnp.concatenate([sent_decays, ids], axis=1))
    got = lax.all_to_all(tails, axes, 0, 0, tiled=False)

    head_rows = 8 if sub_len % (8 * 128) == 0 else 1
    pieces = flat.reshape(n_blk, row_heads * head_rows, sub_len // head_rows)
    got, pieces = lax.optimization_barrier((got, pieces))
    owned = lax.all_to_all(pieces, axes, 0, 0, tiled=False)
    blk_decay = got[:, :row_heads]
    blk_first = got[:, row_heads]
    blk_last = got[:, row_heads + 1]
    last_in = jnp.where(me > 0, jnp.take(blk_last, jnp.maximum(me - 1, 0)), -1.0)
    early = early_terms(local_part, mixer_input, skip_gain)
    factor, reads2 = finish_inputs(cumulative, last_in, read_vectors, document_ids)

    src = jnp.arange(n_blk)
    prev_last = jnp.concatenate([jnp.full((1,), -1.0, jnp.float32), blk_last[:-1]])
    link = jnp.logical_and(src > 0, blk_first == prev_last).astype(jnp.float32)
    factors = blk_decay * link[:, None]
    before = (src[:, None] < src[None, :])[:, :, None]
    gated = jnp.where(before, factors[:, None, :], 1.0)
    coef = jnp.where(before, exclusive_reverse_prod(gated), 0.0)
    result = jnp.concatenate(
        [
            jnp.einsum(
                "ts,trl->srl",
                coef[:, :, j],
                owned[:, j * head_rows:(j + 1) * head_rows],
                precision=lax.Precision.HIGHEST,
            )
            for j in range(row_heads)
        ],
        axis=1,
    )

    back = lax.all_to_all(result, axes, 0, 0, tiled=False)
    states_in = back.reshape(num_heads, state_width)
    return finish(early, factor, reads2, states_in)


def solution(mesh):
    in_specs = (
        P(("grp", "seq"), None),
        P(("grp", "seq"), None),
        P(("grp", "seq"), None),
        P(("grp", "seq"), None),
        P(),
        P(),
        P(("grp", "seq")),
    )
    out_specs = P(("grp", "seq"), None)
    return jax.shard_map(local, mesh=mesh, in_specs=in_specs, out_specs=out_specs, check_vma=False)
```

```python
import numpy as np
import jax
import jax.numpy as jnp
from jax import lax
from jax.sharding import PartitionSpec as P
from jax.experimental import pallas as pl

N = 64
G = 4
TAIL = 128


def local_terms(block_input, write_block, read_block, step_block, rates, doc_block):
    block_rows = block_input.shape[0]
    num_heads = step_block.shape[1]
    per_group = num_heads // G
    width = block_input.shape[1] // num_heads
    grouped = block_input.reshape(block_rows, G, per_group, width)
    writes = write_block.reshape(block_rows, G, N)
    reads = read_block.reshape(block_rows, G, N)
    cumulative = jnp.cumsum(-step_block * rates[None, :], axis=0)
    cum_heads = cumulative.T.reshape(G, per_group, block_rows)
    step_heads = step_block.T.reshape(G, per_group, block_rows)
    positions = jnp.arange(block_rows)
    visible = jnp.logical_and(
        doc_block[:, None] == doc_block[None, :], positions[:, None] >= positions[None, :]
    )
    gaps = jnp.where(
        visible[None, None], cum_heads[:, :, :, None] - cum_heads[:, :, None, :], -jnp.inf
    )
    inner_prod = jnp.einsum("ign,jgn->gij", reads, writes, preferred_element_type=jnp.float32)
    weights = (inner_prod[:, None] * jnp.exp(gaps) * step_heads[:, :, None, :]).astype(jnp.bfloat16)
    local_part = jnp.einsum("ghij,jghp->ighp", weights, grouped, preferred_element_type=jnp.float32)
    same_last = (doc_block == doc_block[-1]).astype(jnp.float32)
    tail_weight = jnp.exp(cumulative[-1][None, :] - cumulative) * step_block * same_last[:, None]
    scaled = (
        writes[:, :, None, :].astype(jnp.float32)
        * tail_weight.reshape(block_rows, G, per_group)[:, :, :, None]
    ).astype(jnp.bfloat16)
    states = jnp.einsum(
        "jghn,jghp->ghnp", scaled, grouped, preferred_element_type=jnp.float32
    ).reshape(num_heads, N * width)
    decays = jnp.exp(jnp.sum(-step_block * rates[None, :], axis=0)) * (
        doc_block[0] == doc_block[-1]
    ).astype(jnp.float32)
    return local_part, states, decays, cumulative


def early_terms(local_part, block_input, gains):
    block_rows = block_input.shape[0]
    num_heads = gains.shape[0]
    per_group = num_heads // G
    width = block_input.shape[1] // num_heads
    direct = gains.reshape(G, per_group)[None, :, :, None] * block_input.reshape(
        block_rows, G, per_group, width
    ).astype(jnp.float32)
    return (local_part + direct).reshape(block_rows, num_heads * width)


def split_bf16(value):
    high = value.astype(jnp.bfloat16)
    low = (value - high.astype(jnp.float32)).astype(jnp.bfloat16)
    return high, low


def finish_kernel(early_ref, factor_ref, reads_ref, pairs_ref, out_ref):
    pairs = pairs_ref.shape[0]
    lanes = pairs_ref.shape[2]
    rows = reads_ref.shape[1]
    per_read = pairs // reads_ref.shape[0]
    lane = lax.broadcasted_iota(jnp.int32, (rows, lanes), 1)
    for k in range(pairs):
        if k % per_read == 0:
            read_hi, read_lo = split_bf16(reads_ref[k // per_read])
        st_hi, st_lo = split_bf16(pairs_ref[k])
        reached = jnp.dot(read_hi, st_hi, preferred_element_type=jnp.float32)
        reached += jnp.dot(read_hi, st_lo, preferred_element_type=jnp.float32)
        reached += jnp.dot(read_lo, st_hi, preferred_element_type=jnp.float32)
        spread = jnp.where(
            lane < lanes // 2, factor_ref[0, :, 2 * k:2 * k + 1], factor_ref[0, :, 2 * k + 1:2 * k + 2]
        )
        cols = slice(k * lanes, (k + 1) * lanes)
        out_ref[:, cols] = (early_ref[:, cols] + reached * spread).astype(out_ref.dtype)


def finish_inputs(cumulative, last_in, read_block, doc_block):
    block_rows = read_block.shape[0]
    num_heads = cumulative.shape[1]
    per_group = num_heads // G
    carried_in = (doc_block.astype(jnp.float32) == last_in).astype(jnp.float32)
    factor = jnp.exp(cumulative) * carried_in[:, None]
    factor = factor.reshape(block_rows, G // 2, 2 * per_group).transpose(1, 0, 2)
    reads = read_block.reshape(block_rows, G, 1, N).astype(jnp.float32)
    reads2 = jnp.broadcast_to(reads, (block_rows, G, 2, N)).transpose(1, 0, 2, 3)
    return factor, reads2.reshape(G, block_rows, 2 * N)


def finish(early, factor, reads2, states_in):
    block_rows = early.shape[0]
    num_heads = states_in.shape[0]
    width = early.shape[1] // num_heads
    pairs = num_heads // G
    held = states_in.reshape(num_heads // 2, 2, N, width)
    upper = jnp.pad(held[:, 0], ((0, 0), (0, 0), (0, width)))
    lower = jnp.pad(held[:, 1], ((0, 0), (0, 0), (width, 0)))
    diag = jnp.concatenate([upper, lower], axis=1)
    lanes = 2 * width
    return pl.pallas_call(
        finish_kernel,
        grid=(G // 2,),
        in_specs=[
            pl.BlockSpec((block_rows, pairs * lanes), lambda g: (0, g)),
            pl.BlockSpec((1, block_rows, 2 * pairs), lambda g: (g, 0, 0)),
            pl.BlockSpec((2, block_rows, 2 * N), lambda g: (g, 0, 0)),
            pl.BlockSpec((pairs, 2 * N, lanes), lambda g: (g, 0, 0)),
        ],
        out_specs=pl.BlockSpec((block_rows, pairs * lanes), lambda g: (0, g)),
        out_shape=jax.ShapeDtypeStruct((block_rows, num_heads * width), jnp.bfloat16),
    )(early, factor, reads2, diag)


def exclusive_reverse_prod(values):
    inclusive = jnp.flip(jnp.cumprod(jnp.flip(values, 0), axis=0), 0)
    return jnp.concatenate([inclusive[1:], jnp.ones_like(values[:1])], axis=0)


def with_tail(rows, tail):
    pad = TAIL - tail.shape[1]
    tail = jnp.concatenate([tail, jnp.zeros((tail.shape[0], pad), jnp.float32)], axis=1)
    return jnp.concatenate([rows, tail], axis=1)


def local(
    mixer_input, write_vectors, read_vectors, step_sizes, decay_rate, skip_gain, document_ids
):
    num_heads = step_sizes.shape[1]
    axes = ("grp", "seq")
    n_blk = lax.axis_size(axes)
    me = lax.axis_index(axes)
    local_part, states, decays, cumulative = local_terms(
        mixer_input, write_vectors, read_vectors, step_sizes, decay_rate, document_ids
    )
    state_width = states.shape[1]
    docs_f = document_ids.astype(jnp.float32)
    first_id = docs_f[0]
    last_id = docs_f[-1]

    flat = states.reshape(n_blk, -1)
    row_len = flat.shape[1]
    row_heads = max(1, num_heads // n_blk)
    sub_len = row_len // row_heads
    if n_blk <= num_heads:
        sent_decays = decays.reshape(n_blk, row_heads)
    else:
        sent_decays = jnp.repeat(decays, n_blk // num_heads)[:, None]
    col = lax.broadcasted_iota(jnp.int32, (n_blk, TAIL), 1)
    tails = jnp.where(col == row_heads, first_id, jnp.where(col == row_heads + 1, last_id, 0.0))
    for j in range(row_heads):
        tails = jnp.where(col == j, sent_decays[:, j:j + 1], tails)
    got = lax.all_to_all(tails, axes, 0, 0, tiled=False)

    head_rows = 8 if sub_len % (8 * 128) == 0 else 1
    pieces = flat.reshape(n_blk, row_heads * head_rows, sub_len // head_rows)
    got, pieces = lax.optimization_barrier((got, pieces))
    owned = lax.all_to_all(pieces, axes, 0, 0, tiled=False)
    blk_decay = got[:, :row_heads]
    blk_first = got[:, row_heads]
    blk_last = got[:, row_heads + 1]
    last_in = jnp.where(me > 0, jnp.take(blk_last, jnp.maximum(me - 1, 0)), -1.0)
    early = early_terms(local_part, mixer_input, skip_gain)
    factor, reads2 = finish_inputs(cumulative, last_in, read_vectors, document_ids)

    src = jnp.arange(n_blk)
    prev_last = jnp.concatenate([jnp.full((1,), -1.0, jnp.float32), blk_last[:-1]])
    link = jnp.logical_and(src > 0, blk_first == prev_last).astype(jnp.float32)
    factors = blk_decay * link[:, None]
    before = (src[:, None] < src[None, :])[:, :, None]
    gated = jnp.where(before, factors[:, None, :], 1.0)
    coef = jnp.where(before, exclusive_reverse_prod(gated), 0.0)
    result = jnp.concatenate(
        [
            jnp.einsum(
                "ts,trl->srl",
                coef[:, :, j],
                owned[:, j * head_rows:(j + 1) * head_rows],
                precision=lax.Precision.HIGHEST,
            )
            for j in range(row_heads)
        ],
        axis=1,
    )

    back = lax.all_to_all(result, axes, 0, 0, tiled=False)
    states_in = back.reshape(num_heads, state_width)
    return finish(early, factor, reads2, states_in)


def solution(mesh):
    in_specs = (
        P(("grp", "seq"), None),
        P(("grp", "seq"), None),
        P(("grp", "seq"), None),
        P(("grp", "seq"), None),
        P(),
        P(),
        P(("grp", "seq")),
    )
    out_specs = P(("grp", "seq"), None)
    return jax.shard_map(local, mesh=mesh, in_specs=in_specs, out_specs=out_specs, check_vma=False)
```

```python
import numpy as np
import jax
import jax.numpy as jnp
from jax import lax
from jax.sharding import PartitionSpec as P
from jax.experimental import pallas as pl

N = 64
G = 4
TAIL = 128


def local_terms(block_input, write_block, read_block, step_block, rates, doc_block):
    block_rows = block_input.shape[0]
    num_heads = step_block.shape[1]
    per_group = num_heads // G
    width = block_input.shape[1] // num_heads
    grouped = block_input.reshape(block_rows, G, per_group, width)
    writes = write_block.reshape(block_rows, G, N)
    reads = read_block.reshape(block_rows, G, N)
    cumulative = jnp.cumsum(-step_block * rates[None, :], axis=0)
    cum_heads = cumulative.T.reshape(G, per_group, block_rows)
    step_heads = step_block.T.reshape(G, per_group, block_rows)
    positions = jnp.arange(block_rows)
    visible = jnp.logical_and(
        doc_block[:, None] == doc_block[None, :], positions[:, None] >= positions[None, :]
    )
    gaps = jnp.where(
        visible[None, None], cum_heads[:, :, :, None] - cum_heads[:, :, None, :], -jnp.inf
    )
    inner_prod = jnp.einsum("ign,jgn->gij", reads, writes, preferred_element_type=jnp.float32)
    weights = (inner_prod[:, None] * jnp.exp(gaps) * step_heads[:, :, None, :]).astype(jnp.bfloat16)
    local_part = jnp.einsum("ghij,jghp->ighp", weights, grouped, preferred_element_type=jnp.float32)
    same_last = (doc_block == doc_block[-1]).astype(jnp.float32)
    tail_weight = jnp.exp(cumulative[-1][None, :] - cumulative) * step_block * same_last[:, None]
    scaled = (
        writes[:, :, None, :].astype(jnp.float32)
        * tail_weight.reshape(block_rows, G, per_group)[:, :, :, None]
    ).astype(jnp.bfloat16)
    states = jnp.einsum(
        "jghn,jghp->ghnp", scaled, grouped, preferred_element_type=jnp.float32
    ).reshape(num_heads, N * width)
    decays = jnp.exp(cumulative[-1]) * (doc_block[0] == doc_block[-1]).astype(jnp.float32)
    return local_part, states, decays, cumulative


def early_terms(local_part, block_input, gains):
    block_rows = block_input.shape[0]
    num_heads = gains.shape[0]
    per_group = num_heads // G
    width = block_input.shape[1] // num_heads
    direct = gains.reshape(G, per_group)[None, :, :, None] * block_input.reshape(
        block_rows, G, per_group, width
    ).astype(jnp.float32)
    return (local_part + direct).reshape(block_rows, num_heads * width)


def split_bf16(value):
    high = value.astype(jnp.bfloat16)
    low = (value - high.astype(jnp.float32)).astype(jnp.bfloat16)
    return high, low


def finish_kernel(early_ref, factor_ref, reads_ref, pairs_ref, out_ref):
    pairs = pairs_ref.shape[0]
    lanes = pairs_ref.shape[2]
    rows = reads_ref.shape[1]
    per_read = pairs // reads_ref.shape[0]
    lane = lax.broadcasted_iota(jnp.int32, (rows, lanes), 1)
    for k in range(pairs):
        if k % per_read == 0:
            read_hi, read_lo = split_bf16(reads_ref[k // per_read])
        st_hi, st_lo = split_bf16(pairs_ref[k])
        reached = jnp.dot(read_hi, st_hi, preferred_element_type=jnp.float32)
        reached += jnp.dot(read_hi, st_lo, preferred_element_type=jnp.float32)
        reached += jnp.dot(read_lo, st_hi, preferred_element_type=jnp.float32)
        spread = jnp.where(
            lane < lanes // 2, factor_ref[0, :, 2 * k:2 * k + 1], factor_ref[0, :, 2 * k + 1:2 * k + 2]
        )
        cols = slice(k * lanes, (k + 1) * lanes)
        out_ref[:, cols] = (early_ref[:, cols] + reached * spread).astype(out_ref.dtype)


def finish_inputs(cumulative, last_in, read_block, doc_block):
    block_rows = read_block.shape[0]
    num_heads = cumulative.shape[1]
    per_group = num_heads // G
    carried_in = (doc_block.astype(jnp.float32) == last_in).astype(jnp.float32)
    factor = jnp.exp(cumulative) * carried_in[:, None]
    factor = factor.reshape(block_rows, G // 2, 2 * per_group).transpose(1, 0, 2)
    reads = read_block.reshape(block_rows, G, 1, N).astype(jnp.float32)
    reads2 = jnp.broadcast_to(reads, (block_rows, G, 2, N)).transpose(1, 0, 2, 3)
    return factor, reads2.reshape(G, block_rows, 2 * N)


def finish(early, factor, reads2, states_in):
    block_rows = early.shape[0]
    num_heads = states_in.shape[0]
    width = early.shape[1] // num_heads
    pairs = num_heads // G
    held = states_in.reshape(num_heads // 2, 2, N, width)
    upper = jnp.pad(held[:, 0], ((0, 0), (0, 0), (0, width)))
    lower = jnp.pad(held[:, 1], ((0, 0), (0, 0), (width, 0)))
    diag = jnp.concatenate([upper, lower], axis=1)
    lanes = 2 * width
    return pl.pallas_call(
        finish_kernel,
        grid=(G // 2,),
        in_specs=[
            pl.BlockSpec((block_rows, pairs * lanes), lambda g: (0, g)),
            pl.BlockSpec((1, block_rows, 2 * pairs), lambda g: (g, 0, 0)),
            pl.BlockSpec((2, block_rows, 2 * N), lambda g: (g, 0, 0)),
            pl.BlockSpec((pairs, 2 * N, lanes), lambda g: (g, 0, 0)),
        ],
        out_specs=pl.BlockSpec((block_rows, pairs * lanes), lambda g: (0, g)),
        out_shape=jax.ShapeDtypeStruct((block_rows, num_heads * width), jnp.bfloat16),
    )(early, factor, reads2, diag)


def exclusive_reverse_prod(values):
    inclusive = jnp.flip(jnp.cumprod(jnp.flip(values, 0), axis=0), 0)
    return jnp.concatenate([inclusive[1:], jnp.ones_like(values[:1])], axis=0)


def with_tail(rows, tail):
    pad = TAIL - tail.shape[1]
    tail = jnp.concatenate([tail, jnp.zeros((tail.shape[0], pad), jnp.float32)], axis=1)
    return jnp.concatenate([rows, tail], axis=1)


def local(
    mixer_input, write_vectors, read_vectors, step_sizes, decay_rate, skip_gain, document_ids
):
    num_heads = step_sizes.shape[1]
    axes = ("grp", "seq")
    n_blk = lax.axis_size(axes)
    me = lax.axis_index(axes)
    local_part, states, decays, cumulative = local_terms(
        mixer_input, write_vectors, read_vectors, step_sizes, decay_rate, document_ids
    )
    state_width = states.shape[1]
    docs_f = document_ids.astype(jnp.float32)
    first_id = docs_f[0]
    last_id = docs_f[-1]

    flat = states.reshape(n_blk, -1)
    row_len = flat.shape[1]
    row_heads = max(1, num_heads // n_blk)
    sub_len = row_len // row_heads
    if n_blk <= num_heads:
        sent_decays = decays.reshape(n_blk, row_heads)
    else:
        sent_decays = jnp.repeat(decays, n_blk // num_heads)[:, None]
    ids = jnp.broadcast_to(jnp.stack([first_id, last_id])[None, :], (n_blk, 2))
    tails = with_tail(jnp.zeros((n_blk, 0), jnp.float32), jnp.concatenate([sent_decays, ids], axis=1))
    got = lax.all_to_all(tails, axes, 0, 0, tiled=False)

    head_rows = 8 if sub_len % (8 * 128) == 0 else 1
    pieces = flat.reshape(n_blk, row_heads * head_rows, sub_len // head_rows)
    got, pieces = lax.optimization_barrier((got, pieces))
    owned = lax.all_to_all(pieces, axes, 0, 0, tiled=False)
    blk_decay = got[:, :row_heads]
    blk_first = got[:, row_heads]
    blk_last = got[:, row_heads + 1]
    last_in = jnp.where(me > 0, jnp.take(blk_last, jnp.maximum(me - 1, 0)), -1.0)
    early = early_terms(local_part, mixer_input, skip_gain)
    factor, reads2 = finish_inputs(cumulative, last_in, read_vectors, document_ids)

    src = jnp.arange(n_blk)
    prev_last = jnp.concatenate([jnp.full((1,), -1.0, jnp.float32), blk_last[:-1]])
    link = jnp.logical_and(src > 0, blk_first == prev_last).astype(jnp.float32)
    factors = blk_decay * link[:, None]
    before = (src[:, None] < src[None, :])[:, :, None]
    gated = jnp.where(before, factors[:, None, :], 1.0)
    coef = jnp.where(before, exclusive_reverse_prod(gated), 0.0)
    stacked = owned.reshape(n_blk, row_heads, head_rows, -1)
    result = jnp.einsum("tsh,thrl->shrl", coef, stacked, precision=lax.Precision.HIGHEST)
    result = result.reshape(owned.shape)

    back = lax.all_to_all(result, axes, 0, 0, tiled=False)
    states_in = back.reshape(num_heads, state_width)
    return finish(early, factor, reads2, states_in)


def solution(mesh):
    in_specs = (
        P(("grp", "seq"), None),
        P(("grp", "seq"), None),
        P(("grp", "seq"), None),
        P(("grp", "seq"), None),
        P(),
        P(),
        P(("grp", "seq")),
    )
    out_specs = P(("grp", "seq"), None)
    return jax.shard_map(local, mesh=mesh, in_specs=in_specs, out_specs=out_specs, check_vma=False)
```

```python
import numpy as np
import jax
import jax.numpy as jnp
from jax import lax
from jax.sharding import PartitionSpec as P
from jax.experimental import pallas as pl

N = 64
G = 4
TAIL = 128


def local_terms(block_input, write_block, read_block, step_block, rates, doc_block):
    block_rows = block_input.shape[0]
    num_heads = step_block.shape[1]
    per_group = num_heads // G
    width = block_input.shape[1] // num_heads
    grouped = block_input.reshape(block_rows, G, per_group, width)
    writes = write_block.reshape(block_rows, G, N)
    reads = read_block.reshape(block_rows, G, N)
    cumulative = jnp.cumsum(-step_block * rates[None, :], axis=0)
    cum_heads = cumulative.T.reshape(G, per_group, block_rows)
    step_heads = step_block.T.reshape(G, per_group, block_rows)
    positions = jnp.arange(block_rows)
    visible = jnp.logical_and(
        doc_block[:, None] == doc_block[None, :], positions[:, None] >= positions[None, :]
    )
    gaps = jnp.where(
        visible[None, None], cum_heads[:, :, :, None] - cum_heads[:, :, None, :], -jnp.inf
    )
    inner_prod = jnp.einsum("ign,jgn->gij", reads, writes, preferred_element_type=jnp.float32)
    weights = (inner_prod[:, None] * jnp.exp(gaps) * step_heads[:, :, None, :]).astype(jnp.bfloat16)
    local_part = jnp.einsum("ghij,jghp->ighp", weights, grouped, preferred_element_type=jnp.float32)
    same_last = (doc_block == doc_block[-1]).astype(jnp.float32)
    tail_weight = jnp.exp(cumulative[-1][None, :] - cumulative) * step_block * same_last[:, None]
    scaled = (
        writes[:, :, None, :].astype(jnp.float32)
        * tail_weight.reshape(block_rows, G, per_group)[:, :, :, None]
    ).astype(jnp.bfloat16)
    states = jnp.einsum(
        "jghn,jghp->ghnp", scaled, grouped, preferred_element_type=jnp.float32
    ).reshape(num_heads, N * width)
    decays = jnp.exp(cumulative[-1]) * (doc_block[0] == doc_block[-1]).astype(jnp.float32)
    return local_part, states, decays, cumulative


def early_terms(local_part, block_input, gains):
    block_rows = block_input.shape[0]
    num_heads = gains.shape[0]
    per_group = num_heads // G
    width = block_input.shape[1] // num_heads
    direct = gains.reshape(G, per_group)[None, :, :, None] * block_input.reshape(
        block_rows, G, per_group, width
    ).astype(jnp.float32)
    return (local_part + direct).reshape(block_rows, num_heads * width)


def split_bf16(value):
    high = value.astype(jnp.bfloat16)
    low = (value - high.astype(jnp.float32)).astype(jnp.bfloat16)
    return high, low


def finish_kernel(early_ref, factor_ref, reads_ref, held_ref, out_ref):
    pairs = held_ref.shape[0]
    depth = held_ref.shape[2]
    width = held_ref.shape[3]
    lanes = 2 * width
    rows = reads_ref.shape[1]
    per_read = pairs // reads_ref.shape[0]
    lane = lax.broadcasted_iota(jnp.int32, (rows, lanes), 1)
    sel_row = lax.broadcasted_iota(jnp.int32, (width, lanes), 0)
    sel_lane = lax.broadcasted_iota(jnp.int32, (width, lanes), 1)
    place = [(sel_lane == sel_row + h * width).astype(jnp.bfloat16) for h in range(2)]
    for k in range(pairs):
        if k % per_read == 0:
            read_hi, read_lo = split_bf16(reads_ref[k // per_read])
        parts_hi, parts_lo = [], []
        for h in range(2):
            part_hi, part_lo = split_bf16(held_ref[k, h])
            parts_hi.append(jnp.dot(part_hi, place[h], preferred_element_type=jnp.float32))
            parts_lo.append(jnp.dot(part_lo, place[h], preferred_element_type=jnp.float32))
        st_hi = jnp.concatenate(parts_hi, axis=0).astype(jnp.bfloat16)
        st_lo = jnp.concatenate(parts_lo, axis=0).astype(jnp.bfloat16)
        reached = jnp.dot(read_hi, st_hi, preferred_element_type=jnp.float32)
        reached += jnp.dot(read_hi, st_lo, preferred_element_type=jnp.float32)
        reached += jnp.dot(read_lo, st_hi, preferred_element_type=jnp.float32)
        spread = jnp.where(
            lane < lanes // 2, factor_ref[0, :, 2 * k:2 * k + 1], factor_ref[0, :, 2 * k + 1:2 * k + 2]
        )
        cols = slice(k * lanes, (k + 1) * lanes)
        out_ref[:, cols] = (early_ref[:, cols] + reached * spread).astype(out_ref.dtype)


def finish_inputs(cumulative, last_in, read_block, doc_block):
    block_rows = read_block.shape[0]
    num_heads = cumulative.shape[1]
    per_group = num_heads // G
    carried_in = (doc_block.astype(jnp.float32) == last_in).astype(jnp.float32)
    factor = jnp.exp(cumulative) * carried_in[:, None]
    factor = factor.reshape(block_rows, G // 2, 2 * per_group).transpose(1, 0, 2)
    reads = read_block.reshape(block_rows, G, 1, N).astype(jnp.float32)
    reads2 = jnp.broadcast_to(reads, (block_rows, G, 2, N)).transpose(1, 0, 2, 3)
    return factor, reads2.reshape(G, block_rows, 2 * N)


def finish(early, factor, reads2, states_in):
    block_rows = early.shape[0]
    num_heads = states_in.shape[0]
    width = early.shape[1] // num_heads
    pairs = num_heads // G
    held = states_in.reshape(num_heads // 2, 2, N, width)
    lanes = 2 * width
    return pl.pallas_call(
        finish_kernel,
        grid=(G // 2,),
        in_specs=[
            pl.BlockSpec((block_rows, pairs * lanes), lambda g: (0, g)),
            pl.BlockSpec((1, block_rows, 2 * pairs), lambda g: (g, 0, 0)),
            pl.BlockSpec((2, block_rows, 2 * N), lambda g: (g, 0, 0)),
            pl.BlockSpec((pairs, 2, N, width), lambda g: (g, 0, 0, 0)),
        ],
        out_specs=pl.BlockSpec((block_rows, pairs * lanes), lambda g: (0, g)),
        out_shape=jax.ShapeDtypeStruct((block_rows, num_heads * width), jnp.bfloat16),
    )(early, factor, reads2, held)


def exclusive_reverse_prod(values):
    inclusive = jnp.flip(jnp.cumprod(jnp.flip(values, 0), axis=0), 0)
    return jnp.concatenate([inclusive[1:], jnp.ones_like(values[:1])], axis=0)


def with_tail(rows, tail):
    pad = TAIL - tail.shape[1]
    tail = jnp.concatenate([tail, jnp.zeros((tail.shape[0], pad), jnp.float32)], axis=1)
    return jnp.concatenate([rows, tail], axis=1)


def local(
    mixer_input, write_vectors, read_vectors, step_sizes, decay_rate, skip_gain, document_ids
):
    num_heads = step_sizes.shape[1]
    axes = ("grp", "seq")
    n_blk = lax.axis_size(axes)
    me = lax.axis_index(axes)
    local_part, states, decays, cumulative = local_terms(
        mixer_input, write_vectors, read_vectors, step_sizes, decay_rate, document_ids
    )
    state_width = states.shape[1]
    docs_f = document_ids.astype(jnp.float32)
    first_id = docs_f[0]
    last_id = docs_f[-1]

    flat = states.reshape(n_blk, -1)
    row_len = flat.shape[1]
    row_heads = max(1, num_heads // n_blk)
    sub_len = row_len // row_heads
    if n_blk <= num_heads:
        sent_decays = decays.reshape(n_blk, row_heads)
    else:
        sent_decays = jnp.repeat(decays, n_blk // num_heads)[:, None]
    ids = jnp.broadcast_to(jnp.stack([first_id, last_id])[None, :], (n_blk, 2))
    tails = with_tail(jnp.zeros((n_blk, 0), jnp.float32), jnp.concatenate([sent_decays, ids], axis=1))
    got = lax.all_to_all(tails, axes, 0, 0, tiled=False)

    head_rows = 8 if sub_len % (8 * 128) == 0 else 1
    pieces = flat.reshape(n_blk, row_heads * head_rows, sub_len // head_rows)
    got, pieces = lax.optimization_barrier((got, pieces))
    owned = lax.all_to_all(pieces, axes, 0, 0, tiled=False)
    blk_decay = got[:, :row_heads]
    blk_first = got[:, row_heads]
    blk_last = got[:, row_heads + 1]
    last_in = jnp.where(me > 0, jnp.take(blk_last, jnp.maximum(me - 1, 0)), -1.0)
    early = early_terms(local_part, mixer_input, skip_gain)
    factor, reads2 = finish_inputs(cumulative, last_in, read_vectors, document_ids)

    src = jnp.arange(n_blk)
    prev_last = jnp.concatenate([jnp.full((1,), -1.0, jnp.float32), blk_last[:-1]])
    link = jnp.logical_and(src > 0, blk_first == prev_last).astype(jnp.float32)
    factors = blk_decay * link[:, None]
    before = (src[:, None] < src[None, :])[:, :, None]
    gated = jnp.where(before, factors[:, None, :], 1.0)
    coef = jnp.where(before, exclusive_reverse_prod(gated), 0.0)
    stacked = owned.reshape(n_blk, row_heads, head_rows, -1)
    result = jnp.einsum("tsh,thrl->shrl", coef, stacked, precision=lax.Precision.HIGHEST)
    result = result.reshape(owned.shape)

    back = lax.all_to_all(result, axes, 0, 0, tiled=False)
    states_in = back.reshape(num_heads, state_width)
    return finish(early, factor, reads2, states_in)


def solution(mesh):
    in_specs = (
        P(("grp", "seq"), None),
        P(("grp", "seq"), None),
        P(("grp", "seq"), None),
        P(("grp", "seq"), None),
        P(),
        P(),
        P(("grp", "seq")),
    )
    out_specs = P(("grp", "seq"), None)
    return jax.shard_map(local, mesh=mesh, in_specs=in_specs, out_specs=out_specs, check_vma=False)
```

```python
import numpy as np
import jax
import jax.numpy as jnp
from jax import lax
from jax.sharding import PartitionSpec as P
from jax.experimental import pallas as pl

N = 64
G = 4
TAIL = 128


def local_terms(block_input, write_block, read_block, step_block, rates, doc_block):
    block_rows = block_input.shape[0]
    num_heads = step_block.shape[1]
    per_group = num_heads // G
    width = block_input.shape[1] // num_heads
    grouped = block_input.reshape(block_rows, G, per_group, width)
    writes = write_block.reshape(block_rows, G, N)
    reads = read_block.reshape(block_rows, G, N)
    cumulative = jnp.cumsum(-step_block * rates[None, :], axis=0)
    cum_heads = cumulative.T.reshape(G, per_group, block_rows)
    step_heads = step_block.T.reshape(G, per_group, block_rows)
    positions = jnp.arange(block_rows)
    visible = jnp.logical_and(
        doc_block[:, None] == doc_block[None, :], positions[:, None] >= positions[None, :]
    )
    gaps = jnp.where(
        visible[None, None], cum_heads[:, :, :, None] - cum_heads[:, :, None, :], -jnp.inf
    )
    inner_prod = jnp.einsum("ign,jgn->gij", reads, writes, preferred_element_type=jnp.float32)
    weights = (inner_prod[:, None] * jnp.exp(gaps) * step_heads[:, :, None, :]).astype(jnp.bfloat16)
    local_part = jnp.einsum("ghij,jghp->ighp", weights, grouped, preferred_element_type=jnp.float32)
    same_last = (doc_block == doc_block[-1]).astype(jnp.float32)
    tail_weight = jnp.exp(cumulative[-1][None, :] - cumulative) * step_block * same_last[:, None]
    scaled = (
        writes[:, :, None, :].astype(jnp.float32)
        * tail_weight.reshape(block_rows, G, per_group)[:, :, :, None]
    ).astype(jnp.bfloat16)
    states = jnp.einsum(
        "jghn,jghp->ghnp", scaled, grouped, preferred_element_type=jnp.float32
    ).reshape(num_heads, N * width)
    decays = jnp.exp(cumulative[-1]) * (doc_block[0] == doc_block[-1]).astype(jnp.float32)
    return local_part, states, decays, cumulative


def early_terms(local_part, block_input, gains):
    block_rows = block_input.shape[0]
    num_heads = gains.shape[0]
    per_group = num_heads // G
    width = block_input.shape[1] // num_heads
    direct = gains.reshape(G, per_group)[None, :, :, None] * block_input.reshape(
        block_rows, G, per_group, width
    ).astype(jnp.float32)
    return (local_part + direct).reshape(block_rows, num_heads * width)


def split_bf16(value):
    high = value.astype(jnp.bfloat16)
    low = (value - high.astype(jnp.float32)).astype(jnp.bfloat16)
    return high, low


def finish_kernel(early_ref, factor_ref, reads_ref, pairs_ref, out_ref):
    pairs = pairs_ref.shape[0]
    lanes = pairs_ref.shape[2]
    rows = reads_ref.shape[1]
    per_read = pairs // reads_ref.shape[0]
    lane = lax.broadcasted_iota(jnp.int32, (rows, lanes), 1)
    for k in range(pairs):
        if k % per_read == 0:
            read = reads_ref[k // per_read]
        st_hi, st_lo = split_bf16(pairs_ref[k])
        reached = jnp.dot(read, st_hi, preferred_element_type=jnp.float32)
        reached += jnp.dot(read, st_lo, preferred_element_type=jnp.float32)
        spread = jnp.where(
            lane < lanes // 2, factor_ref[0, :, 2 * k:2 * k + 1], factor_ref[0, :, 2 * k + 1:2 * k + 2]
        )
        cols = slice(k * lanes, (k + 1) * lanes)
        out_ref[:, cols] = (early_ref[:, cols] + reached * spread).astype(out_ref.dtype)


def finish_inputs(cumulative, last_in, read_block, doc_block):
    block_rows = read_block.shape[0]
    num_heads = cumulative.shape[1]
    per_group = num_heads // G
    carried_in = (doc_block.astype(jnp.float32) == last_in).astype(jnp.float32)
    factor = jnp.exp(cumulative) * carried_in[:, None]
    factor = factor.reshape(block_rows, G // 2, 2 * per_group).transpose(1, 0, 2)
    reads = read_block.reshape(block_rows, G, 1, N)
    reads2 = jnp.broadcast_to(reads, (block_rows, G, 2, N)).transpose(1, 0, 2, 3)
    return factor, reads2.reshape(G, block_rows, 2 * N)


def finish(early, factor, reads2, states_in):
    block_rows = early.shape[0]
    num_heads = states_in.shape[0]
    width = early.shape[1] // num_heads
    pairs = num_heads // G
    held = states_in.reshape(num_heads // 2, 2, N, width)
    upper = jnp.pad(held[:, 0], ((0, 0), (0, 0), (0, width)))
    lower = jnp.pad(held[:, 1], ((0, 0), (0, 0), (width, 0)))
    diag = jnp.concatenate([upper, lower], axis=1)
    lanes = 2 * width
    return pl.pallas_call(
        finish_kernel,
        grid=(G // 2,),
        in_specs=[
            pl.BlockSpec((block_rows, pairs * lanes), lambda g: (0, g)),
            pl.BlockSpec((1, block_rows, 2 * pairs), lambda g: (g, 0, 0)),
            pl.BlockSpec((2, block_rows, 2 * N), lambda g: (g, 0, 0)),
            pl.BlockSpec((pairs, 2 * N, lanes), lambda g: (g, 0, 0)),
        ],
        out_specs=pl.BlockSpec((block_rows, pairs * lanes), lambda g: (0, g)),
        out_shape=jax.ShapeDtypeStruct((block_rows, num_heads * width), jnp.bfloat16),
    )(early, factor, reads2, diag)


def exclusive_reverse_prod(values):
    inclusive = jnp.flip(jnp.cumprod(jnp.flip(values, 0), axis=0), 0)
    return jnp.concatenate([inclusive[1:], jnp.ones_like(values[:1])], axis=0)


def with_tail(rows, tail):
    pad = TAIL - tail.shape[1]
    tail = jnp.concatenate([tail, jnp.zeros((tail.shape[0], pad), jnp.float32)], axis=1)
    return jnp.concatenate([rows, tail], axis=1)


def local(
    mixer_input, write_vectors, read_vectors, step_sizes, decay_rate, skip_gain, document_ids
):
    num_heads = step_sizes.shape[1]
    axes = ("grp", "seq")
    n_blk = lax.axis_size(axes)
    me = lax.axis_index(axes)
    local_part, states, decays, cumulative = local_terms(
        mixer_input, write_vectors, read_vectors, step_sizes, decay_rate, document_ids
    )
    state_width = states.shape[1]
    docs_f = document_ids.astype(jnp.float32)
    first_id = docs_f[0]
    last_id = docs_f[-1]

    flat = states.reshape(n_blk, -1)
    row_len = flat.shape[1]
    row_heads = max(1, num_heads // n_blk)
    sub_len = row_len // row_heads
    if n_blk <= num_heads:
        sent_decays = decays.reshape(n_blk, row_heads)
    else:
        sent_decays = jnp.repeat(decays, n_blk // num_heads)[:, None]
    ids = jnp.broadcast_to(jnp.stack([first_id, last_id])[None, :], (n_blk, 2))
    tails = with_tail(jnp.zeros((n_blk, 0), jnp.float32), jnp.concatenate([sent_decays, ids], axis=1))
    got = lax.all_to_all(tails, axes, 0, 0, tiled=False)

    head_rows = 8 if sub_len % (8 * 128) == 0 else 1
    pieces = flat.reshape(n_blk, row_heads * head_rows, sub_len // head_rows)
    got, pieces = lax.optimization_barrier((got, pieces))
    owned = lax.all_to_all(pieces, axes, 0, 0, tiled=False)
    blk_decay = got[:, :row_heads]
    blk_first = got[:, row_heads]
    blk_last = got[:, row_heads + 1]
    last_in = jnp.where(me > 0, jnp.take(blk_last, jnp.maximum(me - 1, 0)), -1.0)
    early = early_terms(local_part, mixer_input, skip_gain)
    factor, reads2 = finish_inputs(cumulative, last_in, read_vectors, document_ids)

    src = jnp.arange(n_blk)
    prev_last = jnp.concatenate([jnp.full((1,), -1.0, jnp.float32), blk_last[:-1]])
    link = jnp.logical_and(src > 0, blk_first == prev_last).astype(jnp.float32)
    factors = blk_decay * link[:, None]
    before = (src[:, None] < src[None, :])[:, :, None]
    gated = jnp.where(before, factors[:, None, :], 1.0)
    coef = jnp.where(before, exclusive_reverse_prod(gated), 0.0)
    stacked = owned.reshape(n_blk, row_heads, head_rows, -1)
    result = jnp.einsum("tsh,thrl->shrl", coef, stacked, precision=lax.Precision.HIGHEST)
    result = result.reshape(owned.shape)

    back = lax.all_to_all(result, axes, 0, 0, tiled=False)
    states_in = back.reshape(num_heads, state_width)
    return finish(early, factor, reads2, states_in)


def solution(mesh):
    in_specs = (
        P(("grp", "seq"), None),
        P(("grp", "seq"), None),
        P(("grp", "seq"), None),
        P(("grp", "seq"), None),
        P(),
        P(),
        P(("grp", "seq")),
    )
    out_specs = P(("grp", "seq"), None)
    return jax.shard_map(local, mesh=mesh, in_specs=in_specs, out_specs=out_specs, check_vma=False)
```

```python
import numpy as np
import jax
import jax.numpy as jnp
from jax import lax
from jax.sharding import PartitionSpec as P
from jax.experimental import pallas as pl

N = 64
G = 4
TAIL = 128


def local_terms(block_input, write_block, read_block, step_block, rates, doc_block):
    block_rows = block_input.shape[0]
    num_heads = step_block.shape[1]
    per_group = num_heads // G
    width = block_input.shape[1] // num_heads
    grouped = block_input.reshape(block_rows, G, per_group, width)
    writes = write_block.reshape(block_rows, G, N)
    reads = read_block.reshape(block_rows, G, N)
    cumulative = jnp.cumsum(-step_block * rates[None, :], axis=0)
    cum_heads = cumulative.T.reshape(G, per_group, block_rows)
    step_heads = step_block.T.reshape(G, per_group, block_rows)
    positions = jnp.arange(block_rows)
    visible = jnp.logical_and(
        doc_block[:, None] == doc_block[None, :], positions[:, None] >= positions[None, :]
    )
    gaps = jnp.where(
        visible[None, None], cum_heads[:, :, :, None] - cum_heads[:, :, None, :], -jnp.inf
    )
    inner_prod = jnp.einsum("ign,jgn->gij", reads, writes, preferred_element_type=jnp.float32)
    weights = (inner_prod[:, None] * jnp.exp(gaps) * step_heads[:, :, None, :]).astype(jnp.bfloat16)
    local_part = jnp.einsum("ghij,jghp->ighp", weights, grouped, preferred_element_type=jnp.float32)
    same_last = (doc_block == doc_block[-1]).astype(jnp.float32)
    tail_weight = jnp.exp(cumulative[-1][None, :] - cumulative) * step_block * same_last[:, None]
    scaled = (
        writes[:, :, None, :].astype(jnp.float32)
        * tail_weight.reshape(block_rows, G, per_group)[:, :, :, None]
    ).astype(jnp.bfloat16)
    states = jnp.einsum(
        "jghn,jghp->ghnp", scaled, grouped, preferred_element_type=jnp.float32
    ).reshape(num_heads, N * width)
    decays = jnp.exp(cumulative[-1]) * (doc_block[0] == doc_block[-1]).astype(jnp.float32)
    return local_part, states, decays, cumulative


def early_terms(local_part, block_input, gains):
    block_rows = block_input.shape[0]
    num_heads = gains.shape[0]
    per_group = num_heads // G
    width = block_input.shape[1] // num_heads
    direct = gains.reshape(G, per_group)[None, :, :, None] * block_input.reshape(
        block_rows, G, per_group, width
    ).astype(jnp.float32)
    return (local_part + direct).reshape(block_rows, num_heads * width)


def split_bf16(value):
    high = value.astype(jnp.bfloat16)
    low = (value - high.astype(jnp.float32)).astype(jnp.bfloat16)
    return high, low


def finish_kernel(early_ref, factor_ref, reads_ref, pairs_ref, out_ref):
    pairs = pairs_ref.shape[0]
    lanes = pairs_ref.shape[2]
    rows = reads_ref.shape[1]
    per_read = pairs // reads_ref.shape[0]
    heads = factor_ref.shape[2]
    span = pairs * lanes
    pick = (
        lax.broadcasted_iota(jnp.int32, (heads, span), 0)
        == lax.broadcasted_iota(jnp.int32, (heads, span), 1) // (lanes // 2)
    ).astype(jnp.bfloat16)
    fac = factor_ref[0]
    fac_hi = fac.astype(jnp.bfloat16)
    rest = fac - fac_hi.astype(jnp.float32)
    fac_mid = rest.astype(jnp.bfloat16)
    fac_lo = (rest - fac_mid.astype(jnp.float32)).astype(jnp.bfloat16)
    spread_all = jnp.dot(fac_hi, pick, preferred_element_type=jnp.float32)
    spread_all += jnp.dot(fac_mid, pick, preferred_element_type=jnp.float32)
    spread_all += jnp.dot(fac_lo, pick, preferred_element_type=jnp.float32)
    for k in range(pairs):
        if k % per_read == 0:
            read = reads_ref[k // per_read]
        st_hi, st_lo = split_bf16(pairs_ref[k])
        reached = jnp.dot(read, st_hi, preferred_element_type=jnp.float32)
        reached += jnp.dot(read, st_lo, preferred_element_type=jnp.float32)
        cols = slice(k * lanes, (k + 1) * lanes)
        spread = spread_all[:, cols]
        out_ref[:, cols] = (early_ref[:, cols] + reached * spread).astype(out_ref.dtype)


def finish_inputs(cumulative, last_in, read_block, doc_block):
    block_rows = read_block.shape[0]
    num_heads = cumulative.shape[1]
    per_group = num_heads // G
    carried_in = (doc_block.astype(jnp.float32) == last_in).astype(jnp.float32)
    factor = jnp.exp(cumulative) * carried_in[:, None]
    factor = factor.reshape(block_rows, G // 2, 2 * per_group).transpose(1, 0, 2)
    reads = read_block.reshape(block_rows, G, 1, N)
    reads2 = jnp.broadcast_to(reads, (block_rows, G, 2, N)).transpose(1, 0, 2, 3)
    return factor, reads2.reshape(G, block_rows, 2 * N)


def finish(early, factor, reads2, states_in):
    block_rows = early.shape[0]
    num_heads = states_in.shape[0]
    width = early.shape[1] // num_heads
    pairs = num_heads // G
    held = states_in.reshape(num_heads // 2, 2, N, width)
    upper = jnp.pad(held[:, 0], ((0, 0), (0, 0), (0, width)))
    lower = jnp.pad(held[:, 1], ((0, 0), (0, 0), (width, 0)))
    diag = jnp.concatenate([upper, lower], axis=1)
    lanes = 2 * width
    return pl.pallas_call(
        finish_kernel,
        grid=(G // 2,),
        in_specs=[
            pl.BlockSpec((block_rows, pairs * lanes), lambda g: (0, g)),
            pl.BlockSpec((1, block_rows, 2 * pairs), lambda g: (g, 0, 0)),
            pl.BlockSpec((2, block_rows, 2 * N), lambda g: (g, 0, 0)),
            pl.BlockSpec((pairs, 2 * N, lanes), lambda g: (g, 0, 0)),
        ],
        out_specs=pl.BlockSpec((block_rows, pairs * lanes), lambda g: (0, g)),
        out_shape=jax.ShapeDtypeStruct((block_rows, num_heads * width), jnp.bfloat16),
    )(early, factor, reads2, diag)


def exclusive_reverse_prod(values):
    inclusive = jnp.flip(jnp.cumprod(jnp.flip(values, 0), axis=0), 0)
    return jnp.concatenate([inclusive[1:], jnp.ones_like(values[:1])], axis=0)


def with_tail(rows, tail):
    pad = TAIL - tail.shape[1]
    tail = jnp.concatenate([tail, jnp.zeros((tail.shape[0], pad), jnp.float32)], axis=1)
    return jnp.concatenate([rows, tail], axis=1)


def local(
    mixer_input, write_vectors, read_vectors, step_sizes, decay_rate, skip_gain, document_ids
):
    num_heads = step_sizes.shape[1]
    axes = ("grp", "seq")
    n_blk = lax.axis_size(axes)
    me = lax.axis_index(axes)
    local_part, states, decays, cumulative = local_terms(
        mixer_input, write_vectors, read_vectors, step_sizes, decay_rate, document_ids
    )
    state_width = states.shape[1]
    docs_f = document_ids.astype(jnp.float32)
    first_id = docs_f[0]
    last_id = docs_f[-1]

    flat = states.reshape(n_blk, -1)
    row_len = flat.shape[1]
    row_heads = max(1, num_heads // n_blk)
    sub_len = row_len // row_heads
    if n_blk <= num_heads:
        sent_decays = decays.reshape(n_blk, row_heads)
    else:
        sent_decays = jnp.repeat(decays, n_blk // num_heads)[:, None]
    ids = jnp.broadcast_to(jnp.stack([first_id, last_id])[None, :], (n_blk, 2))
    tails = with_tail(jnp.zeros((n_blk, 0), jnp.float32), jnp.concatenate([sent_decays, ids], axis=1))
    got = lax.all_to_all(tails, axes, 0, 0, tiled=False)

    head_rows = 8 if sub_len % (8 * 128) == 0 else 1
    pieces = flat.reshape(n_blk, row_heads * head_rows, sub_len // head_rows)
    got, pieces = lax.optimization_barrier((got, pieces))
    owned = lax.all_to_all(pieces, axes, 0, 0, tiled=False)
    blk_decay = got[:, :row_heads]
    blk_first = got[:, row_heads]
    blk_last = got[:, row_heads + 1]
    last_in = jnp.where(me > 0, jnp.take(blk_last, jnp.maximum(me - 1, 0)), -1.0)
    early = early_terms(local_part, mixer_input, skip_gain)
    factor, reads2 = finish_inputs(cumulative, last_in, read_vectors, document_ids)

    src = jnp.arange(n_blk)
    prev_last = jnp.concatenate([jnp.full((1,), -1.0, jnp.float32), blk_last[:-1]])
    link = jnp.logical_and(src > 0, blk_first == prev_last).astype(jnp.float32)
    factors = blk_decay * link[:, None]
    before = (src[:, None] < src[None, :])[:, :, None]
    gated = jnp.where(before, factors[:, None, :], 1.0)
    coef = jnp.where(before, exclusive_reverse_prod(gated), 0.0)
    stacked = owned.reshape(n_blk, row_heads, head_rows, -1)
    result = jnp.einsum("tsh,thrl->shrl", coef, stacked, precision=lax.Precision.HIGHEST)
    result = result.reshape(owned.shape)

    back = lax.all_to_all(result, axes, 0, 0, tiled=False)
    states_in = back.reshape(num_heads, state_width)
    return finish(early, factor, reads2, states_in)


def solution(mesh):
    in_specs = (
        P(("grp", "seq"), None),
        P(("grp", "seq"), None),
        P(("grp", "seq"), None),
        P(("grp", "seq"), None),
        P(),
        P(),
        P(("grp", "seq")),
    )
    out_specs = P(("grp", "seq"), None)
    return jax.shard_map(local, mesh=mesh, in_specs=in_specs, out_specs=out_specs, check_vma=False)
```

```python
import numpy as np
import jax
import jax.numpy as jnp
from jax import lax
from jax.sharding import PartitionSpec as P
from jax.experimental import pallas as pl

N = 64
G = 4
TAIL = 128


def local_terms(block_input, write_block, read_block, step_block, rates, doc_block):
    block_rows = block_input.shape[0]
    num_heads = step_block.shape[1]
    per_group = num_heads // G
    width = block_input.shape[1] // num_heads
    grouped = block_input.reshape(block_rows, G, per_group, width)
    writes = write_block.reshape(block_rows, G, N)
    reads = read_block.reshape(block_rows, G, N)
    cumulative = jnp.cumsum(-step_block * rates[None, :], axis=0)
    cum_heads = cumulative.T.reshape(G, per_group, block_rows)
    step_heads = step_block.T.reshape(G, per_group, block_rows)
    positions = jnp.arange(block_rows)
    visible = jnp.logical_and(
        doc_block[:, None] == doc_block[None, :], positions[:, None] >= positions[None, :]
    )
    gaps = jnp.where(
        visible[None, None], cum_heads[:, :, :, None] - cum_heads[:, :, None, :], -jnp.inf
    )
    inner_prod = jnp.einsum("ign,jgn->gij", reads, writes, preferred_element_type=jnp.float32)
    weights = (inner_prod[:, None] * jnp.exp(gaps) * step_heads[:, :, None, :]).astype(jnp.bfloat16)
    local_part = jnp.einsum("ghij,jghp->ighp", weights, grouped, preferred_element_type=jnp.float32)
    same_last = (doc_block == doc_block[-1]).astype(jnp.float32)
    tail_weight = jnp.exp(cumulative[-1][None, :] - cumulative) * step_block * same_last[:, None]
    scaled = (
        writes[:, :, None, :].astype(jnp.float32)
        * tail_weight.reshape(block_rows, G, per_group)[:, :, :, None]
    ).astype(jnp.bfloat16)
    states = jnp.einsum(
        "jghn,jghp->ghnp", scaled, grouped, preferred_element_type=jnp.float32
    ).reshape(num_heads, N * width)
    decays = jnp.exp(cumulative[-1]) * (doc_block[0] == doc_block[-1]).astype(jnp.float32)
    return local_part, states, decays, cumulative


def early_terms(local_part, block_input, gains):
    block_rows = block_input.shape[0]
    num_heads = gains.shape[0]
    per_group = num_heads // G
    width = block_input.shape[1] // num_heads
    direct = gains.reshape(G, per_group)[None, :, :, None] * block_input.reshape(
        block_rows, G, per_group, width
    ).astype(jnp.float32)
    return (local_part + direct).reshape(block_rows, num_heads * width)


def split_bf16(value):
    high = value.astype(jnp.bfloat16)
    low = (value - high.astype(jnp.float32)).astype(jnp.bfloat16)
    return high, low


def finish_kernel(early_ref, factor_ref, reads_ref, pairs_ref, out_ref):
    pairs = pairs_ref.shape[0]
    lanes = pairs_ref.shape[2]
    rows = reads_ref.shape[1]
    per_read = pairs // reads_ref.shape[0]
    lane = lax.broadcasted_iota(jnp.int32, (rows, lanes), 1)
    for k in range(pairs):
        if k % per_read == 0:
            read = reads_ref[k // per_read]
        st_hi = pairs_ref[k, :lanes]
        st_lo = pairs_ref[k, lanes:]
        reached = jnp.dot(read, st_hi, preferred_element_type=jnp.float32)
        reached += jnp.dot(read, st_lo, preferred_element_type=jnp.float32)
        spread = jnp.where(
            lane < lanes // 2, factor_ref[0, :, 2 * k:2 * k + 1], factor_ref[0, :, 2 * k + 1:2 * k + 2]
        )
        cols = slice(k * lanes, (k + 1) * lanes)
        out_ref[:, cols] = (early_ref[:, cols] + reached * spread).astype(out_ref.dtype)


def finish_inputs(cumulative, last_in, read_block, doc_block):
    block_rows = read_block.shape[0]
    num_heads = cumulative.shape[1]
    per_group = num_heads // G
    carried_in = (doc_block.astype(jnp.float32) == last_in).astype(jnp.float32)
    factor = jnp.exp(cumulative) * carried_in[:, None]
    factor = factor.reshape(block_rows, G // 2, 2 * per_group).transpose(1, 0, 2)
    reads = read_block.reshape(block_rows, G, 1, N)
    reads2 = jnp.broadcast_to(reads, (block_rows, G, 2, N)).transpose(1, 0, 2, 3)
    return factor, reads2.reshape(G, block_rows, 2 * N)


def finish(early, factor, reads2, states_in):
    block_rows = early.shape[0]
    num_heads = states_in.shape[0]
    width = early.shape[1] // num_heads
    pairs = num_heads // G
    held = states_in.reshape(num_heads // 2, 2, N, width)
    upper = jnp.pad(held[:, 0], ((0, 0), (0, 0), (0, width)))
    lower = jnp.pad(held[:, 1], ((0, 0), (0, 0), (width, 0)))
    diag = jnp.concatenate([upper, lower], axis=1)
    diag_hi = lax.reduce_precision(diag, exponent_bits=8, mantissa_bits=7)
    diag = jnp.concatenate(
        [diag_hi.astype(jnp.bfloat16), (diag - diag_hi).astype(jnp.bfloat16)], axis=1
    )
    lanes = 2 * width
    return pl.pallas_call(
        finish_kernel,
        grid=(G // 2,),
        in_specs=[
            pl.BlockSpec((block_rows, pairs * lanes), lambda g: (0, g)),
            pl.BlockSpec((1, block_rows, 2 * pairs), lambda g: (g, 0, 0)),
            pl.BlockSpec((2, block_rows, 2 * N), lambda g: (g, 0, 0)),
            pl.BlockSpec((pairs, 4 * N, lanes), lambda g: (g, 0, 0)),
        ],
        out_specs=pl.BlockSpec((block_rows, pairs * lanes), lambda g: (0, g)),
        out_shape=jax.ShapeDtypeStruct((block_rows, num_heads * width), jnp.bfloat16),
    )(early, factor, reads2, diag)


def exclusive_reverse_prod(values):
    inclusive = jnp.flip(jnp.cumprod(jnp.flip(values, 0), axis=0), 0)
    return jnp.concatenate([inclusive[1:], jnp.ones_like(values[:1])], axis=0)


def with_tail(rows, tail):
    pad = TAIL - tail.shape[1]
    tail = jnp.concatenate([tail, jnp.zeros((tail.shape[0], pad), jnp.float32)], axis=1)
    return jnp.concatenate([rows, tail], axis=1)


def local(
    mixer_input, write_vectors, read_vectors, step_sizes, decay_rate, skip_gain, document_ids
):
    num_heads = step_sizes.shape[1]
    axes = ("grp", "seq")
    n_blk = lax.axis_size(axes)
    me = lax.axis_index(axes)
    local_part, states, decays, cumulative = local_terms(
        mixer_input, write_vectors, read_vectors, step_sizes, decay_rate, document_ids
    )
    state_width = states.shape[1]
    docs_f = document_ids.astype(jnp.float32)
    first_id = docs_f[0]
    last_id = docs_f[-1]

    flat = states.reshape(n_blk, -1)
    row_len = flat.shape[1]
    row_heads = max(1, num_heads // n_blk)
    sub_len = row_len // row_heads
    if n_blk <= num_heads:
        sent_decays = decays.reshape(n_blk, row_heads)
    else:
        sent_decays = jnp.repeat(decays, n_blk // num_heads)[:, None]
    ids = jnp.broadcast_to(jnp.stack([first_id, last_id])[None, :], (n_blk, 2))
    tails = with_tail(jnp.zeros((n_blk, 0), jnp.float32), jnp.concatenate([sent_decays, ids], axis=1))
    got = lax.all_to_all(tails, axes, 0, 0, tiled=False)

    head_rows = 8 if sub_len % (8 * 128) == 0 else 1
    pieces = flat.reshape(n_blk, row_heads * head_rows, sub_len // head_rows)
    got, pieces = lax.optimization_barrier((got, pieces))
    owned = lax.all_to_all(pieces, axes, 0, 0, tiled=False)
    blk_decay = got[:, :row_heads]
    blk_first = got[:, row_heads]
    blk_last = got[:, row_heads + 1]
    last_in = jnp.where(me > 0, jnp.take(blk_last, jnp.maximum(me - 1, 0)), -1.0)
    early = early_terms(local_part, mixer_input, skip_gain)
    factor, reads2 = finish_inputs(cumulative, last_in, read_vectors, document_ids)

    src = jnp.arange(n_blk)
    prev_last = jnp.concatenate([jnp.full((1,), -1.0, jnp.float32), blk_last[:-1]])
    link = jnp.logical_and(src > 0, blk_first == prev_last).astype(jnp.float32)
    factors = blk_decay * link[:, None]
    before = (src[:, None] < src[None, :])[:, :, None]
    gated = jnp.where(before, factors[:, None, :], 1.0)
    coef = jnp.where(before, exclusive_reverse_prod(gated), 0.0)
    stacked = owned.reshape(n_blk, row_heads, head_rows, -1)
    result = jnp.einsum("tsh,thrl->shrl", coef, stacked, precision=lax.Precision.HIGHEST)
    result = result.reshape(owned.shape)

    back = lax.all_to_all(result, axes, 0, 0, tiled=False)
    states_in = back.reshape(num_heads, state_width)
    return finish(early, factor, reads2, states_in)


def solution(mesh):
    in_specs = (
        P(("grp", "seq"), None),
        P(("grp", "seq"), None),
        P(("grp", "seq"), None),
        P(("grp", "seq"), None),
        P(),
        P(),
        P(("grp", "seq")),
    )
    out_specs = P(("grp", "seq"), None)
    return jax.shard_map(local, mesh=mesh, in_specs=in_specs, out_specs=out_specs, check_vma=False)
```

```python
import numpy as np
import jax
import jax.numpy as jnp
from jax import lax
from jax.sharding import PartitionSpec as P
from jax.experimental import pallas as pl

N = 64
G = 4
TAIL = 128


def local_terms(block_input, write_block, read_block, step_block, rates, doc_block):
    block_rows = block_input.shape[0]
    num_heads = step_block.shape[1]
    per_group = num_heads // G
    width = block_input.shape[1] // num_heads
    grouped = block_input.reshape(block_rows, G, per_group, width)
    writes = write_block.reshape(block_rows, G, N)
    reads = read_block.reshape(block_rows, G, N)
    cumulative = jnp.cumsum(-step_block * rates[None, :], axis=0)
    cum_heads = cumulative.T.reshape(G, per_group, block_rows)
    step_heads = step_block.T.reshape(G, per_group, block_rows)
    positions = jnp.arange(block_rows)
    visible = jnp.logical_and(
        doc_block[:, None] == doc_block[None, :], positions[:, None] >= positions[None, :]
    )
    gaps = jnp.where(
        visible[None, None], cum_heads[:, :, :, None] - cum_heads[:, :, None, :], -jnp.inf
    )
    inner_prod = jnp.einsum("ign,jgn->gij", reads, writes, preferred_element_type=jnp.float32)
    weights = (inner_prod[:, None] * jnp.exp(gaps) * step_heads[:, :, None, :]).astype(jnp.bfloat16)
    local_part = jnp.einsum("ghij,jghp->ighp", weights, grouped, preferred_element_type=jnp.float32)
    same_last = (doc_block == doc_block[-1]).astype(jnp.float32)
    tail_weight = jnp.exp(cumulative[-1][None, :] - cumulative) * step_block * same_last[:, None]
    scaled = (
        writes[:, :, None, :].astype(jnp.float32)
        * tail_weight.reshape(block_rows, G, per_group)[:, :, :, None]
    ).astype(jnp.bfloat16)
    states = jnp.einsum(
        "jghn,jghp->ghnp", scaled, grouped, preferred_element_type=jnp.float32
    ).reshape(num_heads, N * width)
    decays = jnp.exp(cumulative[-1]) * (doc_block[0] == doc_block[-1]).astype(jnp.float32)
    return local_part, states, decays, cumulative


def early_terms(local_part, block_input, gains):
    block_rows = block_input.shape[0]
    num_heads = gains.shape[0]
    per_group = num_heads // G
    width = block_input.shape[1] // num_heads
    direct = gains.reshape(G, per_group)[None, :, :, None] * block_input.reshape(
        block_rows, G, per_group, width
    ).astype(jnp.float32)
    return (local_part + direct).reshape(block_rows, num_heads * width)


def split_bf16(value):
    high = value.astype(jnp.bfloat16)
    low = (value - high.astype(jnp.float32)).astype(jnp.bfloat16)
    return high, low


def finish_kernel(early_ref, factor_ref, reads_ref, pairs_ref, out_ref):
    pairs = pairs_ref.shape[0]
    lanes = pairs_ref.shape[2]
    rows = reads_ref.shape[1]
    per_read = pairs // reads_ref.shape[0]
    lane = lax.broadcasted_iota(jnp.int32, (rows, lanes), 1)
    for k in range(pairs):
        if k % per_read == 0:
            read = reads_ref[k // per_read]
        st_hi, st_lo = split_bf16(pairs_ref[k])
        reached = jnp.dot(read, st_hi, preferred_element_type=jnp.float32)
        reached += jnp.dot(read, st_lo, preferred_element_type=jnp.float32)
        spread = jnp.where(
            lane < lanes // 2, factor_ref[0, :, 2 * k:2 * k + 1], factor_ref[0, :, 2 * k + 1:2 * k + 2]
        )
        cols = slice(k * lanes, (k + 1) * lanes)
        out_ref[:, cols] = (early_ref[:, cols] + reached * spread).astype(out_ref.dtype)


def finish_inputs(cumulative, last_in, read_block, doc_block):
    block_rows = read_block.shape[0]
    num_heads = cumulative.shape[1]
    per_group = num_heads // G
    carried_in = (doc_block.astype(jnp.float32) == last_in).astype(jnp.float32)
    factor = jnp.exp(cumulative) * carried_in[:, None]
    factor = factor.reshape(block_rows, G // 2, 2 * per_group).transpose(1, 0, 2)
    reads = read_block.reshape(block_rows, G, 1, N)
    reads2 = jnp.broadcast_to(reads, (block_rows, G, 2, N)).transpose(1, 0, 2, 3)
    return factor, reads2.reshape(G, block_rows, 2 * N)


def finish(early, factor, reads2, states_in):
    block_rows = early.shape[0]
    num_heads = states_in.shape[0]
    width = early.shape[1] // num_heads
    pairs = num_heads // G
    held = states_in.reshape(num_heads // 2, 2, N, width)
    upper = jnp.pad(held[:, 0], ((0, 0), (0, 0), (0, width)))
    lower = jnp.pad(held[:, 1], ((0, 0), (0, 0), (width, 0)))
    diag = jnp.concatenate([upper, lower], axis=1)
    lanes = 2 * width
    return pl.pallas_call(
        finish_kernel,
        grid=(G // 2,),
        in_specs=[
            pl.BlockSpec((block_rows, pairs * lanes), lambda g: (0, g)),
            pl.BlockSpec((1, block_rows, 2 * pairs), lambda g: (g, 0, 0)),
            pl.BlockSpec((2, block_rows, 2 * N), lambda g: (g, 0, 0)),
            pl.BlockSpec((pairs, 2 * N, lanes), lambda g: (g, 0, 0)),
        ],
        out_specs=pl.BlockSpec((block_rows, pairs * lanes), lambda g: (0, g)),
        out_shape=jax.ShapeDtypeStruct((block_rows, num_heads * width), jnp.bfloat16),
    )(early, factor, reads2, diag)


def exclusive_reverse_prod(values):
    inclusive = jnp.flip(jnp.cumprod(jnp.flip(values, 0), axis=0), 0)
    return jnp.concatenate([inclusive[1:], jnp.ones_like(values[:1])], axis=0)


def with_tail(rows, tail):
    pad = TAIL - tail.shape[1]
    tail = jnp.concatenate([tail, jnp.zeros((tail.shape[0], pad), jnp.float32)], axis=1)
    return jnp.concatenate([rows, tail], axis=1)


def local(
    mixer_input, write_vectors, read_vectors, step_sizes, decay_rate, skip_gain, document_ids
):
    num_heads = step_sizes.shape[1]
    axes = ("grp", "seq")
    n_blk = lax.axis_size(axes)
    me = lax.axis_index(axes)
    local_part, states, decays, cumulative = local_terms(
        mixer_input, write_vectors, read_vectors, step_sizes, decay_rate, document_ids
    )
    state_width = states.shape[1]
    docs_f = document_ids.astype(jnp.float32)
    first_id = docs_f[0]
    last_id = docs_f[-1]

    flat = states.reshape(n_blk, -1)
    row_len = flat.shape[1]
    row_heads = max(1, num_heads // n_blk)
    sub_len = row_len // row_heads
    if n_blk <= num_heads:
        sent_decays = decays.reshape(n_blk, row_heads)
    else:
        sent_decays = jnp.repeat(decays, n_blk // num_heads)[:, None]
    col = lax.broadcasted_iota(jnp.int32, (n_blk, TAIL), 1)
    tails = jnp.where(col == row_heads, first_id, jnp.where(col == row_heads + 1, last_id, 0.0))
    for j in range(row_heads):
        tails = jnp.where(col == j, sent_decays[:, j:j + 1], tails)
    got = lax.all_to_all(tails, axes, 0, 0, tiled=False)

    head_rows = 8 if sub_len % (8 * 128) == 0 else 1
    pieces = flat.reshape(n_blk, row_heads * head_rows, sub_len // head_rows)
    got, pieces = lax.optimization_barrier((got, pieces))
    owned = lax.all_to_all(pieces, axes, 0, 0, tiled=False)
    blk_decay = got[:, :row_heads]
    blk_first = got[:, row_heads]
    blk_last = got[:, row_heads + 1]
    last_in = jnp.where(me > 0, jnp.take(blk_last, jnp.maximum(me - 1, 0)), -1.0)
    early = early_terms(local_part, mixer_input, skip_gain)
    factor, reads2 = finish_inputs(cumulative, last_in, read_vectors, document_ids)

    src = jnp.arange(n_blk)
    prev_last = jnp.concatenate([jnp.full((1,), -1.0, jnp.float32), blk_last[:-1]])
    link = jnp.logical_and(src > 0, blk_first == prev_last).astype(jnp.float32)
    factors = blk_decay * link[:, None]
    before = (src[:, None] < src[None, :])[:, :, None]
    gated = jnp.where(before, factors[:, None, :], 1.0)
    coef = jnp.where(before, exclusive_reverse_prod(gated), 0.0)
    stacked = owned.reshape(n_blk, row_heads, head_rows, -1)
    result = jnp.einsum("tsh,thrl->shrl", coef, stacked, precision=lax.Precision.HIGHEST)
    result = result.reshape(owned.shape)

    back = lax.all_to_all(result, axes, 0, 0, tiled=False)
    states_in = back.reshape(num_heads, state_width)
    return finish(early, factor, reads2, states_in)


def solution(mesh):
    in_specs = (
        P(("grp", "seq"), None),
        P(("grp", "seq"), None),
        P(("grp", "seq"), None),
        P(("grp", "seq"), None),
        P(),
        P(),
        P(("grp", "seq")),
    )
    out_specs = P(("grp", "seq"), None)
    return jax.shard_map(local, mesh=mesh, in_specs=in_specs, out_specs=out_specs, check_vma=False)
```
